32 devices in a mesh: row: 4 (over x, core), col: 8 (over z, y).
Axes of the slice: x: 2, y: 2, z: 4, core: 2. Of those that a mesh axis runs over, the one named last changes fastest.
Arguments:
- panel_blocks: bfloat16 [3, 32, 8, 128, 128], P(None, 'col', 'row'), may hold values from -0.5 to 0.5
- user_weights: float32 [3, 32, 128], P(None, 'col'), may hold values from 0.1 to 10
- slot_offset: int32 [3, 32, 8], P(None, 'col', 'row'), may hold values from 0 to 7
Outputs:
- gram: float32 [8192, 8192], P('row', 'col')
The draws below stay inside these ranges and needn't reach their ends.
All inputs are finite; a program needn't handle non-finite values.
Results may differ from the reference program's by a relative error of at most 0.0022.
Values may be sent and summed in bfloat16 or wider, within the bound.
No kernel may reach another device: no remote copies, remote signals or barrier semaphores. Data moves between devices by JAX's collectives and lax.ppermute only.
A program may use at most 128 MiB of HBM per device.

```python
import math
import jax
import jax.numpy as jnp
from jax import lax

BLK = 128
PANELS = 3
IBS = 8
UB = 32
SLOTS = 8
NBI = 64
ITEMS = 8192


def plant(drawn, rng, smallest, top_value):
    index_at = [jax.random.randint(jax.random.fold_in(rng, axis), (), 0, length) for axis, length in enumerate(drawn.shape)]
    longest = drawn.shape.index(max(drawn.shape))
    next_to = index_at[:longest] + [(index_at[longest] + 1) % drawn.shape[longest]] + index_at[longest + 1:]
    return drawn.at[tuple(index_at)].set(smallest).at[tuple(next_to)].set(top_value)


def block_scale(key, dims, pieces, smallest, largest):
    level = 1.0
    for axis_at, blocks in pieces:
        heights = jax.random.uniform(jax.random.fold_in(jax.random.fold_in(key, 6), axis_at), (blocks,), jnp.float32, smallest / len(pieces), largest / len(pieces))
        level = level * jnp.repeat(jnp.exp(heights), dims[axis_at] // blocks).reshape((-1,) + (1,) * (len(dims) - 1 - axis_at))
    return level


def noise(rng, extent, width, reach, shards=(), kind=jnp.bfloat16):
    loudness = block_scale(rng, extent, shards, -0.22, 0.18) if shards else 1.0
    drawn = jax.random.normal(rng, extent, jnp.float32) * width * loudness
    return jnp.minimum(jnp.maximum(drawn, -reach), reach).astype(kind)


def setup_inputs(seed: int = 0) -> dict:
    seeds = jax.random.split(jax.random.key(seed), 4)
    return {
        "panel_blocks": noise(seeds[0], (PANELS, UB, SLOTS, BLK, BLK), 0.07, 0.5, ((1, 8), (2, 4))),
        "user_weights": jnp.clip(jnp.exp(math.log(10.0) - 4.6051702 * jax.random.uniform(seeds[1], (PANELS, UB, BLK), jnp.float32) ** block_scale(seeds[1], (PANELS, UB, BLK), ((1, 8),), -0.2, 0.2)), 0.1, 10.0),
        "slot_offset": plant(jax.random.randint(seeds[2], (PANELS, UB, SLOTS), 0, IBS), jax.random.fold_in(seeds[2], 1), 0, IBS - 1).astype(jnp.int32),
    }


def reference(panel_blocks, user_weights, slot_offset):
    position = slot_offset + jnp.arange(SLOTS, dtype=jnp.int32)[None, None, :] * IBS
    flat_blocks = panel_blocks.reshape(PANELS * UB, SLOTS, BLK, BLK)
    flat_weights = user_weights.reshape(PANELS * UB, BLK)
    flat_position = position.reshape(PANELS * UB, SLOTS).astype(jnp.int32)

    def accumulate(step_index, gram_blocks):
        blocks = lax.dynamic_index_in_dim(flat_blocks, step_index, 0, keepdims=False)
        weights_row = lax.dynamic_index_in_dim(flat_weights, step_index, 0, keepdims=False)
        places = lax.dynamic_index_in_dim(flat_position, step_index, 0, keepdims=False)
        weighted = (weights_row[None, :, None] * blocks.astype(jnp.float32)).astype(jnp.bfloat16)
        products = jnp.einsum("sxa,txb->stab", weighted.astype(jnp.float32), blocks.astype(jnp.float32))
        return gram_blocks.at[places[:, None], places[None, :]].add(products)

    start_blocks = jnp.zeros((NBI, NBI, BLK, BLK), jnp.float32)
    gram_blocks = lax.fori_loop(0, PANELS * UB, accumulate, start_blocks)
    return gram_blocks.transpose(0, 2, 1, 3).reshape(ITEMS, ITEMS)
```

```python
import functools

import jax
import jax.numpy as jnp
from jax import lax
from jax.experimental import pallas as pl
from jax.experimental.pallas import tpu as pltpu
from jax.sharding import PartitionSpec as P

IBS = 8
CHUNK = 8


def gram_kernel(offs_ref, bs_ref, w_ref, bc_ref, o_ref, *, chunk, local_slots, blk):
    step = pl.program_id(0)

    @pl.when(step == 0)
    def _():
        o_ref[...] = jnp.zeros_like(o_ref)

    stride = local_slots + 1
    for k in range(chunk):
        g = step * chunk + k
        w = w_ref[pl.ds(k, 1), :]
        lhs = jnp.concatenate(
            [
                (bs_ref[k, s].astype(jnp.float32).T * w).astype(jnp.bfloat16)
                for s in range(local_slots)
            ],
            axis=0,
        )
        prod = jnp.dot(lhs, bc_ref[k], preferred_element_type=jnp.float32)
        col = pl.multiple_of(offs_ref[g * stride + local_slots] * blk, blk)
        for s in range(local_slots):
            row = pl.multiple_of((s * IBS + offs_ref[g * stride + s]) * blk, blk)
            o_ref[pl.ds(row, blk), pl.ds(col, blk)] += prod[s * blk : (s + 1) * blk]


def gram_call(offs, bs, w, bc):
    n, local_slots, blk, _ = bs.shape
    chunk = CHUNK
    kernel = functools.partial(gram_kernel, chunk=chunk, local_slots=local_slots, blk=blk)
    out_rows, out_cols = local_slots * IBS * blk, IBS * blk
    return pl.pallas_call(
        kernel,
        grid_spec=pltpu.PrefetchScalarGridSpec(
            num_scalar_prefetch=1,
            grid=(n // chunk,),
            in_specs=[
                pl.BlockSpec((chunk, local_slots, blk, blk), lambda i, o: (i, 0, 0, 0)),
                pl.BlockSpec((chunk, blk), lambda i, o: (i, 0)),
                pl.BlockSpec((chunk, blk, blk), lambda i, o: (i, 0, 0)),
            ],
            out_specs=pl.BlockSpec((out_rows, out_cols), lambda i, o: (0, 0)),
        ),
        out_shape=jax.ShapeDtypeStruct((out_rows, out_cols), jnp.float32),
        compiler_params=pltpu.CompilerParams(
            dimension_semantics=("arbitrary",), vmem_limit_bytes=48 * 1024 * 1024
        ),
        cost_estimate=pl.CostEstimate(
            flops=2 * n * local_slots * blk * blk * blk,
            transcendentals=0,
            bytes_accessed=n * (local_slots + 1) * blk * blk * 2 + out_rows * out_cols * 4,
        ),
    )(offs, bs, w, bc)


def local(panel_blocks, user_weights, slot_offset, *, nrow, ncol):
    panels, _, local_slots, blk, _ = panel_blocks.shape
    r = lax.axis_index("row")
    c = lax.axis_index("col")
    blocks = lax.all_gather(panel_blocks, "col", axis=1, tiled=True)
    weights = lax.all_gather(user_weights, "col", axis=1, tiled=True)
    offsets = lax.all_gather(slot_offset, "col", axis=1, tiled=True)
    all_offsets = lax.all_gather(offsets, "row", axis=2, tiled=True)
    users = blocks.shape[1]

    src = c // local_slots
    own = lax.dynamic_index_in_dim(blocks, c % local_slots, axis=2, keepdims=False)
    received = [own]
    for k in range(1, nrow):
        perm = [
            ((cc // local_slots) * ncol + cc, ((cc // local_slots + k) % nrow) * ncol + cc)
            for cc in range(ncol)
        ]
        received.append(lax.ppermute(own, ("row", "col"), perm))
    which = (r - src + nrow) % nrow
    column_blocks = received[0]
    for k in range(1, nrow):
        column_blocks = jnp.where(which == k, received[k], column_blocks)

    col_offsets = lax.dynamic_index_in_dim(all_offsets, c, axis=2, keepdims=True)
    offs = jnp.concatenate([offsets, col_offsets], axis=2)
    offs = jnp.clip(offs, 0, IBS - 1).reshape(-1).astype(jnp.int32)

    n = panels * users
    return gram_call(
        offs,
        blocks.reshape(n, local_slots, blk, blk),
        weights.reshape(n, blk),
        column_blocks.reshape(n, blk, blk),
    )


def solution(mesh):
    nrow, ncol = mesh.shape["row"], mesh.shape["col"]
    return jax.shard_map(
        functools.partial(local, nrow=nrow, ncol=ncol),
        mesh=mesh,
        in_specs=(P(None, "col", "row", None, None), P(None, "col", None), P(None, "col", "row")),
        out_specs=P("row", "col"),
        check_vma=False,
    )
```

```python
import functools

import jax
import jax.numpy as jnp
from jax import lax
from jax.experimental import pallas as pl
from jax.experimental.pallas import tpu as pltpu
from jax.sharding import PartitionSpec as P

IBS = 8
CHUNK = 8
META = 16


def gram_kernel(offs_ref, bs_ref, bc_ref, o_ref, *, chunk, local_slots, blk):
    step = pl.program_id(0)

    @pl.when(step == 0)
    def _():
        o_ref[...] = jnp.zeros_like(o_ref)

    stride = local_slots + 1
    for k in range(chunk):
        g = step * chunk + k
        meta = bs_ref[k, 0, blk : blk + META].astype(jnp.float32)
        w = meta[0:1] + meta[1:2] + meta[2:3]
        lhs = jnp.concatenate(
            [
                (bs_ref[k, s, :blk].astype(jnp.float32).T * w).astype(jnp.bfloat16)
                for s in range(local_slots)
            ],
            axis=0,
        )
        prod = jnp.dot(lhs, bc_ref[k, :blk], preferred_element_type=jnp.float32)
        col = pl.multiple_of(offs_ref[g * stride + local_slots] * blk, blk)
        for s in range(local_slots):
            row = pl.multiple_of((s * IBS + offs_ref[g * stride + s]) * blk, blk)
            o_ref[pl.ds(row, blk), pl.ds(col, blk)] += prod[s * blk : (s + 1) * blk]


def gram_call(offs, bs, bc):
    n, local_slots, rows, blk = bs.shape
    chunk = CHUNK
    kernel = functools.partial(gram_kernel, chunk=chunk, local_slots=local_slots, blk=blk)
    out_rows, out_cols = local_slots * IBS * blk, IBS * blk
    return pl.pallas_call(
        kernel,
        grid_spec=pltpu.PrefetchScalarGridSpec(
            num_scalar_prefetch=1,
            grid=(n // chunk,),
            in_specs=[
                pl.BlockSpec((chunk, local_slots, rows, blk), lambda i, o: (i, 0, 0, 0)),
                pl.BlockSpec((chunk, rows, blk), lambda i, o: (i, 0, 0)),
            ],
            out_specs=pl.BlockSpec((out_rows, out_cols), lambda i, o: (0, 0)),
        ),
        out_shape=jax.ShapeDtypeStruct((out_rows, out_cols), jnp.float32),
        compiler_params=pltpu.CompilerParams(
            dimension_semantics=("arbitrary",), vmem_limit_bytes=48 * 1024 * 1024
        ),
        cost_estimate=pl.CostEstimate(
            flops=2 * n * local_slots * blk * blk * blk,
            transcendentals=0,
            bytes_accessed=n * (local_slots + 1) * blk * blk * 2 + out_rows * out_cols * 4,
        ),
    )(offs, bs, bc)


def with_meta(panel_blocks, user_weights, slot_offset):
    panels, users, local_slots, blk, _ = panel_blocks.shape
    hi = lax.reduce_precision(user_weights, exponent_bits=8, mantissa_bits=7)
    rest = user_weights - hi
    mid = lax.reduce_precision(rest, exponent_bits=8, mantissa_bits=7)
    low = rest - mid
    weight_rows = jnp.stack([hi, mid, low], axis=2).astype(jnp.bfloat16)[:, :, None]
    weight_rows = jnp.broadcast_to(weight_rows, (panels, users, local_slots, 3, blk))
    offset_rows = jnp.broadcast_to(
        slot_offset.astype(jnp.bfloat16)[..., None, None], (panels, users, local_slots, 1, blk)
    )
    pad = jnp.zeros((panels, users, local_slots, META - 4, blk), jnp.bfloat16)
    return jnp.concatenate([panel_blocks, weight_rows, offset_rows, pad], axis=3)


def local(panel_blocks, user_weights, slot_offset, *, nrow, ncol):
    panels, _, local_slots, blk, _ = panel_blocks.shape
    r = lax.axis_index("row")
    c = lax.axis_index("col")
    blocks = lax.all_gather(
        with_meta(panel_blocks, user_weights, slot_offset), "col", axis=1, tiled=True
    )
    users = blocks.shape[1]

    src = c // local_slots
    own = lax.dynamic_index_in_dim(blocks, c % local_slots, axis=2, keepdims=False)
    received = [own]
    for k in range(1, nrow):
        perm = [
            ((cc // local_slots) * ncol + cc, ((cc // local_slots + k) % nrow) * ncol + cc)
            for cc in range(ncol)
        ]
        received.append(lax.ppermute(own, ("row", "col"), perm))
    which = (r - src + nrow) % nrow
    column_blocks = received[0]
    for k in range(1, nrow):
        column_blocks = jnp.where(which == k, received[k], column_blocks)

    offs = jnp.concatenate(
        [blocks[:, :, :, blk + 3, 0], column_blocks[:, :, blk + 3, 0][:, :, None]], axis=2
    )
    offs = jnp.clip(offs.astype(jnp.int32), 0, IBS - 1).reshape(-1)

    n = panels * users
    return gram_call(
        offs,
        blocks.reshape(n, local_slots, blk + META, blk),
        column_blocks.reshape(n, blk + META, blk),
    )


def solution(mesh):
    nrow, ncol = mesh.shape["row"], mesh.shape["col"]
    return jax.shard_map(
        functools.partial(local, nrow=nrow, ncol=ncol),
        mesh=mesh,
        in_specs=(P(None, "col", "row", None, None), P(None, "col", None), P(None, "col", "row")),
        out_specs=P("row", "col"),
        check_vma=False,
    )
```

```python
import functools

import jax
import jax.numpy as jnp
from jax import lax
from jax.experimental import pallas as pl
from jax.experimental.pallas import tpu as pltpu
from jax.sharding import PartitionSpec as P

IBS = 8
CHUNK = 8
META = 16


def gram_kernel(offs_ref, bs_ref, bc_ref, *refs, chunk, local_slots, blk):
    o_ref = refs[-1]
    step = pl.program_id(0)

    @pl.when(step == 0)
    def _():
        if len(refs) == 2:
            o_ref[...] = refs[0][...]
        else:
            o_ref[...] = jnp.zeros_like(o_ref)

    stride = local_slots + 1
    for k in range(chunk):
        g = step * chunk + k
        meta = bs_ref[k, 0, blk : blk + META].astype(jnp.float32)
        w = meta[0:1] + meta[1:2] + meta[2:3]
        lhs = jnp.concatenate(
            [
                (bs_ref[k, s, :blk].astype(jnp.float32).T * w).astype(jnp.bfloat16)
                for s in range(local_slots)
            ],
            axis=0,
        )
        prod = jnp.dot(lhs, bc_ref[k, :blk], preferred_element_type=jnp.float32)
        col = pl.multiple_of(offs_ref[g * stride + local_slots] * blk, blk)
        for s in range(local_slots):
            row = pl.multiple_of((s * IBS + offs_ref[g * stride + s]) * blk, blk)
            o_ref[pl.ds(row, blk), pl.ds(col, blk)] += prod[s * blk : (s + 1) * blk]


def gram_call(offs, bs, bc, acc=None):
    n, local_slots, rows, blk = bs.shape
    chunk = CHUNK
    kernel = functools.partial(gram_kernel, chunk=chunk, local_slots=local_slots, blk=blk)
    out_rows, out_cols = local_slots * IBS * blk, IBS * blk
    acc_specs = [] if acc is None else [pl.BlockSpec((out_rows, out_cols), lambda i, o: (0, 0))]
    acc_args = () if acc is None else (acc,)
    return pl.pallas_call(
        kernel,
        grid_spec=pltpu.PrefetchScalarGridSpec(
            num_scalar_prefetch=1,
            grid=(n // chunk,),
            in_specs=[
                pl.BlockSpec((chunk, local_slots, rows, blk), lambda i, o: (i, 0, 0, 0)),
                pl.BlockSpec((chunk, rows, blk), lambda i, o: (i, 0, 0)),
            ]
            + acc_specs,
            out_specs=pl.BlockSpec((out_rows, out_cols), lambda i, o: (0, 0)),
        ),
        out_shape=jax.ShapeDtypeStruct((out_rows, out_cols), jnp.float32),
        input_output_aliases={} if acc is None else {3: 0},
        compiler_params=pltpu.CompilerParams(
            dimension_semantics=("arbitrary",), vmem_limit_bytes=56 * 1024 * 1024
        ),
        cost_estimate=pl.CostEstimate(
            flops=2 * n * local_slots * blk * blk * blk,
            transcendentals=0,
            bytes_accessed=n * (local_slots + 1) * blk * blk * 2 + out_rows * out_cols * 4,
        ),
    )(offs, bs, bc, *acc_args)


def with_meta(panel_blocks, user_weights, slot_offset):
    panels, users, local_slots, blk, _ = panel_blocks.shape
    hi = lax.reduce_precision(user_weights, exponent_bits=8, mantissa_bits=7)
    rest = user_weights - hi
    mid = lax.reduce_precision(rest, exponent_bits=8, mantissa_bits=7)
    low = rest - mid
    weight_rows = jnp.stack([hi, mid, low], axis=2).astype(jnp.bfloat16)[:, :, None]
    weight_rows = jnp.broadcast_to(weight_rows, (panels, users, local_slots, 3, blk))
    offset_rows = jnp.broadcast_to(
        slot_offset.astype(jnp.bfloat16)[..., None, None], (panels, users, local_slots, 1, blk)
    )
    pad = jnp.zeros((panels, users, local_slots, META - 4, blk), jnp.bfloat16)
    return jnp.concatenate([panel_blocks, weight_rows, offset_rows, pad], axis=3)


def local(panel_blocks, user_weights, slot_offset, *, nrow, ncol):
    panels, _, local_slots, blk, _ = panel_blocks.shape
    r = lax.axis_index("row")
    c = lax.axis_index("col")
    extended = with_meta(panel_blocks, user_weights, slot_offset)
    src = c // local_slots
    which = (r - src + nrow) % nrow
    acc = None
    for p in range(panels):
        blocks = lax.all_gather(extended[p], "col", axis=0, tiled=True)
        users = blocks.shape[0]
        own = lax.dynamic_index_in_dim(blocks, c % local_slots, axis=1, keepdims=False)
        column_blocks = own
        for k in range(1, nrow):
            perm = [
                ((cc // local_slots) * ncol + cc, ((cc // local_slots + k) % nrow) * ncol + cc)
                for cc in range(ncol)
            ]
            column_blocks = jnp.where(
                which == k, lax.ppermute(own, ("row", "col"), perm), column_blocks
            )
        offs = jnp.concatenate(
            [blocks[:, :, blk + 3, 0], column_blocks[:, blk + 3, 0][:, None]], axis=1
        )
        offs = jnp.clip(offs.astype(jnp.int32), 0, IBS - 1).reshape(-1)
        acc = gram_call(offs, blocks, column_blocks, acc)
    return acc


def solution(mesh):
    nrow, ncol = mesh.shape["row"], mesh.shape["col"]
    return jax.shard_map(
        functools.partial(local, nrow=nrow, ncol=ncol),
        mesh=mesh,
        in_specs=(P(None, "col", "row", None, None), P(None, "col", None), P(None, "col", "row")),
        out_specs=P("row", "col"),
        check_vma=False,
    )
```

```python
import functools

import jax
import jax.numpy as jnp
from jax import lax
from jax.experimental import pallas as pl
from jax.experimental.pallas import tpu as pltpu
from jax.sharding import PartitionSpec as P

IBS = 8
CHUNK = 8
META = 16


def gram_kernel(offs_ref, bs_ref, bc_ref, o_ref, *, chunk, local_slots, blk):
    step = pl.program_id(0)

    @pl.when(step == 0)
    def _():
        o_ref[...] = jnp.zeros_like(o_ref)

    stride = local_slots + 1
    for k in range(chunk):
        g = step * chunk + k
        meta = bs_ref[k, 0, blk : blk + META].astype(jnp.float32)
        w = meta[0:1] + meta[1:2] + meta[2:3]
        lhs = jnp.concatenate(
            [
                (bs_ref[k, s, :blk].astype(jnp.float32).T * w).astype(jnp.bfloat16)
                for s in range(local_slots)
            ],
            axis=0,
        )
        prod = jnp.dot(lhs, bc_ref[k, :blk], preferred_element_type=jnp.float32)
        col = pl.multiple_of(offs_ref[g * stride + local_slots] * blk, blk)
        for s in range(local_slots):
            row = pl.multiple_of((s * IBS + offs_ref[g * stride + s]) * blk, blk)
            o_ref[pl.ds(row, blk), pl.ds(col, blk)] += prod[s * blk : (s + 1) * blk]


def gram_call(offs, bs, bc):
    n, local_slots, rows, blk = bs.shape
    chunk = CHUNK
    kernel = functools.partial(gram_kernel, chunk=chunk, local_slots=local_slots, blk=blk)
    out_rows, out_cols = local_slots * IBS * blk, IBS * blk
    return pl.pallas_call(
        kernel,
        grid_spec=pltpu.PrefetchScalarGridSpec(
            num_scalar_prefetch=1,
            grid=(n // chunk,),
            in_specs=[
                pl.BlockSpec((chunk, local_slots, rows, blk), lambda i, o: (i, 0, 0, 0)),
                pl.BlockSpec((chunk, rows, blk), lambda i, o: (i, 0, 0)),
            ],
            out_specs=pl.BlockSpec((out_rows, out_cols), lambda i, o: (0, 0)),
        ),
        out_shape=jax.ShapeDtypeStruct((out_rows, out_cols), jnp.float32),
        compiler_params=pltpu.CompilerParams(
            dimension_semantics=("arbitrary",), vmem_limit_bytes=48 * 1024 * 1024
        ),
        cost_estimate=pl.CostEstimate(
            flops=2 * n * local_slots * blk * blk * blk,
            transcendentals=0,
            bytes_accessed=n * (local_slots + 1) * blk * blk * 2 + out_rows * out_cols * 4,
        ),
    )(offs, bs, bc)


def with_meta(panel_blocks, user_weights, slot_offset):
    panels, users, local_slots, blk, _ = panel_blocks.shape
    hi = lax.reduce_precision(user_weights, exponent_bits=8, mantissa_bits=7)
    rest = user_weights - hi
    mid = lax.reduce_precision(rest, exponent_bits=8, mantissa_bits=7)
    low = rest - mid
    weight_rows = jnp.stack([hi, mid, low], axis=2).astype(jnp.bfloat16)[:, :, None]
    weight_rows = jnp.broadcast_to(weight_rows, (panels, users, local_slots, 3, blk))
    offset_rows = jnp.broadcast_to(
        slot_offset.astype(jnp.bfloat16)[..., None, None], (panels, users, local_slots, 1, blk)
    )
    pad = jnp.zeros((panels, users, local_slots, META - 4, blk), jnp.bfloat16)
    return jnp.concatenate([panel_blocks, weight_rows, offset_rows, pad], axis=3)


def broadcast_slot(own, r, src, nrow, ncol, local_slots):
    nx = nrow // 2
    half = own.shape[0] // 2
    source_of = lambda cc: cc // local_slots

    def send(x, pairs):
        return lax.ppermute(x, ("row", "col"), [(a * ncol + cc, b * ncol + cc) for cc, a, b in pairs])

    partner = send(own, [(cc, source_of(cc), source_of(cc) ^ 1) for cc in range(ncol)])
    x_r, x_s = r // 2, src // 2
    j_r = (x_r - x_s + nx) % nx
    first, second = own[:half], own[half:]
    result_first, result_second = first, second
    for j in range(1, nx):
        to = lambda cc: 2 * ((source_of(cc) // 2 + j) % nx)
        a_even = send(first, [(cc, source_of(cc), to(cc)) for cc in range(ncol)])
        b_odd = send(second, [(cc, source_of(cc), to(cc) + 1) for cc in range(ncol)])
        a_odd = send(a_even, [(cc, to(cc), to(cc) + 1) for cc in range(ncol)])
        b_even = send(b_odd, [(cc, to(cc) + 1, to(cc)) for cc in range(ncol)])
        even = r % 2 == 0
        result_first = jnp.where(j_r == j, jnp.where(even, a_even, a_odd), result_first)
        result_second = jnp.where(j_r == j, jnp.where(even, b_even, b_odd), result_second)
    other = jnp.concatenate([result_first, result_second], axis=0)
    return jnp.where(j_r == 0, jnp.where(r == src, own, partner), other)


def local(panel_blocks, user_weights, slot_offset, *, nrow, ncol):
    panels, _, local_slots, blk, _ = panel_blocks.shape
    r = lax.axis_index("row")
    c = lax.axis_index("col")
    blocks = lax.all_gather(
        with_meta(panel_blocks, user_weights, slot_offset), "col", axis=1, tiled=True
    )
    n = panels * blocks.shape[1]
    blocks = blocks.reshape(n, local_slots, blk + META, blk)

    src = c // local_slots
    own = lax.dynamic_index_in_dim(blocks, c % local_slots, axis=1, keepdims=False)
    column_blocks = broadcast_slot(own, r, src, nrow, ncol, local_slots)

    offs = jnp.concatenate([blocks[:, :, blk + 3, 0], column_blocks[:, blk + 3, 0][:, None]], axis=1)
    offs = jnp.clip(offs.astype(jnp.int32), 0, IBS - 1).reshape(-1)
    return gram_call(offs, blocks, column_blocks)


def solution(mesh):
    nrow, ncol = mesh.shape["row"], mesh.shape["col"]
    return jax.shard_map(
        functools.partial(local, nrow=nrow, ncol=ncol),
        mesh=mesh,
        in_specs=(P(None, "col", "row", None, None), P(None, "col", None), P(None, "col", "row")),
        out_specs=P("row", "col"),
        check_vma=False,
    )
```

```python
import functools

import jax
import jax.numpy as jnp
from jax import lax
from jax.experimental import pallas as pl
from jax.experimental.pallas import tpu as pltpu
from jax.sharding import PartitionSpec as P

IBS = 8
CHUNK = 8
META = 16


def gram_kernel(offs_ref, bs_ref, bc_ref, o_ref, *, chunk, local_slots, blk):
    step = pl.program_id(0)

    @pl.when(step == 0)
    def _():
        o_ref[...] = jnp.zeros_like(o_ref)

    stride = local_slots + 1
    for k in range(chunk):
        g = step * chunk + k
        meta = bs_ref[k, 0, blk : blk + META].astype(jnp.float32)
        w = meta[0:1] + meta[1:2] + meta[2:3]
        lhs = jnp.concatenate(
            [
                (bs_ref[k, s, :blk].astype(jnp.float32).T * w).astype(jnp.bfloat16)
                for s in range(local_slots)
            ],
            axis=0,
        )
        prod = jnp.dot(lhs, bc_ref[k, :blk], preferred_element_type=jnp.float32)
        col = pl.multiple_of(offs_ref[g * stride + local_slots] * blk, blk)
        for s in range(local_slots):
            row = pl.multiple_of((s * IBS + offs_ref[g * stride + s]) * blk, blk)
            o_ref[pl.ds(row, blk), pl.ds(col, blk)] += prod[s * blk : (s + 1) * blk]


def gram_call(offs, bs, bc):
    n, local_slots, rows, blk = bs.shape
    chunk = CHUNK
    kernel = functools.partial(gram_kernel, chunk=chunk, local_slots=local_slots, blk=blk)
    out_rows, out_cols = local_slots * IBS * blk, IBS * blk
    return pl.pallas_call(
        kernel,
        grid_spec=pltpu.PrefetchScalarGridSpec(
            num_scalar_prefetch=1,
            grid=(n // chunk,),
            in_specs=[
                pl.BlockSpec((chunk, local_slots, rows, blk), lambda i, o: (i, 0, 0, 0)),
                pl.BlockSpec((chunk, rows, blk), lambda i, o: (i, 0, 0)),
            ],
            out_specs=pl.BlockSpec((out_rows, out_cols), lambda i, o: (0, 0)),
        ),
        out_shape=jax.ShapeDtypeStruct((out_rows, out_cols), jnp.float32),
        compiler_params=pltpu.CompilerParams(
            dimension_semantics=("arbitrary",), vmem_limit_bytes=48 * 1024 * 1024
        ),
        cost_estimate=pl.CostEstimate(
            flops=2 * n * local_slots * blk * blk * blk,
            transcendentals=0,
            bytes_accessed=n * (local_slots + 1) * blk * blk * 2 + out_rows * out_cols * 4,
        ),
    )(offs, bs, bc)


def with_meta(panel_blocks, user_weights, slot_offset):
    panels, users, local_slots, blk, _ = panel_blocks.shape
    hi = lax.reduce_precision(user_weights, exponent_bits=8, mantissa_bits=7)
    rest = user_weights - hi
    mid = lax.reduce_precision(rest, exponent_bits=8, mantissa_bits=7)
    low = rest - mid
    weight_rows = jnp.stack([hi, mid, low], axis=2).astype(jnp.bfloat16)[:, :, None]
    weight_rows = jnp.broadcast_to(weight_rows, (panels, users, local_slots, 3, blk))
    offset_rows = jnp.broadcast_to(
        slot_offset.astype(jnp.bfloat16)[..., None, None], (panels, users, local_slots, 1, blk)
    )
    pad = jnp.zeros((panels, users, local_slots, META - 4, blk), jnp.bfloat16)
    return jnp.concatenate([panel_blocks, weight_rows, offset_rows, pad], axis=3)


def broadcast_slot(own, r, src, nrow, ncol, local_slots):
    nx = nrow // 2
    half = own.shape[0] // 2
    source_of = lambda cc: cc // local_slots

    def send(x, pairs):
        return lax.ppermute(x, ("row", "col"), [(a * ncol + cc, b * ncol + cc) for cc, a, b in pairs])

    partner = send(own, [(cc, source_of(cc), source_of(cc) ^ 1) for cc in range(ncol)])
    x_r, x_s = r // 2, src // 2
    j_r = (x_r - x_s + nx) % nx
    first, second = own[:half], own[half:]
    result_first, result_second = first, second
    for j in range(1, nx):
        to = lambda cc: 2 * ((source_of(cc) // 2 + j) % nx)
        a_even = send(first, [(cc, source_of(cc), to(cc)) for cc in range(ncol)])
        b_odd = send(second, [(cc, source_of(cc), to(cc) + 1) for cc in range(ncol)])
        a_odd = send(a_even, [(cc, to(cc), to(cc) + 1) for cc in range(ncol)])
        b_even = send(b_odd, [(cc, to(cc) + 1, to(cc)) for cc in range(ncol)])
        even = r % 2 == 0
        result_first = jnp.where(j_r == j, jnp.where(even, a_even, a_odd), result_first)
        result_second = jnp.where(j_r == j, jnp.where(even, b_even, b_odd), result_second)
    other = jnp.concatenate([result_first, result_second], axis=0)
    return jnp.where(j_r == 0, jnp.where(r == src, own, partner), other)


def ring_gather(x, ncol):
    outer = ncol // 2
    cycle = [a * 2 for a in range(outer)] + [a * 2 + 1 for a in reversed(range(outer))]
    forward = [(cycle[i], cycle[(i + 1) % ncol]) for i in range(ncol)]
    backward = [(b, a) for a, b in forward]
    half = x.shape[1] // 2
    a, b = x[:, :half], x[:, half:]
    pieces_a, pieces_b = [a], [b]
    for _ in range(1, ncol):
        a = lax.ppermute(a, "col", forward)
        b = lax.ppermute(b, "col", backward)
        pieces_a.append(a)
        pieces_b.append(b)
    return jnp.concatenate(pieces_a + pieces_b, axis=1)


def local(panel_blocks, user_weights, slot_offset, *, nrow, ncol):
    panels, _, local_slots, blk, _ = panel_blocks.shape
    r = lax.axis_index("row")
    c = lax.axis_index("col")
    blocks = ring_gather(with_meta(panel_blocks, user_weights, slot_offset), ncol)
    n = panels * blocks.shape[1]
    blocks = blocks.reshape(n, local_slots, blk + META, blk)

    src = c // local_slots
    own = lax.dynamic_index_in_dim(blocks, c % local_slots, axis=1, keepdims=False)
    column_blocks = broadcast_slot(own, r, src, nrow, ncol, local_slots)

    offs = jnp.concatenate([blocks[:, :, blk + 3, 0], column_blocks[:, blk + 3, 0][:, None]], axis=1)
    offs = jnp.clip(offs.astype(jnp.int32), 0, IBS - 1).reshape(-1)
    return gram_call(offs, blocks, column_blocks)


def solution(mesh):
    nrow, ncol = mesh.shape["row"], mesh.shape["col"]
    return jax.shard_map(
        functools.partial(local, nrow=nrow, ncol=ncol),
        mesh=mesh,
        in_specs=(P(None, "col", "row", None, None), P(None, "col", None), P(None, "col", "row")),
        out_specs=P("row", "col"),
        check_vma=False,
    )
```

```python
import functools

import jax
import jax.numpy as jnp
from jax import lax
from jax.experimental import pallas as pl
from jax.experimental.pallas import tpu as pltpu
from jax.sharding import PartitionSpec as P

IBS = 8
CHUNK = 8
META = 16


def gram_kernel(offs_ref, bs_ref, bc_ref, o_ref, *, chunk, local_slots, blk):
    step = pl.program_id(0)

    @pl.when(step == 0)
    def _():
        o_ref[...] = jnp.zeros_like(o_ref)

    stride = local_slots + 1
    for k in range(chunk):
        g = step * chunk + k
        meta = bs_ref[k, 0, blk : blk + META].astype(jnp.float32)
        w = meta[0:1] + meta[1:2] + meta[2:3]
        lhs = jnp.concatenate(
            [
                (bs_ref[k, s, :blk].astype(jnp.float32).T * w).astype(jnp.bfloat16)
                for s in range(local_slots)
            ],
            axis=0,
        )
        prod = jnp.dot(lhs, bc_ref[k, :blk], preferred_element_type=jnp.float32)
        col = pl.multiple_of(offs_ref[g * stride + local_slots] * blk, blk)
        for s in range(local_slots):
            row = pl.multiple_of((s * IBS + offs_ref[g * stride + s]) * blk, blk)
            o_ref[pl.ds(row, blk), pl.ds(col, blk)] += prod[s * blk : (s + 1) * blk]


def gram_call(offs, bs, bc):
    n, local_slots, rows, blk = bs.shape
    chunk = CHUNK
    kernel = functools.partial(gram_kernel, chunk=chunk, local_slots=local_slots, blk=blk)
    out_rows, out_cols = local_slots * IBS * blk, IBS * blk
    return pl.pallas_call(
        kernel,
        grid_spec=pltpu.PrefetchScalarGridSpec(
            num_scalar_prefetch=1,
            grid=(n // chunk,),
            in_specs=[
                pl.BlockSpec((chunk, local_slots, rows, blk), lambda i, o: (i, 0, 0, 0)),
                pl.BlockSpec((chunk, rows, blk), lambda i, o: (i, 0, 0)),
            ],
            out_specs=pl.BlockSpec((out_rows, out_cols), lambda i, o: (0, 0)),
        ),
        out_shape=jax.ShapeDtypeStruct((out_rows, out_cols), jnp.float32),
        compiler_params=pltpu.CompilerParams(
            dimension_semantics=("arbitrary",), vmem_limit_bytes=48 * 1024 * 1024
        ),
        cost_estimate=pl.CostEstimate(
            flops=2 * n * local_slots * blk * blk * blk,
            transcendentals=0,
            bytes_accessed=n * (local_slots + 1) * blk * blk * 2 + out_rows * out_cols * 4,
        ),
    )(offs, bs, bc)


def with_meta(panel_blocks, user_weights, slot_offset):
    panels, users, local_slots, blk, _ = panel_blocks.shape
    hi = lax.reduce_precision(user_weights, exponent_bits=8, mantissa_bits=7)
    rest = user_weights - hi
    mid = lax.reduce_precision(rest, exponent_bits=8, mantissa_bits=7)
    low = rest - mid
    weight_rows = jnp.stack([hi, mid, low], axis=2).astype(jnp.bfloat16)[:, :, None]
    weight_rows = jnp.broadcast_to(weight_rows, (panels, users, local_slots, 3, blk))
    offset_rows = jnp.broadcast_to(
        slot_offset.astype(jnp.bfloat16)[..., None, None], (panels, users, local_slots, 1, blk)
    )
    pad = jnp.zeros((panels, users, local_slots, META - 4, blk), jnp.bfloat16)
    return jnp.concatenate([panel_blocks, weight_rows, offset_rows, pad], axis=3)


def local(panel_blocks, user_weights, slot_offset, *, nrow, ncol):
    panels, _, local_slots, blk, _ = panel_blocks.shape
    r = lax.axis_index("row")
    c = lax.axis_index("col")
    x = with_meta(panel_blocks, user_weights, slot_offset)

    outer = ncol // 2
    cycle = [a * 2 for a in range(outer)] + [a * 2 + 1 for a in reversed(range(outer))]
    forward = [(cycle[i], cycle[(i + 1) % ncol]) for i in range(ncol)]
    backward = [(b, a) for a, b in forward]

    src = c // local_slots
    which = (r - src + nrow) % nrow
    slot = c % local_slots
    fans = [
        [
            ((cc // local_slots) * ncol + cc, ((cc // local_slots + j) % nrow) * ncol + cc)
            for cc in range(ncol)
        ]
        for j in range(1, nrow)
    ]

    def pick_slot(piece):
        return lax.dynamic_index_in_dim(piece, slot, axis=2, keepdims=False)

    half = x.shape[1] // 2
    a, b = x[:, :half], x[:, half:]
    pieces, columns = [], []
    for step in range(ncol):
        if step:
            a = lax.ppermute(a, "col", forward)
            b = lax.ppermute(b, "col", backward)
        pieces += [a, b]
        own = jnp.concatenate([pick_slot(a), pick_slot(b)], axis=1)
        got = own
        for j, fan in enumerate(fans, start=1):
            got = jnp.where(which == j, lax.ppermute(own, ("row", "col"), fan), got)
        columns.append(got)

    blocks = jnp.concatenate(pieces, axis=1)
    column_blocks = jnp.concatenate(columns, axis=1)
    n = panels * blocks.shape[1]
    blocks = blocks.reshape(n, local_slots, blk + META, blk)
    column_blocks = column_blocks.reshape(n, blk + META, blk)

    offs = jnp.concatenate([blocks[:, :, blk + 3, 0], column_blocks[:, blk + 3, 0][:, None]], axis=1)
    offs = jnp.clip(offs.astype(jnp.int32), 0, IBS - 1).reshape(-1)
    return gram_call(offs, blocks, column_blocks)


def solution(mesh):
    nrow, ncol = mesh.shape["row"], mesh.shape["col"]
    return jax.shard_map(
        functools.partial(local, nrow=nrow, ncol=ncol),
        mesh=mesh,
        in_specs=(P(None, "col", "row", None, None), P(None, "col", None), P(None, "col", "row")),
        out_specs=P("row", "col"),
        check_vma=False,
    )
```

```python
import functools

import jax
import jax.numpy as jnp
from jax import lax
from jax.experimental import pallas as pl
from jax.experimental.pallas import tpu as pltpu
from jax.sharding import PartitionSpec as P

IBS = 8
CHUNK = 8
META = 16


def gram_kernel(offs_ref, *refs, pieces, halves, local_slots, blk):
    o_ref = refs[-1]
    w_refs, c_refs = refs[:pieces], refs[pieces:-1]
    p = pl.program_id(0)

    @pl.when(p == 0)
    def _():
        o_ref[...] = jnp.zeros_like(o_ref)

    stride = local_slots + 1
    for k in range(pieces):
        for h in range(halves):
            g = (p * pieces + k) * halves + h
            w_ref = w_refs[k]
            meta = w_ref[0, h, 0, blk : blk + META].astype(jnp.float32)
            w = meta[0:1] + meta[1:2] + meta[2:3]
            lhs = jnp.concatenate(
                [
                    (w_ref[0, h, s, :blk].astype(jnp.float32).T * w).astype(jnp.bfloat16)
                    for s in range(local_slots)
                ],
                axis=0,
            )
            rhs = c_refs[k // 2][0, (k % 2) * halves + h, :blk]
            prod = jnp.dot(lhs, rhs, preferred_element_type=jnp.float32)
            col = pl.multiple_of(offs_ref[g * stride + local_slots] * blk, blk)
            for s in range(local_slots):
                row = pl.multiple_of((s * IBS + offs_ref[g * stride + s]) * blk, blk)
                o_ref[pl.ds(row, blk), pl.ds(col, blk)] += prod[s * blk : (s + 1) * blk]


def gram_call(offs, w_pieces, c_pieces):
    panels, halves, local_slots, rows, blk = w_pieces[0].shape
    pieces = len(w_pieces)
    kernel = functools.partial(
        gram_kernel, pieces=pieces, halves=halves, local_slots=local_slots, blk=blk
    )
    out_rows, out_cols = local_slots * IBS * blk, IBS * blk
    n = panels * pieces * halves
    w_spec = pl.BlockSpec((1, halves, local_slots, rows, blk), lambda i, o: (i, 0, 0, 0, 0))
    c_spec = pl.BlockSpec((1, 2 * halves, rows, blk), lambda i, o: (i, 0, 0, 0))
    return pl.pallas_call(
        kernel,
        grid_spec=pltpu.PrefetchScalarGridSpec(
            num_scalar_prefetch=1,
            grid=(panels,),
            in_specs=[w_spec] * pieces + [c_spec] * len(c_pieces),
            out_specs=pl.BlockSpec((out_rows, out_cols), lambda i, o: (0, 0)),
        ),
        out_shape=jax.ShapeDtypeStruct((out_rows, out_cols), jnp.float32),
        compiler_params=pltpu.CompilerParams(
            dimension_semantics=("arbitrary",), vmem_limit_bytes=56 * 1024 * 1024
        ),
        cost_estimate=pl.CostEstimate(
            flops=2 * n * local_slots * blk * blk * blk,
            transcendentals=0,
            bytes_accessed=n * (local_slots + 1) * blk * blk * 2 + out_rows * out_cols * 4,
        ),
    )(offs, *w_pieces, *c_pieces)


def with_meta(panel_blocks, user_weights, slot_offset):
    panels, users, local_slots, blk, _ = panel_blocks.shape
    hi = lax.reduce_precision(user_weights, exponent_bits=8, mantissa_bits=7)
    rest = user_weights - hi
    mid = lax.reduce_precision(rest, exponent_bits=8, mantissa_bits=7)
    low = rest - mid
    weight_rows = jnp.stack([hi, mid, low], axis=2).astype(jnp.bfloat16)[:, :, None]
    weight_rows = jnp.broadcast_to(weight_rows, (panels, users, local_slots, 3, blk))
    offset_rows = jnp.broadcast_to(
        slot_offset.astype(jnp.bfloat16)[..., None, None], (panels, users, local_slots, 1, blk)
    )
    pad = jnp.zeros((panels, users, local_slots, META - 4, blk), jnp.bfloat16)
    return jnp.concatenate([panel_blocks, weight_rows, offset_rows, pad], axis=3)


def local(panel_blocks, user_weights, slot_offset, *, nrow, ncol):
    panels, _, local_slots, blk, _ = panel_blocks.shape
    r = lax.axis_index("row")
    c = lax.axis_index("col")
    x = with_meta(panel_blocks, user_weights, slot_offset)

    outer = ncol // 2
    cycle = [a * 2 for a in range(outer)] + [a * 2 + 1 for a in reversed(range(outer))]
    forward = [(cycle[i], cycle[(i + 1) % ncol]) for i in range(ncol)]
    backward = [(b, a) for a, b in forward]

    src = c // local_slots
    slot = c % local_slots
    nx = nrow // 2
    up = (r - src + nrow) % nrow
    is_s, is_p, is_d1 = up == 0, r == src + 1 - 2 * (src % 2), (up % 2 == 0) & (up != 0)
    chip_step = up // 2

    def send(v, pairs):
        return lax.ppermute(v, ("row", "col"), [(a * ncol + cc, b * ncol + cc) for a, b, cc in pairs])

    first_hop = []
    for cc in range(ncol):
        s0 = cc // local_slots
        first_hop.append((s0, s0 ^ 1, cc))
        first_hop += [((s0 + 2 * j) % nrow, ((s0 + 2 * j) % nrow) ^ 1, cc) for j in range(1, nx)]
    cross = [[(cc // local_slots, (cc // local_slots + 2 * j) % nrow, cc) for cc in range(ncol)] for j in range(1, nx)]

    def pick_slot(piece):
        return lax.dynamic_index_in_dim(piece, slot, axis=2, keepdims=False)

    half = x.shape[1] // 2
    a, b = x[:, :half], x[:, half:]
    pieces, owns, hops, crossed = [], [], [], []
    forwarded = None
    for step in range(ncol + 1):
        if step < ncol:
            if step:
                a = lax.ppermute(a, "col", forward)
                b = lax.ppermute(b, "col", backward)
            pieces += [a, b]
            own = jnp.concatenate([pick_slot(a), pick_slot(b)], axis=1)
            owns.append(own)
            operand = own if forwarded is None else jnp.where(is_s, own, forwarded)
        else:
            operand = forwarded
        hops.append(send(operand, first_hop))
        if step < ncol:
            got = None
            for j, pairs in enumerate(cross, start=1):
                v = send(own, pairs)
                got = v if got is None else jnp.where(chip_step == j, v, got)
            crossed.append(got)
            forwarded = got

    columns = [
        jnp.where(is_s, owns[k], jnp.where(is_p, hops[k], jnp.where(is_d1, crossed[k], hops[k + 1])))
        for k in range(ncol)
    ]

    w_offs = jnp.stack([piece[:, :, :, blk + 3, 0] for piece in pieces], axis=1)
    c_offs = jnp.stack(
        [columns[k // 2][:, (k % 2) * half : (k % 2 + 1) * half, blk + 3, 0] for k in range(2 * ncol)],
        axis=1,
    )
    offs = jnp.concatenate([w_offs, c_offs[..., None]], axis=3)
    offs = jnp.clip(offs.astype(jnp.int32), 0, IBS - 1).reshape(-1)
    return gram_call(offs, pieces, columns)


def solution(mesh):
    nrow, ncol = mesh.shape["row"], mesh.shape["col"]
    return jax.shard_map(
        functools.partial(local, nrow=nrow, ncol=ncol),
        mesh=mesh,
        in_specs=(P(None, "col", "row", None, None), P(None, "col", None), P(None, "col", "row")),
        out_specs=P("row", "col"),
        check_vma=False,
    )
```

```python
import functools

import jax
import jax.numpy as jnp
from jax import lax
from jax.experimental import pallas as pl
from jax.experimental.pallas import tpu as pltpu
from jax.sharding import PartitionSpec as P

IBS = 8
CHUNK = 8
META = 16


def gram_kernel(offs_ref, *refs, pieces, halves, local_slots, blk):
    o_ref = refs[-1]
    w_refs, c_refs = refs[:pieces], refs[pieces:-1]
    p = pl.program_id(0)

    @pl.when(p == 0)
    def _():
        o_ref[...] = jnp.zeros_like(o_ref)

    stride = local_slots + 1
    for k in range(pieces):
        for h in range(halves):
            g = (p * pieces + k) * halves + h
            w_ref = w_refs[k]
            meta = w_ref[0, h, 0, blk : blk + META].astype(jnp.float32)
            w = meta[0:1] + meta[1:2] + meta[2:3]
            lhs = jnp.concatenate(
                [
                    (w_ref[0, h, s, :blk].astype(jnp.float32).T * w).astype(jnp.bfloat16)
                    for s in range(local_slots)
                ],
                axis=0,
            )
            rhs = c_refs[k // 2][0, (k % 2) * halves + h, :blk]
            prod = jnp.dot(lhs, rhs, preferred_element_type=jnp.float32)
            col = pl.multiple_of(offs_ref[g * stride + local_slots] * blk, blk)
            for s in range(local_slots):
                row = pl.multiple_of((s * IBS + offs_ref[g * stride + s]) * blk, blk)
                o_ref[pl.ds(row, blk), pl.ds(col, blk)] += prod[s * blk : (s + 1) * blk]


def gram_call(offs, w_pieces, c_pieces):
    panels, halves, local_slots, rows, blk = w_pieces[0].shape
    pieces = len(w_pieces)
    kernel = functools.partial(
        gram_kernel, pieces=pieces, halves=halves, local_slots=local_slots, blk=blk
    )
    out_rows, out_cols = local_slots * IBS * blk, IBS * blk
    n = panels * pieces * halves
    w_spec = pl.BlockSpec((1, halves, local_slots, rows, blk), lambda i, o: (i, 0, 0, 0, 0))
    c_spec = pl.BlockSpec((1, 2 * halves, rows, blk), lambda i, o: (i, 0, 0, 0))
    return pl.pallas_call(
        kernel,
        grid_spec=pltpu.PrefetchScalarGridSpec(
            num_scalar_prefetch=1,
            grid=(panels,),
            in_specs=[w_spec] * pieces + [c_spec] * len(c_pieces),
            out_specs=pl.BlockSpec((out_rows, out_cols), lambda i, o: (0, 0)),
        ),
        out_shape=jax.ShapeDtypeStruct((out_rows, out_cols), jnp.float32),
        compiler_params=pltpu.CompilerParams(
            dimension_semantics=("arbitrary",), vmem_limit_bytes=56 * 1024 * 1024
        ),
        cost_estimate=pl.CostEstimate(
            flops=2 * n * local_slots * blk * blk * blk,
            transcendentals=0,
            bytes_accessed=n * (local_slots + 1) * blk * blk * 2 + out_rows * out_cols * 4,
        ),
    )(offs, *w_pieces, *c_pieces)


def with_meta(panel_blocks, user_weights, slot_offset):
    panels, users, local_slots, blk, _ = panel_blocks.shape
    hi = lax.reduce_precision(user_weights, exponent_bits=8, mantissa_bits=7)
    rest = user_weights - hi
    mid = lax.reduce_precision(rest, exponent_bits=8, mantissa_bits=7)
    low = rest - mid
    weight_rows = jnp.stack([hi, mid, low], axis=2).astype(jnp.bfloat16)[:, :, None]
    weight_rows = jnp.broadcast_to(weight_rows, (panels, users, local_slots, 3, blk))
    offset_rows = jnp.broadcast_to(
        slot_offset.astype(jnp.bfloat16)[..., None, None], (panels, users, local_slots, 1, blk)
    )
    pad = jnp.zeros((panels, users, local_slots, META - 4, blk), jnp.bfloat16)
    return jnp.concatenate([panel_blocks, weight_rows, offset_rows, pad], axis=3)


def local(panel_blocks, user_weights, slot_offset, *, nrow, ncol):
    panels, _, local_slots, blk, _ = panel_blocks.shape
    r = lax.axis_index("row")
    c = lax.axis_index("col")
    x = with_meta(panel_blocks, user_weights, slot_offset)

    outer = ncol // 2
    cycle = [a * 2 for a in range(outer)] + [a * 2 + 1 for a in reversed(range(outer))]
    forward = [(cycle[i], cycle[(i + 1) % ncol]) for i in range(ncol)]
    backward = [(b, a) for a, b in forward]

    src = c // local_slots
    which = (r - src + nrow) % nrow
    slot = c % local_slots
    fans = [
        [
            ((cc // local_slots) * ncol + cc, ((cc // local_slots + j) % nrow) * ncol + cc)
            for cc in range(ncol)
        ]
        for j in range(1, nrow)
    ]

    def pick_slot(piece):
        return lax.dynamic_index_in_dim(piece, slot, axis=2, keepdims=False)

    half = x.shape[1] // 2
    a, b = x[:, :half], x[:, half:]
    pieces, columns = [], []
    for step in range(ncol):
        if step:
            a = lax.ppermute(a, "col", forward)
            b = lax.ppermute(b, "col", backward)
        pieces += [a, b]
        own = jnp.concatenate([pick_slot(a), pick_slot(b)], axis=1)
        got = own
        for j, fan in enumerate(fans, start=1):
            got = jnp.where(which == j, lax.ppermute(own, ("row", "col"), fan), got)
        columns.append(got)

    w_offs = jnp.stack([piece[:, :, :, blk + 3, 0] for piece in pieces], axis=1)
    c_offs = jnp.stack(
        [columns[k // 2][:, (k % 2) * half : (k % 2 + 1) * half, blk + 3, 0] for k in range(2 * ncol)],
        axis=1,
    )
    offs = jnp.concatenate([w_offs, c_offs[..., None]], axis=3)
    offs = jnp.clip(offs.astype(jnp.int32), 0, IBS - 1).reshape(-1)
    return gram_call(offs, pieces, columns)


def solution(mesh):
    nrow, ncol = mesh.shape["row"], mesh.shape["col"]
    return jax.shard_map(
        functools.partial(local, nrow=nrow, ncol=ncol),
        mesh=mesh,
        in_specs=(P(None, "col", "row", None, None), P(None, "col", None), P(None, "col", "row")),
        out_specs=P("row", "col"),
        check_vma=False,
    )
```

```python
import functools

import jax
import jax.numpy as jnp
from jax import lax
from jax.experimental import pallas as pl
from jax.experimental.pallas import tpu as pltpu
from jax.sharding import PartitionSpec as P

IBS = 8
CHUNK = 8
META = 16


def gram_kernel(offs_ref, bs_ref, bc_ref, o_ref, *, chunk, local_slots, blk):
    step = pl.program_id(0)

    @pl.when(step == 0)
    def _():
        o_ref[...] = jnp.zeros_like(o_ref)

    stride = local_slots + 1
    for k in range(chunk):
        g = step * chunk + k
        meta = bs_ref[k, 0, blk : blk + META].astype(jnp.float32)
        w = meta[0:1] + meta[1:2] + meta[2:3]
        lhs = jnp.concatenate(
            [
                (bs_ref[k, s, :blk].astype(jnp.float32).T * w).astype(jnp.bfloat16)
                for s in range(local_slots)
            ],
            axis=0,
        )
        prod = jnp.dot(lhs, bc_ref[k, :blk], preferred_element_type=jnp.float32)
        col = pl.multiple_of(offs_ref[g * stride + local_slots] * blk, blk)
        for s in range(local_slots):
            row = pl.multiple_of((s * IBS + offs_ref[g * stride + s]) * blk, blk)
            o_ref[pl.ds(row, blk), pl.ds(col, blk)] += prod[s * blk : (s + 1) * blk]


def gram_call(offs, bs, bc):
    n, local_slots, rows, blk = bs.shape
    chunk = CHUNK
    kernel = functools.partial(gram_kernel, chunk=chunk, local_slots=local_slots, blk=blk)
    out_rows, out_cols = local_slots * IBS * blk, IBS * blk
    return pl.pallas_call(
        kernel,
        grid_spec=pltpu.PrefetchScalarGridSpec(
            num_scalar_prefetch=1,
            grid=(n // chunk,),
            in_specs=[
                pl.BlockSpec((chunk, local_slots, rows, blk), lambda i, o: (i, 0, 0, 0)),
                pl.BlockSpec((chunk, rows, blk), lambda i, o: (i, 0, 0)),
            ],
            out_specs=pl.BlockSpec((out_rows, out_cols), lambda i, o: (0, 0)),
        ),
        out_shape=jax.ShapeDtypeStruct((out_rows, out_cols), jnp.float32),
        compiler_params=pltpu.CompilerParams(
            dimension_semantics=("arbitrary",), vmem_limit_bytes=48 * 1024 * 1024
        ),
        cost_estimate=pl.CostEstimate(
            flops=2 * n * local_slots * blk * blk * blk,
            transcendentals=0,
            bytes_accessed=n * (local_slots + 1) * blk * blk * 2 + out_rows * out_cols * 4,
        ),
    )(offs, bs, bc)


def with_meta(panel_blocks, user_weights, slot_offset):
    panels, users, local_slots, blk, _ = panel_blocks.shape
    hi = lax.reduce_precision(user_weights, exponent_bits=8, mantissa_bits=7)
    rest = user_weights - hi
    mid = lax.reduce_precision(rest, exponent_bits=8, mantissa_bits=7)
    low = rest - mid
    weight_rows = jnp.stack([hi, mid, low], axis=2).astype(jnp.bfloat16)[:, :, None]
    weight_rows = jnp.broadcast_to(weight_rows, (panels, users, local_slots, 3, blk))
    offset_rows = jnp.broadcast_to(
        slot_offset.astype(jnp.bfloat16)[..., None, None], (panels, users, local_slots, 1, blk)
    )
    pad = jnp.zeros((panels, users, local_slots, META - 4, blk), jnp.bfloat16)
    return jnp.concatenate([panel_blocks, weight_rows, offset_rows, pad], axis=3)


def local(panel_blocks, user_weights, slot_offset, *, nrow, ncol):
    panels, _, local_slots, blk, _ = panel_blocks.shape
    r = lax.axis_index("row")
    c = lax.axis_index("col")
    x = with_meta(panel_blocks, user_weights, slot_offset)

    outer = ncol // 2
    cycle = [a * 2 for a in range(outer)] + [a * 2 + 1 for a in reversed(range(outer))]
    forward = [(cycle[i], cycle[(i + 1) % ncol]) for i in range(ncol)]
    backward = [(b, a) for a, b in forward]

    src = c // local_slots
    slot = c % local_slots
    nx = nrow // 2
    up = (r - src + nrow) % nrow
    is_s, is_p, is_d1 = up == 0, r == src + 1 - 2 * (src % 2), (up % 2 == 0) & (up != 0)
    chip_step = up // 2

    def send(v, pairs):
        return lax.ppermute(v, ("row", "col"), [(a * ncol + cc, b * ncol + cc) for a, b, cc in pairs])

    first_hop = []
    for cc in range(ncol):
        s0 = cc // local_slots
        first_hop.append((s0, s0 ^ 1, cc))
        first_hop += [((s0 + 2 * j) % nrow, ((s0 + 2 * j) % nrow) ^ 1, cc) for j in range(1, nx)]
    cross = [[(cc // local_slots, (cc // local_slots + 2 * j) % nrow, cc) for cc in range(ncol)] for j in range(1, nx)]

    def pick_slot(piece):
        return lax.dynamic_index_in_dim(piece, slot, axis=2, keepdims=False)

    half = x.shape[1] // 2
    a, b = x[:, :half], x[:, half:]
    pieces, owns, hops, crossed = [], [], [], []
    forwarded = None
    for step in range(ncol + 1):
        if step < ncol:
            if step:
                a = lax.ppermute(a, "col", forward)
                b = lax.ppermute(b, "col", backward)
            pieces += [a, b]
            own = jnp.concatenate([pick_slot(a), pick_slot(b)], axis=1)
            owns.append(own)
            operand = own if forwarded is None else jnp.where(is_s, own, forwarded)
        else:
            operand = forwarded
        hops.append(send(operand, first_hop))
        if step < ncol:
            got = None
            for j, pairs in enumerate(cross, start=1):
                v = send(own, pairs)
                got = v if got is None else jnp.where(chip_step == j, v, got)
            crossed.append(got)
            forwarded = got

    columns = [
        jnp.where(is_s, owns[k], jnp.where(is_p, hops[k], jnp.where(is_d1, crossed[k], hops[k + 1])))
        for k in range(ncol)
    ]

    blocks = jnp.concatenate(pieces, axis=1)
    column_blocks = jnp.concatenate(columns, axis=1)
    n = panels * blocks.shape[1]
    blocks = blocks.reshape(n, local_slots, blk + META, blk)
    column_blocks = column_blocks.reshape(n, blk + META, blk)

    offs = jnp.concatenate([blocks[:, :, blk + 3, 0], column_blocks[:, blk + 3, 0][:, None]], axis=1)
    offs = jnp.clip(offs.astype(jnp.int32), 0, IBS - 1).reshape(-1)
    return gram_call(offs, blocks, column_blocks)


def solution(mesh):
    nrow, ncol = mesh.shape["row"], mesh.shape["col"]
    return jax.shard_map(
        functools.partial(local, nrow=nrow, ncol=ncol),
        mesh=mesh,
        in_specs=(P(None, "col", "row", None, None), P(None, "col", None), P(None, "col", "row")),
        out_specs=P("row", "col"),
        check_vma=False,
    )
```

```python
import functools

import jax
import jax.numpy as jnp
from jax import lax
from jax.experimental import pallas as pl
from jax.experimental.pallas import tpu as pltpu
from jax.sharding import PartitionSpec as P

IBS = 8
CHUNK = 8
META = 16


def gram_kernel(offs_ref, bs_ref, bc_ref, o_ref, *, chunk, local_slots, blk):
    step = pl.program_id(0)

    @pl.when(step == 0)
    def _():
        o_ref[...] = jnp.zeros_like(o_ref)

    stride = local_slots + 1
    for k in range(chunk):
        g = step * chunk + k
        meta = bs_ref[k, 0, blk : blk + META].astype(jnp.float32)
        w = meta[0:1] + meta[1:2] + meta[2:3]
        lhs = jnp.concatenate(
            [
                (bs_ref[k, s, :blk].astype(jnp.float32).T * w).astype(jnp.bfloat16)
                for s in range(local_slots)
            ],
            axis=0,
        )
        prod = jnp.dot(lhs, bc_ref[k, :blk], preferred_element_type=jnp.float32)
        col = pl.multiple_of(offs_ref[g * stride + local_slots] * blk, blk)
        for s in range(local_slots):
            row = pl.multiple_of((s * IBS + offs_ref[g * stride + s]) * blk, blk)
            o_ref[pl.ds(row, blk), pl.ds(col, blk)] += prod[s * blk : (s + 1) * blk]


def gram_call(offs, bs, bc):
    n, local_slots, rows, blk = bs.shape
    chunk = CHUNK
    kernel = functools.partial(gram_kernel, chunk=chunk, local_slots=local_slots, blk=blk)
    out_rows, out_cols = local_slots * IBS * blk, IBS * blk
    return pl.pallas_call(
        kernel,
        grid_spec=pltpu.PrefetchScalarGridSpec(
            num_scalar_prefetch=1,
            grid=(n // chunk,),
            in_specs=[
                pl.BlockSpec((chunk, local_slots, rows, blk), lambda i, o: (i, 0, 0, 0)),
                pl.BlockSpec((chunk, rows, blk), lambda i, o: (i, 0, 0)),
            ],
            out_specs=pl.BlockSpec((out_rows, out_cols), lambda i, o: (0, 0)),
        ),
        out_shape=jax.ShapeDtypeStruct((out_rows, out_cols), jnp.float32),
        compiler_params=pltpu.CompilerParams(
            dimension_semantics=("arbitrary",), vmem_limit_bytes=48 * 1024 * 1024
        ),
        cost_estimate=pl.CostEstimate(
            flops=2 * n * local_slots * blk * blk * blk,
            transcendentals=0,
            bytes_accessed=n * (local_slots + 1) * blk * blk * 2 + out_rows * out_cols * 4,
        ),
    )(offs, bs, bc)


def with_meta(panel_blocks, user_weights, slot_offset):
    panels, users, local_slots, blk, _ = panel_blocks.shape
    hi = lax.reduce_precision(user_weights, exponent_bits=8, mantissa_bits=7)
    rest = user_weights - hi
    mid = lax.reduce_precision(rest, exponent_bits=8, mantissa_bits=7)
    low = rest - mid
    weight_rows = jnp.stack([hi, mid, low], axis=2).astype(jnp.bfloat16)[:, :, None]
    weight_rows = jnp.broadcast_to(weight_rows, (panels, users, local_slots, 3, blk))
    offset_rows = jnp.broadcast_to(
        slot_offset.astype(jnp.bfloat16)[..., None, None], (panels, users, local_slots, 1, blk)
    )
    pad = jnp.zeros((panels, users, local_slots, META - 4, blk), jnp.bfloat16)
    return jnp.concatenate([panel_blocks, weight_rows, offset_rows, pad], axis=3)


def local(panel_blocks, user_weights, slot_offset, *, nrow, ncol):
    panels, _, local_slots, blk, _ = panel_blocks.shape
    r = lax.axis_index("row")
    c = lax.axis_index("col")
    x = with_meta(panel_blocks, user_weights, slot_offset)

    outer = ncol // 2
    cycle = [a * 2 for a in range(outer)] + [a * 2 + 1 for a in reversed(range(outer))]
    forward = [(cycle[i], cycle[(i + 1) % ncol]) for i in range(ncol)]
    backward = [(b, a) for a, b in forward]

    src = c // local_slots
    which = (r - src + nrow) % nrow
    slot = c % local_slots
    fans = [
        [
            ((cc // local_slots) * ncol + cc, ((cc // local_slots + j) % nrow) * ncol + cc)
            for cc in range(ncol)
        ]
        for j in range(1, nrow)
    ]

    def pick_slot(piece):
        return lax.dynamic_index_in_dim(piece, slot, axis=2, keepdims=False)

    batches = [[k, k + 1] for k in range(0, ncol - 2, 2)] + [[ncol - 2], [ncol - 1]]
    half = x.shape[1] // 2
    a, b = x[:, :half], x[:, half:]
    pieces, columns, pending = [], [], []
    for step in range(ncol):
        if step:
            a = lax.ppermute(a, "col", forward)
            b = lax.ppermute(b, "col", backward)
        pieces += [a, b]
        pending += [pick_slot(a), pick_slot(b)]
        if any(batch[-1] == step for batch in batches):
            own = jnp.concatenate(pending, axis=1)
            pending = []
            got = own
            for j, fan in enumerate(fans, start=1):
                got = jnp.where(which == j, lax.ppermute(own, ("row", "col"), fan), got)
            columns.append(got)

    blocks = jnp.concatenate(pieces, axis=1)
    column_blocks = jnp.concatenate(columns, axis=1)
    n = panels * blocks.shape[1]
    blocks = blocks.reshape(n, local_slots, blk + META, blk)
    column_blocks = column_blocks.reshape(n, blk + META, blk)

    offs = jnp.concatenate([blocks[:, :, blk + 3, 0], column_blocks[:, blk + 3, 0][:, None]], axis=1)
    offs = jnp.clip(offs.astype(jnp.int32), 0, IBS - 1).reshape(-1)
    return gram_call(offs, blocks, column_blocks)


def solution(mesh):
    nrow, ncol = mesh.shape["row"], mesh.shape["col"]
    return jax.shard_map(
        functools.partial(local, nrow=nrow, ncol=ncol),
        mesh=mesh,
        in_specs=(P(None, "col", "row", None, None), P(None, "col", None), P(None, "col", "row")),
        out_specs=P("row", "col"),
        check_vma=False,
    )
```

```python
import functools

import jax
import jax.numpy as jnp
from jax import lax
from jax.experimental import pallas as pl
from jax.experimental.pallas import tpu as pltpu
from jax.sharding import PartitionSpec as P

IBS = 8
CHUNK = 8
META = 16


def gram_kernel(offs_ref, bs_ref, bc_ref, *refs, chunk, local_slots, blk):
    o_ref = refs[-1]
    step = pl.program_id(0)

    @pl.when(step == 0)
    def _():
        if len(refs) == 2:
            o_ref[...] = refs[0][...]
        else:
            o_ref[...] = jnp.zeros_like(o_ref)

    stride = local_slots + 1
    for k in range(chunk):
        g = step * chunk + k
        meta = bs_ref[k, 0, blk : blk + META].astype(jnp.float32)
        w = meta[0:1] + meta[1:2] + meta[2:3]
        lhs = jnp.concatenate(
            [
                (bs_ref[k, s, :blk].astype(jnp.float32).T * w).astype(jnp.bfloat16)
                for s in range(local_slots)
            ],
            axis=0,
        )
        prod = jnp.dot(lhs, bc_ref[k, :blk], preferred_element_type=jnp.float32)
        col = pl.multiple_of(offs_ref[g * stride + local_slots] * blk, blk)
        for s in range(local_slots):
            row = pl.multiple_of((s * IBS + offs_ref[g * stride + s]) * blk, blk)
            o_ref[pl.ds(row, blk), pl.ds(col, blk)] += prod[s * blk : (s + 1) * blk]


def gram_call(offs, bs, bc, acc=None):
    n, local_slots, rows, blk = bs.shape
    chunk = CHUNK
    kernel = functools.partial(gram_kernel, chunk=chunk, local_slots=local_slots, blk=blk)
    out_rows, out_cols = local_slots * IBS * blk, IBS * blk
    acc_specs = [] if acc is None else [pl.BlockSpec((out_rows, out_cols), lambda i, o: (0, 0))]
    acc_args = () if acc is None else (acc,)
    return pl.pallas_call(
        kernel,
        grid_spec=pltpu.PrefetchScalarGridSpec(
            num_scalar_prefetch=1,
            grid=(n // chunk,),
            in_specs=[
                pl.BlockSpec((chunk, local_slots, rows, blk), lambda i, o: (i, 0, 0, 0)),
                pl.BlockSpec((chunk, rows, blk), lambda i, o: (i, 0, 0)),
            ]
            + acc_specs,
            out_specs=pl.BlockSpec((out_rows, out_cols), lambda i, o: (0, 0)),
        ),
        out_shape=jax.ShapeDtypeStruct((out_rows, out_cols), jnp.float32),
        input_output_aliases={} if acc is None else {3: 0},
        compiler_params=pltpu.CompilerParams(
            dimension_semantics=("arbitrary",), vmem_limit_bytes=56 * 1024 * 1024
        ),
        cost_estimate=pl.CostEstimate(
            flops=2 * n * local_slots * blk * blk * blk,
            transcendentals=0,
            bytes_accessed=n * (local_slots + 1) * blk * blk * 2 + out_rows * out_cols * 4,
        ),
    )(offs, bs, bc, *acc_args)


def with_meta(panel_blocks, user_weights, slot_offset):
    panels, users, local_slots, blk, _ = panel_blocks.shape
    hi = lax.reduce_precision(user_weights, exponent_bits=8, mantissa_bits=7)
    rest = user_weights - hi
    mid = lax.reduce_precision(rest, exponent_bits=8, mantissa_bits=7)
    low = rest - mid
    weight_rows = jnp.stack([hi, mid, low], axis=2).astype(jnp.bfloat16)[:, :, None]
    weight_rows = jnp.broadcast_to(weight_rows, (panels, users, local_slots, 3, blk))
    offset_rows = jnp.broadcast_to(
        slot_offset.astype(jnp.bfloat16)[..., None, None], (panels, users, local_slots, 1, blk)
    )
    pad = jnp.zeros((panels, users, local_slots, META - 4, blk), jnp.bfloat16)
    return jnp.concatenate([panel_blocks, weight_rows, offset_rows, pad], axis=3)


def local(panel_blocks, user_weights, slot_offset, *, nrow, ncol):
    panels, _, local_slots, blk, _ = panel_blocks.shape
    r = lax.axis_index("row")
    c = lax.axis_index("col")
    x = with_meta(panel_blocks, user_weights, slot_offset)

    outer = ncol // 2
    cycle = [a * 2 for a in range(outer)] + [a * 2 + 1 for a in reversed(range(outer))]
    forward = [(cycle[i], cycle[(i + 1) % ncol]) for i in range(ncol)]
    backward = [(b, a) for a, b in forward]

    src = c // local_slots
    which = (r - src + nrow) % nrow
    slot = c % local_slots
    fans = [
        [
            ((cc // local_slots) * ncol + cc, ((cc // local_slots + j) % nrow) * ncol + cc)
            for cc in range(ncol)
        ]
        for j in range(1, nrow)
    ]

    def pick_slot(piece):
        return lax.dynamic_index_in_dim(piece, slot, axis=2, keepdims=False)

    batches = [[k, k + 1] for k in range(0, ncol - 2, 2)] + [[ncol - 2], [ncol - 1]]
    half = x.shape[1] // 2
    a, b = x[:, :half], x[:, half:]
    pieces, columns, pending = [], [], []
    for step in range(ncol):
        if step:
            a = lax.ppermute(a, "col", forward)
            b = lax.ppermute(b, "col", backward)
        pieces += [a, b]
        pending += [pick_slot(a), pick_slot(b)]
        if any(batch[-1] == step for batch in batches):
            own = jnp.concatenate(pending, axis=1)
            pending = []
            got = own
            for j, fan in enumerate(fans, start=1):
                got = jnp.where(which == j, lax.ppermute(own, ("row", "col"), fan), got)
            columns.append(got)

    split = len(pieces) - 4
    acc = None
    for w_part, c_part in ((pieces[:split], columns[:-2]), (pieces[split:], columns[-2:])):
        blocks = jnp.concatenate(w_part, axis=1)
        column_blocks = jnp.concatenate(c_part, axis=1)
        n = panels * blocks.shape[1]
        blocks = blocks.reshape(n, local_slots, blk + META, blk)
        column_blocks = column_blocks.reshape(n, blk + META, blk)
        offs = jnp.concatenate(
            [blocks[:, :, blk + 3, 0], column_blocks[:, blk + 3, 0][:, None]], axis=1
        )
        offs = jnp.clip(offs.astype(jnp.int32), 0, IBS - 1).reshape(-1)
        acc = gram_call(offs, blocks, column_blocks, acc)
    return acc


def solution(mesh):
    nrow, ncol = mesh.shape["row"], mesh.shape["col"]
    return jax.shard_map(
        functools.partial(local, nrow=nrow, ncol=ncol),
        mesh=mesh,
        in_specs=(P(None, "col", "row", None, None), P(None, "col", None), P(None, "col", "row")),
        out_specs=P("row", "col"),
        check_vma=False,
    )
```

```python
import functools

import jax
import jax.numpy as jnp
from jax import lax
from jax.experimental import pallas as pl
from jax.experimental.pallas import tpu as pltpu
from jax.sharding import PartitionSpec as P

IBS = 8
CHUNK = 8
META = 16


def gram_kernel(offs_ref, bs_ref, bc_ref, o_ref, *, chunk, local_slots, blk):
    step = pl.program_id(0)

    @pl.when(step == 0)
    def _():
        o_ref[...] = jnp.zeros_like(o_ref)

    stride = local_slots + 1
    for k in range(chunk):
        g = step * chunk + k
        meta = bs_ref[k, local_slots * blk : local_slots * blk + META].astype(jnp.float32)
        w = meta[0:1] + meta[1:2] + meta[2:3]
        lhs = jnp.concatenate(
            [
                (bs_ref[k, s * blk : (s + 1) * blk].astype(jnp.float32).T * w).astype(jnp.bfloat16)
                for s in range(local_slots)
            ],
            axis=0,
        )
        prod = jnp.dot(lhs, bc_ref[k, :blk], preferred_element_type=jnp.float32)
        col = pl.multiple_of(offs_ref[g * stride + local_slots] * blk, blk)
        for s in range(local_slots):
            row = pl.multiple_of((s * IBS + offs_ref[g * stride + s]) * blk, blk)
            o_ref[pl.ds(row, blk), pl.ds(col, blk)] += prod[s * blk : (s + 1) * blk]


def gram_call(offs, bs, bc, local_slots):
    n, rows, blk = bs.shape
    chunk = CHUNK
    kernel = functools.partial(gram_kernel, chunk=chunk, local_slots=local_slots, blk=blk)
    out_rows, out_cols = local_slots * IBS * blk, IBS * blk
    return pl.pallas_call(
        kernel,
        grid_spec=pltpu.PrefetchScalarGridSpec(
            num_scalar_prefetch=1,
            grid=(n // chunk,),
            in_specs=[
                pl.BlockSpec((chunk, rows, blk), lambda i, o: (i, 0, 0)),
                pl.BlockSpec((chunk, blk + META, blk), lambda i, o: (i, 0, 0)),
            ],
            out_specs=pl.BlockSpec((out_rows, out_cols), lambda i, o: (0, 0)),
        ),
        out_shape=jax.ShapeDtypeStruct((out_rows, out_cols), jnp.float32),
        compiler_params=pltpu.CompilerParams(
            dimension_semantics=("arbitrary",), vmem_limit_bytes=48 * 1024 * 1024
        ),
        cost_estimate=pl.CostEstimate(
            flops=2 * n * local_slots * blk * blk * blk,
            transcendentals=0,
            bytes_accessed=n * (local_slots + 1) * blk * blk * 2 + out_rows * out_cols * 4,
        ),
    )(offs, bs, bc)


def with_meta(panel_blocks, user_weights, slot_offset):
    panels, users, local_slots, blk, _ = panel_blocks.shape
    hi = lax.reduce_precision(user_weights, exponent_bits=8, mantissa_bits=7)
    rest = user_weights - hi
    mid = lax.reduce_precision(rest, exponent_bits=8, mantissa_bits=7)
    low = rest - mid
    weight_rows = jnp.stack([hi, mid, low], axis=2).astype(jnp.bfloat16)
    offset_rows = jnp.broadcast_to(
        slot_offset.astype(jnp.bfloat16)[..., None], (panels, users, local_slots, blk)
    )
    pad = jnp.zeros((panels, users, META - 3 - local_slots, blk), jnp.bfloat16)
    data = panel_blocks.reshape(panels, users, local_slots * blk, blk)
    return jnp.concatenate([data, weight_rows, offset_rows, pad], axis=2)


def local(panel_blocks, user_weights, slot_offset, *, nrow, ncol):
    panels, _, local_slots, blk, _ = panel_blocks.shape
    r = lax.axis_index("row")
    c = lax.axis_index("col")
    x = with_meta(panel_blocks, user_weights, slot_offset)

    outer = ncol // 2
    cycle = [a * 2 for a in range(outer)] + [a * 2 + 1 for a in reversed(range(outer))]
    forward = [(cycle[i], cycle[(i + 1) % ncol]) for i in range(ncol)]
    backward = [(b, a) for a, b in forward]

    src = c // local_slots
    which = (r - src + nrow) % nrow
    slot = c % local_slots
    fans = [
        [
            ((cc // local_slots) * ncol + cc, ((cc // local_slots + j) % nrow) * ncol + cc)
            for cc in range(ncol)
        ]
        for j in range(1, nrow)
    ]

    def pick_slot(piece):
        rows = lax.dynamic_slice_in_dim(piece, slot * blk, blk, axis=2)
        return jnp.concatenate([rows, piece[:, :, local_slots * blk :]], axis=2)

    batches = [[k, k + 1] for k in range(0, ncol - 2, 2)] + [[ncol - 2], [ncol - 1]]
    half = x.shape[1] // 2
    a, b = x[:, :half], x[:, half:]
    pieces, columns, pending = [], [], []
    for step in range(ncol):
        if step:
            a = lax.ppermute(a, "col", forward)
            b = lax.ppermute(b, "col", backward)
        pieces += [a, b]
        pending += [pick_slot(a), pick_slot(b)]
        if any(batch[-1] == step for batch in batches):
            own = jnp.concatenate(pending, axis=1)
            pending = []
            got = own
            for j, fan in enumerate(fans, start=1):
                got = jnp.where(which == j, lax.ppermute(own, ("row", "col"), fan), got)
            columns.append(got)

    blocks = jnp.concatenate(pieces, axis=1)
    column_blocks = jnp.concatenate(columns, axis=1)
    n = panels * blocks.shape[1]
    blocks = blocks.reshape(n, local_slots * blk + META, blk)
    column_blocks = column_blocks.reshape(n, blk + META, blk)

    w_offs = blocks[:, local_slots * blk + 3 : local_slots * blk + 3 + local_slots, 0]
    c_offs = lax.dynamic_index_in_dim(column_blocks[:, blk + 3 : blk + 3 + local_slots, 0], slot, axis=1)
    offs = jnp.concatenate([w_offs, c_offs], axis=1)
    offs = jnp.clip(offs.astype(jnp.int32), 0, IBS - 1).reshape(-1)
    return gram_call(offs, blocks, column_blocks, local_slots)


def solution(mesh):
    nrow, ncol = mesh.shape["row"], mesh.shape["col"]
    return jax.shard_map(
        functools.partial(local, nrow=nrow, ncol=ncol),
        mesh=mesh,
        in_specs=(P(None, "col", "row", None, None), P(None, "col", None), P(None, "col", "row")),
        out_specs=P("row", "col"),
        check_vma=False,
    )
```

```python
import functools

import jax
import jax.numpy as jnp
from jax import lax
from jax.experimental import pallas as pl
from jax.experimental.pallas import tpu as pltpu
from jax.sharding import PartitionSpec as P

IBS = 8
CHUNK = 8
META = 16


def gram_kernel(offs_ref, bs_ref, bc_ref, o_ref, *, chunk, local_slots, blk):
    step = pl.program_id(0)

    @pl.when(step == 0)
    def _():
        o_ref[...] = jnp.zeros_like(o_ref)

    stride = local_slots + 1
    for k in range(chunk):
        g = step * chunk + k
        meta = bs_ref[k, 0, blk : blk + META].astype(jnp.float32)
        w = meta[0:1] + meta[1:2] + meta[2:3]
        lhs = jnp.concatenate(
            [
                (bs_ref[k, s, :blk].astype(jnp.float32).T * w).astype(jnp.bfloat16)
                for s in range(local_slots)
            ],
            axis=0,
        )
        prod = jnp.dot(lhs, bc_ref[k, :blk], preferred_element_type=jnp.float32)
        col = pl.multiple_of(offs_ref[g * stride + local_slots] * blk, blk)
        for s in range(local_slots):
            row = pl.multiple_of((s * IBS + offs_ref[g * stride + s]) * blk, blk)
            o_ref[pl.ds(row, blk), pl.ds(col, blk)] += prod[s * blk : (s + 1) * blk]


def gram_call(offs, bs, bc):
    n, local_slots, rows, blk = bs.shape
    chunk = CHUNK
    kernel = functools.partial(gram_kernel, chunk=chunk, local_slots=local_slots, blk=blk)
    out_rows, out_cols = local_slots * IBS * blk, IBS * blk
    return pl.pallas_call(
        kernel,
        grid_spec=pltpu.PrefetchScalarGridSpec(
            num_scalar_prefetch=1,
            grid=(n // chunk,),
            in_specs=[
                pl.BlockSpec((chunk, local_slots, rows, blk), lambda i, o: (i, 0, 0, 0)),
                pl.BlockSpec((chunk, rows, blk), lambda i, o: (i, 0, 0)),
            ],
            out_specs=pl.BlockSpec((out_rows, out_cols), lambda i, o: (0, 0)),
        ),
        out_shape=jax.ShapeDtypeStruct((out_rows, out_cols), jnp.float32),
        compiler_params=pltpu.CompilerParams(
            dimension_semantics=("arbitrary",), vmem_limit_bytes=48 * 1024 * 1024
        ),
        cost_estimate=pl.CostEstimate(
            flops=2 * n * local_slots * blk * blk * blk,
            transcendentals=0,
            bytes_accessed=n * (local_slots + 1) * blk * blk * 2 + out_rows * out_cols * 4,
        ),
    )(offs, bs, bc)


def with_meta(panel_blocks, user_weights, slot_offset):
    panels, users, local_slots, blk, _ = panel_blocks.shape
    hi = lax.reduce_precision(user_weights, exponent_bits=8, mantissa_bits=7)
    rest = user_weights - hi
    mid = lax.reduce_precision(rest, exponent_bits=8, mantissa_bits=7)
    low = rest - mid
    weight_rows = jnp.stack([hi, mid, low], axis=2).astype(jnp.bfloat16)[:, :, None]
    weight_rows = jnp.broadcast_to(weight_rows, (panels, users, local_slots, 3, blk))
    offset_rows = jnp.broadcast_to(
        slot_offset.astype(jnp.bfloat16)[..., None, None], (panels, users, local_slots, 1, blk)
    )
    pad = jnp.zeros((panels, users, local_slots, META - 4, blk), jnp.bfloat16)
    return jnp.concatenate([panel_blocks, weight_rows, offset_rows, pad], axis=3)


def local(panel_blocks, user_weights, slot_offset, *, nrow, ncol):
    panels, _, local_slots, blk, _ = panel_blocks.shape
    r = lax.axis_index("row")
    c = lax.axis_index("col")
    x = with_meta(panel_blocks, user_weights, slot_offset)

    outer = ncol // 2
    cycle = [a * 2 for a in range(outer)] + [a * 2 + 1 for a in reversed(range(outer))]
    forward = [(cycle[i], cycle[(i + 1) % ncol]) for i in range(ncol)]
    backward = [(b, a) for a, b in forward]

    src = c // local_slots
    which = (r - src + nrow) % nrow
    slot = c % local_slots
    fans = [
        [
            ((cc // local_slots) * ncol + cc, ((cc // local_slots + j) % nrow) * ncol + cc)
            for cc in range(ncol)
        ]
        for j in range(1, nrow)
    ]

    def pick_slot(piece):
        return lax.dynamic_index_in_dim(piece, slot, axis=2, keepdims=False)

    batches = [[k, k + 1] for k in range(0, ncol - 2, 2)] + [[ncol - 2], [ncol - 1]]
    half = x.shape[1] // 2
    a, b = x[:, :half], x[:, half:]
    pieces, columns, pending = [], [], []
    for step in range(ncol):
        if step:
            a = lax.ppermute(a, "col", forward)
            b = lax.ppermute(b, "col", backward)
        pieces += [a, b]
        pending += [pick_slot(a), pick_slot(b)]
        if any(batch[-1] == step for batch in batches):
            own = jnp.concatenate(pending, axis=1)
            pending = []
            got = own
            for j, fan in enumerate(fans, start=1):
                got = jnp.where(which == j, lax.ppermute(own, ("row", "col"), fan), got)
            columns.append(got)

    blocks = jnp.concatenate(pieces, axis=1)
    column_blocks = jnp.concatenate(columns, axis=1)
    n = panels * blocks.shape[1]
    blocks = blocks.reshape(n, local_slots, blk + META, blk)
    column_blocks = column_blocks.reshape(n, blk + META, blk)

    w_offs = jnp.concatenate([piece[:, :, :, blk + 3, 0] for piece in pieces], axis=1)
    c_offs = jnp.concatenate([got[:, :, blk + 3, 0] for got in columns], axis=1)
    offs = jnp.concatenate([w_offs, c_offs[..., None]], axis=2)
    offs = jnp.clip(offs.astype(jnp.int32), 0, IBS - 1).reshape(-1)
    return gram_call(offs, blocks, column_blocks)


def solution(mesh):
    nrow, ncol = mesh.shape["row"], mesh.shape["col"]
    return jax.shard_map(
        functools.partial(local, nrow=nrow, ncol=ncol),
        mesh=mesh,
        in_specs=(P(None, "col", "row", None, None), P(None, "col", None), P(None, "col", "row")),
        out_specs=P("row", "col"),
        check_vma=False,
    )
```

```python
import functools

import jax
import jax.numpy as jnp
from jax import lax
from jax.experimental import pallas as pl
from jax.experimental.pallas import tpu as pltpu
from jax.sharding import PartitionSpec as P

IBS = 8
CHUNK = 32
META = 16


def gram_kernel(offs_ref, bs_ref, bc_ref, o_ref, *, chunk, local_slots, blk):
    s = pl.program_id(0)
    step = pl.program_id(1)

    @pl.when(step == 0)
    def _():
        o_ref[...] = jnp.zeros_like(o_ref)

    stride = local_slots + 1
    for k in range(chunk):
        g = step * chunk + k
        meta = bs_ref[k, 0, blk : blk + META].astype(jnp.float32)
        w = meta[0:1] + meta[1:2] + meta[2:3]
        lhs = (bs_ref[k, 0, :blk].astype(jnp.float32).T * w).astype(jnp.bfloat16)
        prod = jnp.dot(lhs, bc_ref[k, :blk], preferred_element_type=jnp.float32)
        col = pl.multiple_of(offs_ref[g * stride + local_slots] * blk, blk)
        row = pl.multiple_of(offs_ref[g * stride + s] * blk, blk)
        o_ref[pl.ds(row, blk), pl.ds(col, blk)] += prod


def gram_call(offs, bs, bc):
    n, local_slots, rows, blk = bs.shape
    chunk = CHUNK
    kernel = functools.partial(gram_kernel, chunk=chunk, local_slots=local_slots, blk=blk)
    out_rows, out_cols = local_slots * IBS * blk, IBS * blk
    return pl.pallas_call(
        kernel,
        grid_spec=pltpu.PrefetchScalarGridSpec(
            num_scalar_prefetch=1,
            grid=(local_slots, n // chunk),
            in_specs=[
                pl.BlockSpec((chunk, 1, rows, blk), lambda s, i, o: (i, s, 0, 0)),
                pl.BlockSpec((chunk, rows, blk), lambda s, i, o: (i, 0, 0)),
            ],
            out_specs=pl.BlockSpec((IBS * blk, out_cols), lambda s, i, o: (s, 0)),
        ),
        out_shape=jax.ShapeDtypeStruct((out_rows, out_cols), jnp.float32),
        compiler_params=pltpu.CompilerParams(
            dimension_semantics=("arbitrary", "arbitrary"), vmem_limit_bytes=48 * 1024 * 1024
        ),
        cost_estimate=pl.CostEstimate(
            flops=2 * n * local_slots * blk * blk * blk,
            transcendentals=0,
            bytes_accessed=n * (local_slots + 1) * blk * blk * 2 + out_rows * out_cols * 4,
        ),
    )(offs, bs, bc)


def with_meta(panel_blocks, user_weights, slot_offset):
    panels, users, local_slots, blk, _ = panel_blocks.shape
    hi = lax.reduce_precision(user_weights, exponent_bits=8, mantissa_bits=7)
    rest = user_weights - hi
    mid = lax.reduce_precision(rest, exponent_bits=8, mantissa_bits=7)
    low = rest - mid
    weight_rows = jnp.stack([hi, mid, low], axis=2).astype(jnp.bfloat16)[:, :, None]
    weight_rows = jnp.broadcast_to(weight_rows, (panels, users, local_slots, 3, blk))
    offset_rows = jnp.broadcast_to(
        slot_offset.astype(jnp.bfloat16)[..., None, None], (panels, users, local_slots, 1, blk)
    )
    pad = jnp.zeros((panels, users, local_slots, META - 4, blk), jnp.bfloat16)
    return jnp.concatenate([panel_blocks, weight_rows, offset_rows, pad], axis=3)


def local(panel_blocks, user_weights, slot_offset, *, nrow, ncol):
    panels, _, local_slots, blk, _ = panel_blocks.shape
    r = lax.axis_index("row")
    c = lax.axis_index("col")
    x = with_meta(panel_blocks, user_weights, slot_offset)

    outer = ncol // 2
    cycle = [a * 2 for a in range(outer)] + [a * 2 + 1 for a in reversed(range(outer))]
    forward = [(cycle[i], cycle[(i + 1) % ncol]) for i in range(ncol)]
    backward = [(b, a) for a, b in forward]

    src = c // local_slots
    which = (r - src + nrow) % nrow
    slot = c % local_slots
    fans = [
        [
            ((cc // local_slots) * ncol + cc, ((cc // local_slots + j) % nrow) * ncol + cc)
            for cc in range(ncol)
        ]
        for j in range(1, nrow)
    ]

    def pick_slot(piece):
        return lax.dynamic_index_in_dim(piece, slot, axis=2, keepdims=False)

    batches = [[k, k + 1] for k in range(0, ncol - 2, 2)] + [[ncol - 2], [ncol - 1]]
    half = x.shape[1] // 2
    a, b = x[:, :half], x[:, half:]
    pieces, columns, pending = [], [], []
    for step in range(ncol):
        if step:
            a = lax.ppermute(a, "col", forward)
            b = lax.ppermute(b, "col", backward)
        pieces += [a, b]
        pending += [pick_slot(a), pick_slot(b)]
        if any(batch[-1] == step for batch in batches):
            own = jnp.concatenate(pending, axis=1)
            pending = []
            got = own
            for j, fan in enumerate(fans, start=1):
                got = jnp.where(which == j, lax.ppermute(own, ("row", "col"), fan), got)
            columns.append(got)

    blocks = jnp.concatenate(pieces, axis=1)
    column_blocks = jnp.concatenate(columns, axis=1)
    n = panels * blocks.shape[1]
    blocks = blocks.reshape(n, local_slots, blk + META, blk)
    column_blocks = column_blocks.reshape(n, blk + META, blk)

    offs = jnp.concatenate([blocks[:, :, blk + 3, 0], column_blocks[:, blk + 3, 0][:, None]], axis=1)
    offs = jnp.clip(offs.astype(jnp.int32), 0, IBS - 1).reshape(-1)
    return gram_call(offs, blocks, column_blocks)


def solution(mesh):
    nrow, ncol = mesh.shape["row"], mesh.shape["col"]
    return jax.shard_map(
        functools.partial(local, nrow=nrow, ncol=ncol),
        mesh=mesh,
        in_specs=(P(None, "col", "row", None, None), P(None, "col", None), P(None, "col", "row")),
        out_specs=P("row", "col"),
        check_vma=False,
    )
```

```python
import functools

import jax
import jax.numpy as jnp
from jax import lax
from jax.experimental import pallas as pl
from jax.experimental.pallas import tpu as pltpu
from jax.sharding import PartitionSpec as P

IBS = 8
CHUNK = 32
META = 16


def gram_kernel(offs_ref, bs_ref, bc_ref, o_ref, seen_ref, *, chunk, local_slots, blk):
    s = pl.program_id(0)
    step = pl.program_id(1)

    @pl.when(step == 0)
    def _():
        for q in range(IBS * IBS):
            seen_ref[q] = 0

    stride = local_slots + 1
    for k in range(chunk):
        g = step * chunk + k
        meta = bs_ref[k, 0, blk : blk + META].astype(jnp.float32)
        w = meta[0:1] + meta[1:2] + meta[2:3]
        lhs = (bs_ref[k, 0, :blk].astype(jnp.float32).T * w).astype(jnp.bfloat16)
        prod = jnp.dot(lhs, bc_ref[k, :blk], preferred_element_type=jnp.float32)
        ci = offs_ref[g * stride + local_slots]
        ri = offs_ref[g * stride + s]
        q = ri * IBS + ci
        col = pl.multiple_of(ci * blk, blk)
        row = pl.multiple_of(ri * blk, blk)
        first = seen_ref[q] == 0

        @pl.when(first)
        def _():
            o_ref[pl.ds(row, blk), pl.ds(col, blk)] = prod

        @pl.when(jnp.logical_not(first))
        def _():
            o_ref[pl.ds(row, blk), pl.ds(col, blk)] += prod

        seen_ref[q] = 1

    @pl.when(step == pl.num_programs(1) - 1)
    def _():
        for q in range(IBS * IBS):
            i, j = divmod(q, IBS)

            @pl.when(seen_ref[q] == 0)
            def _():
                o_ref[i * blk : (i + 1) * blk, j * blk : (j + 1) * blk] = jnp.zeros(
                    (blk, blk), jnp.float32
                )


def gram_call(offs, bs, bc):
    n, local_slots, rows, blk = bs.shape
    chunk = CHUNK
    kernel = functools.partial(gram_kernel, chunk=chunk, local_slots=local_slots, blk=blk)
    out_rows, out_cols = local_slots * IBS * blk, IBS * blk
    return pl.pallas_call(
        kernel,
        grid_spec=pltpu.PrefetchScalarGridSpec(
            num_scalar_prefetch=1,
            grid=(local_slots, n // chunk),
            in_specs=[
                pl.BlockSpec((chunk, 1, rows, blk), lambda s, i, o: (i, s, 0, 0)),
                pl.BlockSpec((chunk, rows, blk), lambda s, i, o: (i, 0, 0)),
            ],
            out_specs=pl.BlockSpec((IBS * blk, out_cols), lambda s, i, o: (s, 0)),
            scratch_shapes=[pltpu.SMEM((IBS * IBS,), jnp.int32)],
        ),
        out_shape=jax.ShapeDtypeStruct((out_rows, out_cols), jnp.float32),
        compiler_params=pltpu.CompilerParams(
            dimension_semantics=("arbitrary", "arbitrary"), vmem_limit_bytes=48 * 1024 * 1024
        ),
        cost_estimate=pl.CostEstimate(
            flops=2 * n * local_slots * blk * blk * blk,
            transcendentals=0,
            bytes_accessed=n * (local_slots + 1) * blk * blk * 2 + out_rows * out_cols * 4,
        ),
    )(offs, bs, bc)


def with_meta(panel_blocks, user_weights, slot_offset):
    panels, users, local_slots, blk, _ = panel_blocks.shape
    hi = lax.reduce_precision(user_weights, exponent_bits=8, mantissa_bits=7)
    rest = user_weights - hi
    mid = lax.reduce_precision(rest, exponent_bits=8, mantissa_bits=7)
    low = rest - mid
    weight_rows = jnp.stack([hi, mid, low], axis=2).astype(jnp.bfloat16)[:, :, None]
    weight_rows = jnp.broadcast_to(weight_rows, (panels, users, local_slots, 3, blk))
    offset_rows = jnp.broadcast_to(
        slot_offset.astype(jnp.bfloat16)[..., None, None], (panels, users, local_slots, 1, blk)
    )
    pad = jnp.zeros((panels, users, local_slots, META - 4, blk), jnp.bfloat16)
    return jnp.concatenate([panel_blocks, weight_rows, offset_rows, pad], axis=3)


def local(panel_blocks, user_weights, slot_offset, *, nrow, ncol):
    panels, _, local_slots, blk, _ = panel_blocks.shape
    r = lax.axis_index("row")
    c = lax.axis_index("col")
    x = with_meta(panel_blocks, user_weights, slot_offset)

    outer = ncol // 2
    cycle = [a * 2 for a in range(outer)] + [a * 2 + 1 for a in reversed(range(outer))]
    forward = [(cycle[i], cycle[(i + 1) % ncol]) for i in range(ncol)]
    backward = [(b, a) for a, b in forward]

    src = c // local_slots
    which = (r - src + nrow) % nrow
    slot = c % local_slots
    fans = [
        [
            ((cc // local_slots) * ncol + cc, ((cc // local_slots + j) % nrow) * ncol + cc)
            for cc in range(ncol)
        ]
        for j in range(1, nrow)
    ]

    def pick_slot(piece):
        return lax.dynamic_index_in_dim(piece, slot, axis=2, keepdims=False)

    batches = [[k, k + 1] for k in range(0, ncol - 2, 2)] + [[ncol - 2], [ncol - 1]]
    half = x.shape[1] // 2
    a, b = x[:, :half], x[:, half:]
    pieces, columns, pending = [], [], []
    for step in range(ncol):
        if step:
            a = lax.ppermute(a, "col", forward)
            b = lax.ppermute(b, "col", backward)
        pieces += [a, b]
        pending += [pick_slot(a), pick_slot(b)]
        if any(batch[-1] == step for batch in batches):
            own = jnp.concatenate(pending, axis=1)
            pending = []
            got = own
            for j, fan in enumerate(fans, start=1):
                got = jnp.where(which == j, lax.ppermute(own, ("row", "col"), fan), got)
            columns.append(got)

    blocks = jnp.concatenate(pieces, axis=1)
    column_blocks = jnp.concatenate(columns, axis=1)
    n = panels * blocks.shape[1]
    blocks = blocks.reshape(n, local_slots, blk + META, blk)
    column_blocks = column_blocks.reshape(n, blk + META, blk)

    offs = jnp.concatenate([blocks[:, :, blk + 3, 0], column_blocks[:, blk + 3, 0][:, None]], axis=1)
    offs = jnp.clip(offs.astype(jnp.int32), 0, IBS - 1).reshape(-1)
    return gram_call(offs, blocks, column_blocks)


def solution(mesh):
    nrow, ncol = mesh.shape["row"], mesh.shape["col"]
    return jax.shard_map(
        functools.partial(local, nrow=nrow, ncol=ncol),
        mesh=mesh,
        in_specs=(P(None, "col", "row", None, None), P(None, "col", None), P(None, "col", "row")),
        out_specs=P("row", "col"),
        check_vma=False,
    )
```

```python
import functools

import jax
import jax.numpy as jnp
from jax import lax
from jax.experimental import pallas as pl
from jax.experimental.pallas import tpu as pltpu
from jax.sharding import PartitionSpec as P

IBS = 8
CHUNK = 32
META = 16


def gram_kernel(offs_ref, bs_ref, bc_ref, o_ref, *, chunk, local_slots, blk):
    s = pl.program_id(0)
    step = pl.program_id(1)

    @pl.when(step == 0)
    def _():
        o_ref[...] = jnp.zeros_like(o_ref)

    stride = local_slots + 1
    for k in range(chunk):
        g = step * chunk + k
        meta = bs_ref[k, 0, blk : blk + META].astype(jnp.float32)
        w = meta[0:1] + meta[1:2] + meta[2:3]
        lhs = (bs_ref[k, 0, :blk].T.astype(jnp.float32) * w).astype(jnp.bfloat16)
        prod = jnp.dot(lhs, bc_ref[k, :blk], preferred_element_type=jnp.float32)
        col = pl.multiple_of(offs_ref[g * stride + local_slots] * blk, blk)
        row = pl.multiple_of(offs_ref[g * stride + s] * blk, blk)
        o_ref[pl.ds(row, blk), pl.ds(col, blk)] += prod


def gram_call(offs, bs, bc):
    n, local_slots, rows, blk = bs.shape
    chunk = CHUNK
    kernel = functools.partial(gram_kernel, chunk=chunk, local_slots=local_slots, blk=blk)
    out_rows, out_cols = local_slots * IBS * blk, IBS * blk
    return pl.pallas_call(
        kernel,
        grid_spec=pltpu.PrefetchScalarGridSpec(
            num_scalar_prefetch=1,
            grid=(local_slots, n // chunk),
            in_specs=[
                pl.BlockSpec((chunk, 1, rows, blk), lambda s, i, o: (i, s, 0, 0)),
                pl.BlockSpec((chunk, rows, blk), lambda s, i, o: (i, 0, 0)),
            ],
            out_specs=pl.BlockSpec((IBS * blk, out_cols), lambda s, i, o: (s, 0)),
        ),
        out_shape=jax.ShapeDtypeStruct((out_rows, out_cols), jnp.float32),
        compiler_params=pltpu.CompilerParams(
            dimension_semantics=("arbitrary", "arbitrary"), vmem_limit_bytes=48 * 1024 * 1024
        ),
        cost_estimate=pl.CostEstimate(
            flops=2 * n * local_slots * blk * blk * blk,
            transcendentals=0,
            bytes_accessed=n * (local_slots + 1) * blk * blk * 2 + out_rows * out_cols * 4,
        ),
    )(offs, bs, bc)


def with_meta(panel_blocks, user_weights, slot_offset):
    panels, users, local_slots, blk, _ = panel_blocks.shape
    hi = lax.reduce_precision(user_weights, exponent_bits=8, mantissa_bits=7)
    rest = user_weights - hi
    mid = lax.reduce_precision(rest, exponent_bits=8, mantissa_bits=7)
    low = rest - mid
    weight_rows = jnp.stack([hi, mid, low], axis=2).astype(jnp.bfloat16)[:, :, None]
    weight_rows = jnp.broadcast_to(weight_rows, (panels, users, local_slots, 3, blk))
    offset_rows = jnp.broadcast_to(
        slot_offset.astype(jnp.bfloat16)[..., None, None], (panels, users, local_slots, 1, blk)
    )
    pad = jnp.zeros((panels, users, local_slots, META - 4, blk), jnp.bfloat16)
    return jnp.concatenate([panel_blocks, weight_rows, offset_rows, pad], axis=3)


def local(panel_blocks, user_weights, slot_offset, *, nrow, ncol):
    panels, _, local_slots, blk, _ = panel_blocks.shape
    r = lax.axis_index("row")
    c = lax.axis_index("col")
    x = with_meta(panel_blocks, user_weights, slot_offset)

    outer = ncol // 2
    cycle = [a * 2 for a in range(outer)] + [a * 2 + 1 for a in reversed(range(outer))]
    forward = [(cycle[i], cycle[(i + 1) % ncol]) for i in range(ncol)]
    backward = [(b, a) for a, b in forward]

    src = c // local_slots
    which = (r - src + nrow) % nrow
    slot = c % local_slots
    fans = [
        [
            ((cc // local_slots) * ncol + cc, ((cc // local_slots + j) % nrow) * ncol + cc)
            for cc in range(ncol)
        ]
        for j in range(1, nrow)
    ]

    def pick_slot(piece):
        return lax.dynamic_index_in_dim(piece, slot, axis=2, keepdims=False)

    batches = [[k, k + 1] for k in range(0, ncol - 2, 2)] + [[ncol - 2], [ncol - 1]]
    half = x.shape[1] // 2
    a, b = x[:, :half], x[:, half:]
    pieces, columns, pending = [], [], []
    for step in range(ncol):
        if step:
            a = lax.ppermute(a, "col", forward)
            b = lax.ppermute(b, "col", backward)
        pieces += [a, b]
        pending += [pick_slot(a), pick_slot(b)]
        if any(batch[-1] == step for batch in batches):
            own = jnp.concatenate(pending, axis=1)
            pending = []
            got = own
            for j, fan in enumerate(fans, start=1):
                got = jnp.where(which == j, lax.ppermute(own, ("row", "col"), fan), got)
            columns.append(got)

    blocks = jnp.concatenate(pieces, axis=1)
    column_blocks = jnp.concatenate(columns, axis=1)
    n = panels * blocks.shape[1]
    blocks = blocks.reshape(n, local_slots, blk + META, blk)
    column_blocks = column_blocks.reshape(n, blk + META, blk)

    offs = jnp.concatenate([blocks[:, :, blk + 3, 0], column_blocks[:, blk + 3, 0][:, None]], axis=1)
    offs = jnp.clip(offs.astype(jnp.int32), 0, IBS - 1).reshape(-1)
    return gram_call(offs, blocks, column_blocks)


def solution(mesh):
    nrow, ncol = mesh.shape["row"], mesh.shape["col"]
    return jax.shard_map(
        functools.partial(local, nrow=nrow, ncol=ncol),
        mesh=mesh,
        in_specs=(P(None, "col", "row", None, None), P(None, "col", None), P(None, "col", "row")),
        out_specs=P("row", "col"),
        check_vma=False,
    )
```

```python
import functools

import jax
import jax.numpy as jnp
from jax import lax
from jax.experimental import pallas as pl
from jax.experimental.pallas import tpu as pltpu
from jax.sharding import PartitionSpec as P

IBS = 8
CHUNK = 32
META = 16


def gram_kernel(offs_ref, bs_ref, bc_ref, o_ref, *, chunk, local_slots, blk):
    s = pl.program_id(0)
    step = pl.program_id(1)

    @pl.when(step == 0)
    def _():
        o_ref[...] = jnp.zeros_like(o_ref)

    stride = local_slots + 1
    for k in range(chunk):
        g = step * chunk + k
        meta = bs_ref[k, 0, blk : blk + META].astype(jnp.float32)
        w = meta[0:1] + meta[1:2] + meta[2:3]
        lhs = (bs_ref[k, 0, :blk].T.astype(jnp.float32) * w).astype(jnp.bfloat16)
        prod = jnp.dot(lhs, bc_ref[k, :blk], preferred_element_type=jnp.float32)
        col = pl.multiple_of(offs_ref[g * stride + local_slots] * blk, blk)
        row = pl.multiple_of(offs_ref[g * stride + s] * blk, blk)
        o_ref[pl.ds(row, blk), pl.ds(col, blk)] += prod


def gram_call(offs, bs, bc):
    n, local_slots, rows, blk = bs.shape
    chunk = CHUNK
    kernel = functools.partial(gram_kernel, chunk=chunk, local_slots=local_slots, blk=blk)
    out_rows, out_cols = local_slots * IBS * blk, IBS * blk
    return pl.pallas_call(
        kernel,
        grid_spec=pltpu.PrefetchScalarGridSpec(
            num_scalar_prefetch=1,
            grid=(local_slots, n // chunk),
            in_specs=[
                pl.BlockSpec((chunk, 1, rows, blk), lambda s, i, o: (i, s, 0, 0)),
                pl.BlockSpec((chunk, rows, blk), lambda s, i, o: (i, 0, 0)),
            ],
            out_specs=pl.BlockSpec((IBS * blk, out_cols), lambda s, i, o: (s, 0)),
        ),
        out_shape=jax.ShapeDtypeStruct((out_rows, out_cols), jnp.float32),
        compiler_params=pltpu.CompilerParams(
            dimension_semantics=("arbitrary", "arbitrary"), vmem_limit_bytes=48 * 1024 * 1024
        ),
        cost_estimate=pl.CostEstimate(
            flops=2 * n * local_slots * blk * blk * blk,
            transcendentals=0,
            bytes_accessed=n * (local_slots + 1) * blk * blk * 2 + out_rows * out_cols * 4,
        ),
    )(offs, bs, bc)


def with_meta(panel_blocks, user_weights, slot_offset):
    panels, users, local_slots, blk, _ = panel_blocks.shape
    hi = lax.reduce_precision(user_weights, exponent_bits=8, mantissa_bits=7)
    rest = user_weights - hi
    mid = lax.reduce_precision(rest, exponent_bits=8, mantissa_bits=7)
    low = rest - mid
    weight_rows = jnp.stack([hi, mid, low], axis=2).astype(jnp.bfloat16)[:, :, None]
    weight_rows = jnp.broadcast_to(weight_rows, (panels, users, local_slots, 3, blk))
    offset_rows = jnp.broadcast_to(
        slot_offset.astype(jnp.bfloat16)[..., None, None], (panels, users, local_slots, 1, blk)
    )
    pad = jnp.zeros((panels, users, local_slots, META - 4, blk), jnp.bfloat16)
    return jnp.concatenate([panel_blocks, weight_rows, offset_rows, pad], axis=3)


def local(panel_blocks, user_weights, slot_offset, *, nrow, ncol):
    panels, _, local_slots, blk, _ = panel_blocks.shape
    r = lax.axis_index("row")
    c = lax.axis_index("col")
    x = with_meta(panel_blocks, user_weights, slot_offset)

    outer = ncol // 2
    cycle = [a * 2 for a in range(outer)] + [a * 2 + 1 for a in reversed(range(outer))]
    forward = [(cycle[i], cycle[(i + 1) % ncol]) for i in range(ncol)]
    backward = [(b, a) for a, b in forward]

    src = c // local_slots
    which = (r - src + nrow) % nrow
    slot = c % local_slots
    fans = [
        [
            ((cc // local_slots) * ncol + cc, ((cc // local_slots + j) % nrow) * ncol + cc)
            for cc in range(ncol)
        ]
        for j in range(1, nrow)
    ]

    def pick_slot(piece):
        return lax.dynamic_index_in_dim(piece, slot, axis=2, keepdims=False)

    batches = [[k, k + 1] for k in range(0, ncol - 2, 2)] + [[ncol - 2], [ncol - 1]]
    half = x.shape[1] // 2
    a, b = x[:, :half], x[:, half:]
    oa, ob = slot_offset[:, :half], slot_offset[:, half:]
    pieces, columns, pending, w_offs = [], [], [], []
    for step in range(ncol):
        if step:
            a = lax.ppermute(a, "col", forward)
            b = lax.ppermute(b, "col", backward)
            oa = lax.ppermute(oa, "col", forward)
            ob = lax.ppermute(ob, "col", backward)
        pieces += [a, b]
        w_offs += [oa, ob]
        pending += [pick_slot(a), pick_slot(b)]
        if any(batch[-1] == step for batch in batches):
            own = jnp.concatenate(pending, axis=1)
            pending = []
            got = own
            for j, fan in enumerate(fans, start=1):
                got = jnp.where(which == j, lax.ppermute(own, ("row", "col"), fan), got)
            columns.append(got)

    blocks = jnp.concatenate(pieces, axis=1)
    column_blocks = jnp.concatenate(columns, axis=1)
    n = panels * blocks.shape[1]
    blocks = blocks.reshape(n, local_slots, blk + META, blk)
    column_blocks = column_blocks.reshape(n, blk + META, blk)

    w_offs = jnp.concatenate(w_offs, axis=1).reshape(n, local_slots).astype(jnp.bfloat16)
    offs = jnp.concatenate([w_offs, column_blocks[:, blk + 3, 0][:, None]], axis=1)
    offs = jnp.clip(offs.astype(jnp.int32), 0, IBS - 1).reshape(-1)
    return gram_call(offs, blocks, column_blocks)


def solution(mesh):
    nrow, ncol = mesh.shape["row"], mesh.shape["col"]
    return jax.shard_map(
        functools.partial(local, nrow=nrow, ncol=ncol),
        mesh=mesh,
        in_specs=(P(None, "col", "row", None, None), P(None, "col", None), P(None, "col", "row")),
        out_specs=P("row", "col"),
        check_vma=False,
    )
```

```python
import functools

import jax
import jax.numpy as jnp
from jax import lax
from jax.experimental import pallas as pl
from jax.experimental.pallas import tpu as pltpu
from jax.sharding import PartitionSpec as P

IBS = 8
CHUNK = 32
META = 16


def gram_kernel(offs_ref, bs_ref, bc_ref, o_ref, *, chunk, local_slots, blk):
    s = pl.program_id(0)
    step = pl.program_id(1)

    @pl.when(step == 0)
    def _():
        o_ref[...] = jnp.zeros_like(o_ref)

    stride = local_slots + 1
    for k in range(chunk):
        g = step * chunk + k
        meta = bs_ref[k, 0, blk : blk + META].astype(jnp.float32)
        w = meta[0:1] + meta[1:2] + meta[2:3]
        lhs = (bs_ref[k, 0, :blk].T.astype(jnp.float32) * w).astype(jnp.bfloat16)
        prod = jnp.dot(lhs, bc_ref[k, :blk], preferred_element_type=jnp.float32)
        col = pl.multiple_of(offs_ref[g * stride + local_slots] * blk, blk)
        row = pl.multiple_of(offs_ref[g * stride + s] * blk, blk)
        o_ref[pl.ds(row, blk), pl.ds(col, blk)] += prod


def gram_call(offs, bs, bc):
    n, local_slots, rows, blk = bs.shape
    chunk = CHUNK
    kernel = functools.partial(gram_kernel, chunk=chunk, local_slots=local_slots, blk=blk)
    out_rows, out_cols = local_slots * IBS * blk, IBS * blk
    return pl.pallas_call(
        kernel,
        grid_spec=pltpu.PrefetchScalarGridSpec(
            num_scalar_prefetch=1,
            grid=(local_slots, n // chunk),
            in_specs=[
                pl.BlockSpec((chunk, 1, rows, blk), lambda s, i, o: (i, s, 0, 0)),
                pl.BlockSpec((chunk, rows, blk), lambda s, i, o: (i, 0, 0)),
            ],
            out_specs=pl.BlockSpec((IBS * blk, out_cols), lambda s, i, o: (s, 0)),
        ),
        out_shape=jax.ShapeDtypeStruct((out_rows, out_cols), jnp.float32),
        compiler_params=pltpu.CompilerParams(
            dimension_semantics=("arbitrary", "arbitrary"), vmem_limit_bytes=48 * 1024 * 1024
        ),
        cost_estimate=pl.CostEstimate(
            flops=2 * n * local_slots * blk * blk * blk,
            transcendentals=0,
            bytes_accessed=n * (local_slots + 1) * blk * blk * 2 + out_rows * out_cols * 4,
        ),
    )(offs, bs, bc)


def with_meta(panel_blocks, user_weights, slot_offset):
    panels, users, local_slots, blk, _ = panel_blocks.shape
    hi = lax.reduce_precision(user_weights, exponent_bits=8, mantissa_bits=7)
    rest = user_weights - hi
    mid = lax.reduce_precision(rest, exponent_bits=8, mantissa_bits=7)
    low = rest - mid
    weight_rows = jnp.stack([hi, mid, low], axis=2).astype(jnp.bfloat16)[:, :, None]
    weight_rows = jnp.broadcast_to(weight_rows, (panels, users, local_slots, 3, blk))
    offset_rows = jnp.broadcast_to(
        slot_offset.astype(jnp.bfloat16)[..., None, None], (panels, users, local_slots, 1, blk)
    )
    pad = jnp.zeros((panels, users, local_slots, META - 4, blk), jnp.bfloat16)
    return jnp.concatenate([panel_blocks, weight_rows, offset_rows, pad], axis=3)


def local(panel_blocks, user_weights, slot_offset, *, nrow, ncol):
    panels, _, local_slots, blk, _ = panel_blocks.shape
    r = lax.axis_index("row")
    c = lax.axis_index("col")
    x = with_meta(panel_blocks, user_weights, slot_offset)

    outer = ncol // 2
    cycle = [a * 2 for a in range(outer)] + [a * 2 + 1 for a in reversed(range(outer))]
    forward = [(cycle[i], cycle[(i + 1) % ncol]) for i in range(ncol)]
    backward = [(b, a) for a, b in forward]

    src = c // local_slots
    which = (r - src + nrow) % nrow
    slot = c % local_slots
    fans = [
        [
            ((cc // local_slots) * ncol + cc, ((cc // local_slots + j) % nrow) * ncol + cc)
            for cc in range(ncol)
        ]
        for j in range(1, nrow)
    ]

    nx = nrow // 2
    is_s, is_p = which == 0, r == src + 1 - 2 * (src % 2)
    is_d1 = (which % 2 == 0) & (which != 0)

    def send(v, pairs):
        return lax.ppermute(v, ("row", "col"), [(a * ncol + cc, b * ncol + cc) for a, b, cc in pairs])

    def last_fan(own):
        heads = [cc // local_slots for cc in range(ncol)]
        to_partner = send(own, [(h, h ^ 1, cc) for cc, h in enumerate(heads)])
        to_d1 = None
        for j in range(1, nx):
            v = send(own, [(h, (h + 2 * j) % nrow, cc) for cc, h in enumerate(heads)])
            to_d1 = v if to_d1 is None else jnp.where(which // 2 == j, v, to_d1)
        to_d2 = send(
            to_d1,
            [((h + 2 * j) % nrow, ((h + 2 * j) % nrow) ^ 1, cc) for cc, h in enumerate(heads) for j in range(1, nx)],
        )
        return jnp.where(is_s, own, jnp.where(is_p, to_partner, jnp.where(is_d1, to_d1, to_d2)))

    def pick_slot(piece):
        return lax.dynamic_index_in_dim(piece, slot, axis=2, keepdims=False)

    batches = [[k, k + 1] for k in range(0, ncol - 2, 2)] + [[ncol - 2], [ncol - 1]]
    half = x.shape[1] // 2
    a, b = x[:, :half], x[:, half:]
    pieces, columns, pending = [], [], []
    for step in range(ncol):
        if step:
            a = lax.ppermute(a, "col", forward)
            b = lax.ppermute(b, "col", backward)
        pieces += [a, b]
        pending += [pick_slot(a), pick_slot(b)]
        if any(batch[-1] == step for batch in batches):
            own = jnp.concatenate(pending, axis=1)
            pending = []
            if step < ncol - 1:
                got = own
                for j, fan in enumerate(fans, start=1):
                    got = jnp.where(which == j, lax.ppermute(own, ("row", "col"), fan), got)
            else:
                got = last_fan(own)
            columns.append(got)

    blocks = jnp.concatenate(pieces, axis=1)
    column_blocks = jnp.concatenate(columns, axis=1)
    n = panels * blocks.shape[1]
    blocks = blocks.reshape(n, local_slots, blk + META, blk)
    column_blocks = column_blocks.reshape(n, blk + META, blk)

    offs = jnp.concatenate([blocks[:, :, blk + 3, 0], column_blocks[:, blk + 3, 0][:, None]], axis=1)
    offs = jnp.clip(offs.astype(jnp.int32), 0, IBS - 1).reshape(-1)
    return gram_call(offs, blocks, column_blocks)


def solution(mesh):
    nrow, ncol = mesh.shape["row"], mesh.shape["col"]
    return jax.shard_map(
        functools.partial(local, nrow=nrow, ncol=ncol),
        mesh=mesh,
        in_specs=(P(None, "col", "row", None, None), P(None, "col", None), P(None, "col", "row")),
        out_specs=P("row", "col"),
        check_vma=False,
    )
```

```python
import functools

import jax
import jax.numpy as jnp
from jax import lax
from jax.experimental import pallas as pl
from jax.experimental.pallas import tpu as pltpu
from jax.sharding import PartitionSpec as P

IBS = 8
CHUNK = 32
META = 16


def gram_kernel(offs_ref, bs_ref, bc_ref, o_ref, *, chunk, local_slots, blk):
    s = pl.program_id(0)
    step = pl.program_id(1)

    @pl.when(step == 0)
    def _():
        o_ref[...] = jnp.zeros_like(o_ref)

    stride = local_slots + 1
    for k in range(chunk):
        g = step * chunk + k
        meta = bs_ref[k, 0, blk : blk + META].astype(jnp.float32)
        w = meta[0:1] + meta[1:2] + meta[2:3]
        lhs = (bs_ref[k, 0, :blk].T.astype(jnp.float32) * w).astype(jnp.bfloat16)
        prod = jnp.dot(lhs, bc_ref[k, :blk], preferred_element_type=jnp.float32)
        col = pl.multiple_of(offs_ref[g * stride + local_slots] * blk, blk)
        row = pl.multiple_of(offs_ref[g * stride + s] * blk, blk)
        o_ref[pl.ds(row, blk), pl.ds(col, blk)] += prod


def gram_call(offs, bs, bc):
    n, local_slots, rows, blk = bs.shape
    chunk = CHUNK
    kernel = functools.partial(gram_kernel, chunk=chunk, local_slots=local_slots, blk=blk)
    out_rows, out_cols = local_slots * IBS * blk, IBS * blk
    return pl.pallas_call(
        kernel,
        grid_spec=pltpu.PrefetchScalarGridSpec(
            num_scalar_prefetch=1,
            grid=(local_slots, n // chunk),
            in_specs=[
                pl.BlockSpec((chunk, 1, rows, blk), lambda s, i, o: (i, s, 0, 0)),
                pl.BlockSpec((chunk, rows, blk), lambda s, i, o: (i, 0, 0)),
            ],
            out_specs=pl.BlockSpec((IBS * blk, out_cols), lambda s, i, o: (s, 0)),
        ),
        out_shape=jax.ShapeDtypeStruct((out_rows, out_cols), jnp.float32),
        compiler_params=pltpu.CompilerParams(
            dimension_semantics=("arbitrary", "arbitrary"), vmem_limit_bytes=48 * 1024 * 1024
        ),
        cost_estimate=pl.CostEstimate(
            flops=2 * n * local_slots * blk * blk * blk,
            transcendentals=0,
            bytes_accessed=n * (local_slots + 1) * blk * blk * 2 + out_rows * out_cols * 4,
        ),
    )(offs, bs, bc)


def with_meta(panel_blocks, user_weights, slot_offset):
    panels, users, local_slots, blk, _ = panel_blocks.shape
    hi = lax.reduce_precision(user_weights, exponent_bits=8, mantissa_bits=7)
    rest = user_weights - hi
    mid = lax.reduce_precision(rest, exponent_bits=8, mantissa_bits=7)
    low = rest - mid
    weight_rows = jnp.stack([hi, mid, low], axis=2).astype(jnp.bfloat16)[:, :, None]
    weight_rows = jnp.broadcast_to(weight_rows, (panels, users, local_slots, 3, blk))
    offset_rows = jnp.broadcast_to(
        slot_offset.astype(jnp.bfloat16)[..., None, None], (panels, users, local_slots, 1, blk)
    )
    pad = jnp.zeros((panels, users, local_slots, META - 4, blk), jnp.bfloat16)
    return jnp.concatenate([panel_blocks, weight_rows, offset_rows, pad], axis=3)


def local(panel_blocks, user_weights, slot_offset, *, nrow, ncol):
    panels, _, local_slots, blk, _ = panel_blocks.shape
    r = lax.axis_index("row")
    c = lax.axis_index("col")
    x = with_meta(panel_blocks, user_weights, slot_offset)

    outer = ncol // 2
    cycle = [a * 2 for a in range(outer)] + [a * 2 + 1 for a in reversed(range(outer))]
    forward = [(cycle[i], cycle[(i + 1) % ncol]) for i in range(ncol)]
    backward = [(b, a) for a, b in forward]

    src = c // local_slots
    which = (r - src + nrow) % nrow
    slot = c % local_slots
    fans = [
        [
            ((cc // local_slots) * ncol + cc, ((cc // local_slots + j) % nrow) * ncol + cc)
            for cc in range(ncol)
        ]
        for j in range(1, nrow)
    ]

    nx = nrow // 2
    is_s, is_p = which == 0, r == src + 1 - 2 * (src % 2)
    is_d1 = (which % 2 == 0) & (which != 0)

    def send(v, pairs):
        return lax.ppermute(v, ("row", "col"), [(a * ncol + cc, b * ncol + cc) for a, b, cc in pairs])

    def last_fan(own):
        heads = [cc // local_slots for cc in range(ncol)]
        to_partner = send(own, [(h, h ^ 1, cc) for cc, h in enumerate(heads)])
        to_d1 = None
        for j in range(1, nx):
            v = send(own, [(h, (h + 2 * j) % nrow, cc) for cc, h in enumerate(heads)])
            to_d1 = v if to_d1 is None else jnp.where(which // 2 == j, v, to_d1)
        to_d2 = send(
            to_d1,
            [((h + 2 * j) % nrow, ((h + 2 * j) % nrow) ^ 1, cc) for cc, h in enumerate(heads) for j in range(1, nx)],
        )
        return jnp.where(is_s, own, jnp.where(is_p, to_partner, jnp.where(is_d1, to_d1, to_d2)))

    def pick_slot(piece):
        return lax.dynamic_index_in_dim(piece, slot, axis=2, keepdims=False)

    batches = [[k, k + 1] for k in range(0, ncol - 2, 2)] + [[ncol - 2], [ncol - 1]]
    half = x.shape[1] // 2
    a, b = x[:, :half], x[:, half:]
    pieces, columns, pending = [], [], []
    for step in range(ncol):
        if step:
            a = lax.ppermute(a, "col", forward)
            b = lax.ppermute(b, "col", backward)
        pieces += [a, b]
        pending += [pick_slot(a), pick_slot(b)]
        if any(batch[-1] == step for batch in batches):
            own = jnp.concatenate(pending, axis=1)
            pending = []
            if step < ncol - 2:
                got = own
                for j, fan in enumerate(fans, start=1):
                    got = jnp.where(which == j, lax.ppermute(own, ("row", "col"), fan), got)
            else:
                got = last_fan(own)
            columns.append(got)

    blocks = jnp.concatenate(pieces, axis=1)
    column_blocks = jnp.concatenate(columns, axis=1)
    n = panels * blocks.shape[1]
    blocks = blocks.reshape(n, local_slots, blk + META, blk)
    column_blocks = column_blocks.reshape(n, blk + META, blk)

    offs = jnp.concatenate([blocks[:, :, blk + 3, 0], column_blocks[:, blk + 3, 0][:, None]], axis=1)
    offs = jnp.clip(offs.astype(jnp.int32), 0, IBS - 1).reshape(-1)
    return gram_call(offs, blocks, column_blocks)


def solution(mesh):
    nrow, ncol = mesh.shape["row"], mesh.shape["col"]
    return jax.shard_map(
        functools.partial(local, nrow=nrow, ncol=ncol),
        mesh=mesh,
        in_specs=(P(None, "col", "row", None, None), P(None, "col", None), P(None, "col", "row")),
        out_specs=P("row", "col"),
        check_vma=False,
    )
```

```python
import functools

import jax
import jax.numpy as jnp
from jax import lax
from jax.experimental import pallas as pl
from jax.experimental.pallas import tpu as pltpu
from jax.sharding import PartitionSpec as P

IBS = 8
CHUNK = 32
META = 16


def gram_kernel(offs_ref, bs_ref, bc_ref, o_ref, *, chunk, local_slots, blk):
    s = pl.program_id(0)
    step = pl.program_id(1)

    @pl.when(step == 0)
    def _():
        o_ref[...] = jnp.zeros_like(o_ref)

    stride = local_slots + 1
    for k in range(chunk):
        g = step * chunk + k
        meta = bs_ref[k, 0, blk : blk + META].astype(jnp.float32)
        w = meta[0:1] + meta[1:2] + meta[2:3]
        lhs = (bs_ref[k, 0, :blk].T.astype(jnp.float32) * w).astype(jnp.bfloat16)
        prod = jnp.dot(lhs, bc_ref[k, :blk], preferred_element_type=jnp.float32)
        col = pl.multiple_of(offs_ref[g * stride + local_slots] * blk, blk)
        row = pl.multiple_of(offs_ref[g * stride + s] * blk, blk)
        o_ref[pl.ds(row, blk), pl.ds(col, blk)] += prod


def gram_call(offs, bs, bc):
    n, local_slots, rows, blk = bs.shape
    chunk = CHUNK
    kernel = functools.partial(gram_kernel, chunk=chunk, local_slots=local_slots, blk=blk)
    out_rows, out_cols = local_slots * IBS * blk, IBS * blk
    return pl.pallas_call(
        kernel,
        grid_spec=pltpu.PrefetchScalarGridSpec(
            num_scalar_prefetch=1,
            grid=(local_slots, n // chunk),
            in_specs=[
                pl.BlockSpec((chunk, 1, rows, blk), lambda s, i, o: (i, s, 0, 0)),
                pl.BlockSpec((chunk, rows, blk), lambda s, i, o: (i, 0, 0)),
            ],
            out_specs=pl.BlockSpec((IBS * blk, out_cols), lambda s, i, o: (s, 0)),
        ),
        out_shape=jax.ShapeDtypeStruct((out_rows, out_cols), jnp.float32),
        compiler_params=pltpu.CompilerParams(
            dimension_semantics=("arbitrary", "arbitrary"), vmem_limit_bytes=48 * 1024 * 1024
        ),
        cost_estimate=pl.CostEstimate(
            flops=2 * n * local_slots * blk * blk * blk,
            transcendentals=0,
            bytes_accessed=n * (local_slots + 1) * blk * blk * 2 + out_rows * out_cols * 4,
        ),
    )(offs, bs, bc)


def with_meta(panel_blocks, user_weights, slot_offset):
    panels, users, local_slots, blk, _ = panel_blocks.shape
    hi = lax.reduce_precision(user_weights, exponent_bits=8, mantissa_bits=7)
    rest = user_weights - hi
    mid = lax.reduce_precision(rest, exponent_bits=8, mantissa_bits=7)
    low = rest - mid
    weight_rows = jnp.stack([hi, mid, low], axis=2).astype(jnp.bfloat16)[:, :, None]
    weight_rows = jnp.broadcast_to(weight_rows, (panels, users, local_slots, 3, blk))
    offset_rows = jnp.broadcast_to(
        slot_offset.astype(jnp.bfloat16)[..., None, None], (panels, users, local_slots, 1, blk)
    )
    pad = jnp.zeros((panels, users, local_slots, META - 4, blk), jnp.bfloat16)
    return jnp.concatenate([panel_blocks, weight_rows, offset_rows, pad], axis=3)


def local(panel_blocks, user_weights, slot_offset, *, nrow, ncol):
    panels, _, local_slots, blk, _ = panel_blocks.shape
    r = lax.axis_index("row")
    c = lax.axis_index("col")
    x = with_meta(panel_blocks, user_weights, slot_offset)

    outer = ncol // 2
    cycle = [a * 2 for a in range(outer)] + [a * 2 + 1 for a in reversed(range(outer))]
    forward = [(cycle[i], cycle[(i + 1) % ncol]) for i in range(ncol)]
    backward = [(b, a) for a, b in forward]

    src = c // local_slots
    which = (r - src + nrow) % nrow
    slot = c % local_slots
    fans = [
        [
            ((cc // local_slots) * ncol + cc, ((cc // local_slots + j) % nrow) * ncol + cc)
            for cc in range(ncol)
        ]
        for j in range(1, nrow)
    ]

    nx = nrow // 2
    is_s, is_p = which == 0, r == src + 1 - 2 * (src % 2)
    is_d1 = (which % 2 == 0) & (which != 0)

    def send(v, pairs):
        return lax.ppermute(v, ("row", "col"), [(a * ncol + cc, b * ncol + cc) for a, b, cc in pairs])

    def last_fan(own):
        heads = [cc // local_slots for cc in range(ncol)]
        to_partner = send(own, [(h, h ^ 1, cc) for cc, h in enumerate(heads)])
        to_d1 = None
        for j in range(1, nx):
            v = send(own, [(h, (h + 2 * j) % nrow, cc) for cc, h in enumerate(heads)])
            to_d1 = v if to_d1 is None else jnp.where(which // 2 == j, v, to_d1)
        to_d2 = send(
            to_d1,
            [((h + 2 * j) % nrow, ((h + 2 * j) % nrow) ^ 1, cc) for cc, h in enumerate(heads) for j in range(1, nx)],
        )
        return jnp.where(is_s, own, jnp.where(is_p, to_partner, jnp.where(is_d1, to_d1, to_d2)))

    def pick_slot(piece):
        return lax.dynamic_index_in_dim(piece, slot, axis=2, keepdims=False)

    batches = [[k, k + 1] for k in range(0, ncol - 2, 2)] + [[ncol - 2], [ncol - 1]]
    half = x.shape[1] // 2
    a, b = x[:, :half], x[:, half:]
    pieces, columns, pending = [], [], []
    for step in range(ncol):
        if step:
            a = lax.ppermute(a, "col", forward)
            b = lax.ppermute(b, "col", backward)
        pieces += [a, b]
        pending += [pick_slot(a), pick_slot(b)]
        if any(batch[-1] == step for batch in batches):
            own = jnp.concatenate(pending, axis=1)
            pending = []
            if step < 0:
                got = own
                for j, fan in enumerate(fans, start=1):
                    got = jnp.where(which == j, lax.ppermute(own, ("row", "col"), fan), got)
            else:
                got = last_fan(own)
            columns.append(got)

    blocks = jnp.concatenate(pieces, axis=1)
    column_blocks = jnp.concatenate(columns, axis=1)
    n = panels * blocks.shape[1]
    blocks = blocks.reshape(n, local_slots, blk + META, blk)
    column_blocks = column_blocks.reshape(n, blk + META, blk)

    offs = jnp.concatenate([blocks[:, :, blk + 3, 0], column_blocks[:, blk + 3, 0][:, None]], axis=1)
    offs = jnp.clip(offs.astype(jnp.int32), 0, IBS - 1).reshape(-1)
    return gram_call(offs, blocks, column_blocks)


def solution(mesh):
    nrow, ncol = mesh.shape["row"], mesh.shape["col"]
    return jax.shard_map(
        functools.partial(local, nrow=nrow, ncol=ncol),
        mesh=mesh,
        in_specs=(P(None, "col", "row", None, None), P(None, "col", None), P(None, "col", "row")),
        out_specs=P("row", "col"),
        check_vma=False,
    )
```

```python
import functools

import jax
import jax.numpy as jnp
from jax import lax
from jax.experimental import pallas as pl
from jax.experimental.pallas import tpu as pltpu
from jax.sharding import PartitionSpec as P

IBS = 8
CHUNK = 32
META = 16


def gram_kernel(offs_ref, bs_ref, bc_ref, o_ref, *, chunk, local_slots, blk):
    s = pl.program_id(0)
    step = pl.program_id(1)

    @pl.when(step == 0)
    def _():
        o_ref[...] = jnp.zeros_like(o_ref)

    stride = local_slots + 1
    for k in range(chunk):
        g = step * chunk + k
        meta = bs_ref[k, 0, blk : blk + META].astype(jnp.float32)
        w = meta[0:1] + meta[1:2] + meta[2:3]
        lhs = (bs_ref[k, 0, :blk].T.astype(jnp.float32) * w).astype(jnp.bfloat16)
        prod = jnp.dot(lhs, bc_ref[k, :blk], preferred_element_type=jnp.float32)
        col = pl.multiple_of(offs_ref[g * stride + local_slots] * blk, blk)
        row = pl.multiple_of(offs_ref[g * stride + s] * blk, blk)
        o_ref[pl.ds(row, blk), pl.ds(col, blk)] += prod


def gram_call(offs, bs, bc):
    n, local_slots, rows, blk = bs.shape
    chunk = CHUNK
    kernel = functools.partial(gram_kernel, chunk=chunk, local_slots=local_slots, blk=blk)
    out_rows, out_cols = local_slots * IBS * blk, IBS * blk
    return pl.pallas_call(
        kernel,
        grid_spec=pltpu.PrefetchScalarGridSpec(
            num_scalar_prefetch=1,
            grid=(local_slots, n // chunk),
            in_specs=[
                pl.BlockSpec((chunk, 1, rows, blk), lambda s, i, o: (i, s, 0, 0)),
                pl.BlockSpec((chunk, rows, blk), lambda s, i, o: (i, 0, 0)),
            ],
            out_specs=pl.BlockSpec((IBS * blk, out_cols), lambda s, i, o: (s, 0)),
        ),
        out_shape=jax.ShapeDtypeStruct((out_rows, out_cols), jnp.float32),
        compiler_params=pltpu.CompilerParams(
            dimension_semantics=("arbitrary", "arbitrary"), vmem_limit_bytes=48 * 1024 * 1024
        ),
        cost_estimate=pl.CostEstimate(
            flops=2 * n * local_slots * blk * blk * blk,
            transcendentals=0,
            bytes_accessed=n * (local_slots + 1) * blk * blk * 2 + out_rows * out_cols * 4,
        ),
    )(offs, bs, bc)


def with_meta(panel_blocks, user_weights, slot_offset):
    panels, users, local_slots, blk, _ = panel_blocks.shape
    hi = lax.reduce_precision(user_weights, exponent_bits=8, mantissa_bits=7)
    rest = user_weights - hi
    mid = lax.reduce_precision(rest, exponent_bits=8, mantissa_bits=7)
    low = rest - mid
    weight_rows = jnp.stack([hi, mid, low], axis=2).astype(jnp.bfloat16)[:, :, None]
    weight_rows = jnp.broadcast_to(weight_rows, (panels, users, local_slots, 3, blk))
    offset_rows = jnp.broadcast_to(
        slot_offset.astype(jnp.bfloat16)[..., None, None], (panels, users, local_slots, 1, blk)
    )
    pad = jnp.zeros((panels, users, local_slots, META - 4, blk), jnp.bfloat16)
    return jnp.concatenate([panel_blocks, weight_rows, offset_rows, pad], axis=3)


def local(panel_blocks, user_weights, slot_offset, *, nrow, ncol):
    panels, _, local_slots, blk, _ = panel_blocks.shape
    r = lax.axis_index("row")
    c = lax.axis_index("col")
    x = with_meta(panel_blocks, user_weights, slot_offset)

    outer = ncol // 2
    cycle = [a * 2 for a in range(outer)] + [a * 2 + 1 for a in reversed(range(outer))]
    forward = [(cycle[i], cycle[(i + 1) % ncol]) for i in range(ncol)]
    backward = [(b, a) for a, b in forward]

    src = c // local_slots
    which = (r - src + nrow) % nrow
    slot = c % local_slots
    fans = [
        [
            ((cc // local_slots) * ncol + cc, ((cc // local_slots + j) % nrow) * ncol + cc)
            for cc in range(ncol)
        ]
        for j in range(1, nrow)
    ]

    nx = nrow // 2
    is_s, is_p = which == 0, r == src + 1 - 2 * (src % 2)
    is_d1 = (which % 2 == 0) & (which != 0)

    def send(v, pairs):
        return lax.ppermute(v, ("row", "col"), [(a * ncol + cc, b * ncol + cc) for a, b, cc in pairs])

    def last_fan(own):
        heads = [cc // local_slots for cc in range(ncol)]
        to_d1 = None
        for j in range(1, nx):
            v = send(own, [(h, (h + 2 * j) % nrow, cc) for cc, h in enumerate(heads)])
            to_d1 = v if to_d1 is None else jnp.where(which // 2 == j, v, to_d1)
        second_pairs = [(h, h ^ 1, cc) for cc, h in enumerate(heads)]
        second_pairs += [
            ((h + 2 * j) % nrow, ((h + 2 * j) % nrow) ^ 1, cc)
            for cc, h in enumerate(heads)
            for j in range(1, nx)
        ]
        second = send(jnp.where(is_s, own, to_d1), second_pairs)
        return jnp.where(is_s, own, jnp.where(is_d1, to_d1, second))

    def pick_slot(piece):
        return lax.dynamic_index_in_dim(piece, slot, axis=2, keepdims=False)

    batches = [[k, k + 1] for k in range(0, ncol - 2, 2)] + [[ncol - 2], [ncol - 1]]
    half = x.shape[1] // 2
    a, b = x[:, :half], x[:, half:]
    pieces, columns, pending = [], [], []
    for step in range(ncol):
        if step:
            a = lax.ppermute(a, "col", forward)
            b = lax.ppermute(b, "col", backward)
        pieces += [a, b]
        pending += [pick_slot(a), pick_slot(b)]
        if any(batch[-1] == step for batch in batches):
            own = jnp.concatenate(pending, axis=1)
            pending = []
            if step < 0:
                got = own
                for j, fan in enumerate(fans, start=1):
                    got = jnp.where(which == j, lax.ppermute(own, ("row", "col"), fan), got)
            else:
                got = last_fan(own)
            columns.append(got)

    blocks = jnp.concatenate(pieces, axis=1)
    column_blocks = jnp.concatenate(columns, axis=1)
    n = panels * blocks.shape[1]
    blocks = blocks.reshape(n, local_slots, blk + META, blk)
    column_blocks = column_blocks.reshape(n, blk + META, blk)

    offs = jnp.concatenate([blocks[:, :, blk + 3, 0], column_blocks[:, blk + 3, 0][:, None]], axis=1)
    offs = jnp.clip(offs.astype(jnp.int32), 0, IBS - 1).reshape(-1)
    return gram_call(offs, blocks, column_blocks)


def solution(mesh):
    nrow, ncol = mesh.shape["row"], mesh.shape["col"]
    return jax.shard_map(
        functools.partial(local, nrow=nrow, ncol=ncol),
        mesh=mesh,
        in_specs=(P(None, "col", "row", None, None), P(None, "col", None), P(None, "col", "row")),
        out_specs=P("row", "col"),
        check_vma=False,
    )
```

```python
import functools

import jax
import jax.numpy as jnp
from jax import lax
from jax.experimental import pallas as pl
from jax.experimental.pallas import tpu as pltpu
from jax.sharding import PartitionSpec as P

IBS = 8
CHUNK = 32
META = 16


def gram_kernel(offs_ref, bs_ref, bc_ref, o_ref, *, chunk, local_slots, blk):
    s = pl.program_id(0)
    step = pl.program_id(1)

    @pl.when(step == 0)
    def _():
        o_ref[...] = jnp.zeros_like(o_ref)

    stride = local_slots + 1
    for k in range(chunk):
        g = step * chunk + k
        meta = bs_ref[k, 0, blk : blk + META].astype(jnp.float32)
        w = meta[0:1] + meta[1:2] + meta[2:3]
        lhs = (bs_ref[k, 0, :blk].T.astype(jnp.float32) * w).astype(jnp.bfloat16)
        prod = jnp.dot(lhs, bc_ref[k, :blk], preferred_element_type=jnp.float32)
        col = pl.multiple_of(offs_ref[g * stride + local_slots] * blk, blk)
        row = pl.multiple_of(offs_ref[g * stride + s] * blk, blk)
        o_ref[pl.ds(row, blk), pl.ds(col, blk)] += prod


def gram_call(offs, bs, bc):
    n, local_slots, rows, blk = bs.shape
    chunk = CHUNK
    kernel = functools.partial(gram_kernel, chunk=chunk, local_slots=local_slots, blk=blk)
    out_rows, out_cols = local_slots * IBS * blk, IBS * blk
    return pl.pallas_call(
        kernel,
        grid_spec=pltpu.PrefetchScalarGridSpec(
            num_scalar_prefetch=1,
            grid=(local_slots, n // chunk),
            in_specs=[
                pl.BlockSpec((chunk, 1, rows, blk), lambda s, i, o: (i, s, 0, 0)),
                pl.BlockSpec((chunk, rows, blk), lambda s, i, o: (i, 0, 0)),
            ],
            out_specs=pl.BlockSpec((IBS * blk, out_cols), lambda s, i, o: (s, 0)),
        ),
        out_shape=jax.ShapeDtypeStruct((out_rows, out_cols), jnp.float32),
        compiler_params=pltpu.CompilerParams(
            dimension_semantics=("arbitrary", "arbitrary"), vmem_limit_bytes=48 * 1024 * 1024
        ),
        cost_estimate=pl.CostEstimate(
            flops=2 * n * local_slots * blk * blk * blk,
            transcendentals=0,
            bytes_accessed=n * (local_slots + 1) * blk * blk * 2 + out_rows * out_cols * 4,
        ),
    )(offs, bs, bc)


def with_meta(panel_blocks, user_weights, slot_offset):
    panels, users, local_slots, blk, _ = panel_blocks.shape
    hi = lax.reduce_precision(user_weights, exponent_bits=8, mantissa_bits=7)
    rest = user_weights - hi
    mid = lax.reduce_precision(rest, exponent_bits=8, mantissa_bits=7)
    low = rest - mid
    weight_rows = jnp.stack([hi, mid, low], axis=2).astype(jnp.bfloat16)[:, :, None]
    weight_rows = jnp.broadcast_to(weight_rows, (panels, users, local_slots, 3, blk))
    offset_rows = jnp.broadcast_to(
        slot_offset.astype(jnp.bfloat16)[..., None, None], (panels, users, local_slots, 1, blk)
    )
    pad = jnp.zeros((panels, users, local_slots, META - 4, blk), jnp.bfloat16)
    return jnp.concatenate([panel_blocks, weight_rows, offset_rows, pad], axis=3)


def local(panel_blocks, user_weights, slot_offset, *, nrow, ncol):
    panels, _, local_slots, blk, _ = panel_blocks.shape
    r = lax.axis_index("row")
    c = lax.axis_index("col")
    x = with_meta(panel_blocks, user_weights, slot_offset)

    outer = ncol // 2
    cycle = [a * 2 for a in range(outer)] + [a * 2 + 1 for a in reversed(range(outer))]
    forward = [(cycle[i], cycle[(i + 1) % ncol]) for i in range(ncol)]
    backward = [(b, a) for a, b in forward]

    src = c // local_slots
    which = (r - src + nrow) % nrow
    slot = c % local_slots
    fans = [
        [
            ((cc // local_slots) * ncol + cc, ((cc // local_slots + j) % nrow) * ncol + cc)
            for cc in range(ncol)
        ]
        for j in range(1, nrow)
    ]

    nx = nrow // 2
    is_s, is_p = which == 0, r == src + 1 - 2 * (src % 2)
    is_d1 = (which % 2 == 0) & (which != 0)

    def send(v, pairs):
        return lax.ppermute(v, ("row", "col"), [(a * ncol + cc, b * ncol + cc) for a, b, cc in pairs])

    def last_fan(own):
        heads = [cc // local_slots for cc in range(ncol)]
        to_partner = send(own, [(h, h ^ 1, cc) for cc, h in enumerate(heads)])
        to_d1 = None
        for j in range(1, nx):
            v = send(own, [(h, (h + 2 * j) % nrow, cc) for cc, h in enumerate(heads)])
            to_d1 = v if to_d1 is None else jnp.where(which // 2 == j, v, to_d1)
        to_d2 = send(
            to_d1,
            [((h + 2 * j) % nrow, ((h + 2 * j) % nrow) ^ 1, cc) for cc, h in enumerate(heads) for j in range(1, nx)],
        )
        return jnp.where(is_s, own, jnp.where(is_p, to_partner, jnp.where(is_d1, to_d1, to_d2)))

    def pick_slot(piece):
        return lax.dynamic_index_in_dim(piece, slot, axis=2, keepdims=False)

    batches = [list(range(k, min(k + 3, ncol - 2))) for k in range(0, ncol - 2, 3)] + [[ncol - 2], [ncol - 1]]
    half = x.shape[1] // 2
    a, b = x[:, :half], x[:, half:]
    pieces, columns, pending = [], [], []
    for step in range(ncol):
        if step:
            a = lax.ppermute(a, "col", forward)
            b = lax.ppermute(b, "col", backward)
        pieces += [a, b]
        pending += [pick_slot(a), pick_slot(b)]
        if any(batch[-1] == step for batch in batches):
            own = jnp.concatenate(pending, axis=1)
            pending = []
            if step < 0:
                got = own
                for j, fan in enumerate(fans, start=1):
                    got = jnp.where(which == j, lax.ppermute(own, ("row", "col"), fan), got)
            else:
                got = last_fan(own)
            columns.append(got)

    blocks = jnp.concatenate(pieces, axis=1)
    column_blocks = jnp.concatenate(columns, axis=1)
    n = panels * blocks.shape[1]
    blocks = blocks.reshape(n, local_slots, blk + META, blk)
    column_blocks = column_blocks.reshape(n, blk + META, blk)

    offs = jnp.concatenate([blocks[:, :, blk + 3, 0], column_blocks[:, blk + 3, 0][:, None]], axis=1)
    offs = jnp.clip(offs.astype(jnp.int32), 0, IBS - 1).reshape(-1)
    return gram_call(offs, blocks, column_blocks)


def solution(mesh):
    nrow, ncol = mesh.shape["row"], mesh.shape["col"]
    return jax.shard_map(
        functools.partial(local, nrow=nrow, ncol=ncol),
        mesh=mesh,
        in_specs=(P(None, "col", "row", None, None), P(None, "col", None), P(None, "col", "row")),
        out_specs=P("row", "col"),
        check_vma=False,
    )
```

```python
import functools

import jax
import jax.numpy as jnp
from jax import lax
from jax.experimental import pallas as pl
from jax.experimental.pallas import tpu as pltpu
from jax.sharding import PartitionSpec as P

IBS = 8
CHUNK = 32
META = 16


def gram_kernel(offs_ref, bs_ref, bc_ref, o_ref, *, chunk, local_slots, blk):
    s = pl.program_id(0)
    step = pl.program_id(1)

    @pl.when(step == 0)
    def _():
        o_ref[...] = jnp.zeros_like(o_ref)

    stride = local_slots + 1
    for k in range(chunk):
        g = step * chunk + k
        meta = bs_ref[k, 0, blk : blk + META].astype(jnp.float32)
        w = meta[0:1] + meta[1:2] + meta[2:3]
        lhs = (bs_ref[k, 0, :blk].T.astype(jnp.float32) * w).astype(jnp.bfloat16)
        prod = jnp.dot(lhs, bc_ref[k, :blk], preferred_element_type=jnp.float32)
        col = pl.multiple_of(offs_ref[g * stride + local_slots] * blk, blk)
        row = pl.multiple_of(offs_ref[g * stride + s] * blk, blk)
        o_ref[pl.ds(row, blk), pl.ds(col, blk)] += prod


def gram_call(offs, bs, bc):
    n, local_slots, rows, blk = bs.shape
    chunk = CHUNK
    kernel = functools.partial(gram_kernel, chunk=chunk, local_slots=local_slots, blk=blk)
    out_rows, out_cols = local_slots * IBS * blk, IBS * blk
    return pl.pallas_call(
        kernel,
        grid_spec=pltpu.PrefetchScalarGridSpec(
            num_scalar_prefetch=1,
            grid=(local_slots, n // chunk),
            in_specs=[
                pl.BlockSpec((chunk, 1, rows, blk), lambda s, i, o: (i, s, 0, 0)),
                pl.BlockSpec((chunk, rows, blk), lambda s, i, o: (i, 0, 0)),
            ],
            out_specs=pl.BlockSpec((IBS * blk, out_cols), lambda s, i, o: (s, 0)),
        ),
        out_shape=jax.ShapeDtypeStruct((out_rows, out_cols), jnp.float32),
        compiler_params=pltpu.CompilerParams(
            dimension_semantics=("arbitrary", "arbitrary"), vmem_limit_bytes=48 * 1024 * 1024
        ),
        cost_estimate=pl.CostEstimate(
            flops=2 * n * local_slots * blk * blk * blk,
            transcendentals=0,
            bytes_accessed=n * (local_slots + 1) * blk * blk * 2 + out_rows * out_cols * 4,
        ),
    )(offs, bs, bc)


def with_meta(panel_blocks, user_weights, slot_offset):
    panels, users, local_slots, blk, _ = panel_blocks.shape
    hi = lax.reduce_precision(user_weights, exponent_bits=8, mantissa_bits=7)
    rest = user_weights - hi
    mid = lax.reduce_precision(rest, exponent_bits=8, mantissa_bits=7)
    low = rest - mid
    weight_rows = jnp.stack([hi, mid, low], axis=2).astype(jnp.bfloat16)[:, :, None]
    weight_rows = jnp.broadcast_to(weight_rows, (panels, users, local_slots, 3, blk))
    offset_rows = jnp.broadcast_to(
        slot_offset.astype(jnp.bfloat16)[..., None, None], (panels, users, local_slots, 1, blk)
    )
    pad = jnp.zeros((panels, users, local_slots, META - 4, blk), jnp.bfloat16)
    return jnp.concatenate([panel_blocks, weight_rows, offset_rows, pad], axis=3)


def local(panel_blocks, user_weights, slot_offset, *, nrow, ncol):
    panels, _, local_slots, blk, _ = panel_blocks.shape
    r = lax.axis_index("row")
    c = lax.axis_index("col")

    outer = ncol // 2
    cycle = [a * 2 for a in range(outer)] + [a * 2 + 1 for a in reversed(range(outer))]
    forward = [(cycle[i], cycle[(i + 1) % ncol]) for i in range(ncol)]
    backward = [(b, a) for a, b in forward]

    src = c // local_slots
    which = (r - src + nrow) % nrow
    slot = c % local_slots
    fans = [
        [
            ((cc // local_slots) * ncol + cc, ((cc // local_slots + j) % nrow) * ncol + cc)
            for cc in range(ncol)
        ]
        for j in range(1, nrow)
    ]

    nx = nrow // 2
    is_s, is_p = which == 0, r == src + 1 - 2 * (src % 2)
    is_d1 = (which % 2 == 0) & (which != 0)

    def send(v, pairs):
        return lax.ppermute(v, ("row", "col"), [(a * ncol + cc, b * ncol + cc) for a, b, cc in pairs])

    def last_fan(own):
        heads = [cc // local_slots for cc in range(ncol)]
        to_partner = send(own, [(h, h ^ 1, cc) for cc, h in enumerate(heads)])
        to_d1 = None
        for j in range(1, nx):
            v = send(own, [(h, (h + 2 * j) % nrow, cc) for cc, h in enumerate(heads)])
            to_d1 = v if to_d1 is None else jnp.where(which // 2 == j, v, to_d1)
        to_d2 = send(
            to_d1,
            [((h + 2 * j) % nrow, ((h + 2 * j) % nrow) ^ 1, cc) for cc, h in enumerate(heads) for j in range(1, nx)],
        )
        return jnp.where(is_s, own, jnp.where(is_p, to_partner, jnp.where(is_d1, to_d1, to_d2)))

    def pick_slot(piece):
        return lax.dynamic_index_in_dim(piece, slot, axis=2, keepdims=False)

    batches = [[k, k + 1] for k in range(0, ncol - 2, 2)] + [[ncol - 2], [ncol - 1]]
    half = panel_blocks.shape[1] // 2
    a = with_meta(panel_blocks[:, :half], user_weights[:, :half], slot_offset[:, :half])
    b = with_meta(panel_blocks[:, half:], user_weights[:, half:], slot_offset[:, half:])
    pieces, columns, pending = [], [], []
    for step in range(ncol):
        if step:
            a = lax.ppermute(a, "col", forward)
            b = lax.ppermute(b, "col", backward)
        pieces += [a, b]
        pending += [pick_slot(a), pick_slot(b)]
        if any(batch[-1] == step for batch in batches):
            own = jnp.concatenate(pending, axis=1)
            pending = []
            if step < 0:
                got = own
                for j, fan in enumerate(fans, start=1):
                    got = jnp.where(which == j, lax.ppermute(own, ("row", "col"), fan), got)
            else:
                got = last_fan(own)
            columns.append(got)

    blocks = jnp.concatenate(pieces, axis=1)
    column_blocks = jnp.concatenate(columns, axis=1)
    n = panels * blocks.shape[1]
    blocks = blocks.reshape(n, local_slots, blk + META, blk)
    column_blocks = column_blocks.reshape(n, blk + META, blk)

    offs = jnp.concatenate([blocks[:, :, blk + 3, 0], column_blocks[:, blk + 3, 0][:, None]], axis=1)
    offs = jnp.clip(offs.astype(jnp.int32), 0, IBS - 1).reshape(-1)
    return gram_call(offs, blocks, column_blocks)


def solution(mesh):
    nrow, ncol = mesh.shape["row"], mesh.shape["col"]
    return jax.shard_map(
        functools.partial(local, nrow=nrow, ncol=ncol),
        mesh=mesh,
        in_specs=(P(None, "col", "row", None, None), P(None, "col", None), P(None, "col", "row")),
        out_specs=P("row", "col"),
        check_vma=False,
    )
```

```python
import functools

import jax
import jax.numpy as jnp
from jax import lax
from jax.experimental import pallas as pl
from jax.experimental.pallas import tpu as pltpu
from jax.sharding import PartitionSpec as P

IBS = 8
CHUNK = 48
META = 16


def gram_kernel(offs_ref, bs_ref, bc_ref, o_ref, *, chunk, local_slots, blk):
    s = pl.program_id(0)
    step = pl.program_id(1)

    @pl.when(step == 0)
    def _():
        o_ref[...] = jnp.zeros_like(o_ref)

    stride = local_slots + 1
    for k in range(chunk):
        g = step * chunk + k
        meta = bs_ref[k, 0, blk : blk + META].astype(jnp.float32)
        w = meta[0:1] + meta[1:2] + meta[2:3]
        lhs = (bs_ref[k, 0, :blk].T.astype(jnp.float32) * w).astype(jnp.bfloat16)
        prod = jnp.dot(lhs, bc_ref[k, :blk], preferred_element_type=jnp.float32)
        col = pl.multiple_of(offs_ref[g * stride + local_slots] * blk, blk)
        row = pl.multiple_of(offs_ref[g * stride + s] * blk, blk)
        o_ref[pl.ds(row, blk), pl.ds(col, blk)] += prod


def gram_call(offs, bs, bc):
    n, local_slots, rows, blk = bs.shape
    chunk = CHUNK
    kernel = functools.partial(gram_kernel, chunk=chunk, local_slots=local_slots, blk=blk)
    out_rows, out_cols = local_slots * IBS * blk, IBS * blk
    return pl.pallas_call(
        kernel,
        grid_spec=pltpu.PrefetchScalarGridSpec(
            num_scalar_prefetch=1,
            grid=(local_slots, n // chunk),
            in_specs=[
                pl.BlockSpec((chunk, 1, rows, blk), lambda s, i, o: (i, s, 0, 0)),
                pl.BlockSpec((chunk, rows, blk), lambda s, i, o: (i, 0, 0)),
            ],
            out_specs=pl.BlockSpec((IBS * blk, out_cols), lambda s, i, o: (s, 0)),
        ),
        out_shape=jax.ShapeDtypeStruct((out_rows, out_cols), jnp.float32),
        compiler_params=pltpu.CompilerParams(
            dimension_semantics=("arbitrary", "arbitrary"), vmem_limit_bytes=48 * 1024 * 1024
        ),
        cost_estimate=pl.CostEstimate(
            flops=2 * n * local_slots * blk * blk * blk,
            transcendentals=0,
            bytes_accessed=n * (local_slots + 1) * blk * blk * 2 + out_rows * out_cols * 4,
        ),
    )(offs, bs, bc)


def with_meta(panel_blocks, user_weights, slot_offset):
    panels, users, local_slots, blk, _ = panel_blocks.shape
    hi = lax.reduce_precision(user_weights, exponent_bits=8, mantissa_bits=7)
    rest = user_weights - hi
    mid = lax.reduce_precision(rest, exponent_bits=8, mantissa_bits=7)
    low = rest - mid
    weight_rows = jnp.stack([hi, mid, low], axis=2).astype(jnp.bfloat16)[:, :, None]
    weight_rows = jnp.broadcast_to(weight_rows, (panels, users, local_slots, 3, blk))
    offset_rows = jnp.broadcast_to(
        slot_offset.astype(jnp.bfloat16)[..., None, None], (panels, users, local_slots, 1, blk)
    )
    pad = jnp.zeros((panels, users, local_slots, META - 4, blk), jnp.bfloat16)
    return jnp.concatenate([panel_blocks, weight_rows, offset_rows, pad], axis=3)


def local(panel_blocks, user_weights, slot_offset, *, nrow, ncol):
    panels, _, local_slots, blk, _ = panel_blocks.shape
    r = lax.axis_index("row")
    c = lax.axis_index("col")
    x = with_meta(panel_blocks, user_weights, slot_offset)

    outer = ncol // 2
    cycle = [a * 2 for a in range(outer)] + [a * 2 + 1 for a in reversed(range(outer))]
    forward = [(cycle[i], cycle[(i + 1) % ncol]) for i in range(ncol)]
    backward = [(b, a) for a, b in forward]

    src = c // local_slots
    which = (r - src + nrow) % nrow
    slot = c % local_slots
    fans = [
        [
            ((cc // local_slots) * ncol + cc, ((cc // local_slots + j) % nrow) * ncol + cc)
            for cc in range(ncol)
        ]
        for j in range(1, nrow)
    ]

    nx = nrow // 2
    is_s, is_p = which == 0, r == src + 1 - 2 * (src % 2)
    is_d1 = (which % 2 == 0) & (which != 0)

    def send(v, pairs):
        return lax.ppermute(v, ("row", "col"), [(a * ncol + cc, b * ncol + cc) for a, b, cc in pairs])

    def last_fan(own):
        heads = [cc // local_slots for cc in range(ncol)]
        to_partner = send(own, [(h, h ^ 1, cc) for cc, h in enumerate(heads)])
        to_d1 = None
        for j in range(1, nx):
            v = send(own, [(h, (h + 2 * j) % nrow, cc) for cc, h in enumerate(heads)])
            to_d1 = v if to_d1 is None else jnp.where(which // 2 == j, v, to_d1)
        to_d2 = send(
            to_d1,
            [((h + 2 * j) % nrow, ((h + 2 * j) % nrow) ^ 1, cc) for cc, h in enumerate(heads) for j in range(1, nx)],
        )
        return jnp.where(is_s, own, jnp.where(is_p, to_partner, jnp.where(is_d1, to_d1, to_d2)))

    def pick_slot(piece):
        return lax.dynamic_index_in_dim(piece, slot, axis=2, keepdims=False)

    batches = [[k, k + 1] for k in range(0, ncol - 2, 2)] + [[ncol - 2], [ncol - 1]]
    half = x.shape[1] // 2
    a, b = x[:, :half], x[:, half:]
    pieces, columns, pending = [], [], []
    for step in range(ncol):
        if step:
            a = lax.ppermute(a, "col", forward)
            b = lax.ppermute(b, "col", backward)
        pieces += [a, b]
        pending += [pick_slot(a), pick_slot(b)]
        if any(batch[-1] == step for batch in batches):
            own = jnp.concatenate(pending, axis=1)
            pending = []
            if step < 0:
                got = own
                for j, fan in enumerate(fans, start=1):
                    got = jnp.where(which == j, lax.ppermute(own, ("row", "col"), fan), got)
            else:
                got = last_fan(own)
            columns.append(got)

    blocks = jnp.concatenate(pieces, axis=1)
    column_blocks = jnp.concatenate(columns, axis=1)
    n = panels * blocks.shape[1]
    blocks = blocks.reshape(n, local_slots, blk + META, blk)
    column_blocks = column_blocks.reshape(n, blk + META, blk)

    offs = jnp.concatenate([blocks[:, :, blk + 3, 0], column_blocks[:, blk + 3, 0][:, None]], axis=1)
    offs = jnp.clip(offs.astype(jnp.int32), 0, IBS - 1).reshape(-1)
    return gram_call(offs, blocks, column_blocks)


def solution(mesh):
    nrow, ncol = mesh.shape["row"], mesh.shape["col"]
    return jax.shard_map(
        functools.partial(local, nrow=nrow, ncol=ncol),
        mesh=mesh,
        in_specs=(P(None, "col", "row", None, None), P(None, "col", None), P(None, "col", "row")),
        out_specs=P("row", "col"),
        check_vma=False,
    )
```

```python
import functools

import jax
import jax.numpy as jnp
from jax import lax
from jax.experimental import pallas as pl
from jax.experimental.pallas import tpu as pltpu
from jax.sharding import PartitionSpec as P

IBS = 8
CHUNK = 48
META = 16


def gram_kernel(offs_ref, bs_ref, bc_ref, o_ref, *, chunk, local_slots, blk):
    s = pl.program_id(0)
    step = pl.program_id(1)

    @pl.when(step == 0)
    def _():
        o_ref[...] = jnp.zeros_like(o_ref)

    stride = local_slots + 1
    for k in range(chunk):
        g = step * chunk + k
        meta = bs_ref[k, 0, blk : blk + META].astype(jnp.float32)
        w = meta[0:1] + meta[1:2] + meta[2:3]
        lhs = (bs_ref[k, 0, :blk].T.astype(jnp.float32) * w).astype(jnp.bfloat16)
        prod = jnp.dot(lhs, bc_ref[k, :blk], preferred_element_type=jnp.float32)
        col = pl.multiple_of(offs_ref[g * stride + local_slots] * blk, blk)
        row = pl.multiple_of(offs_ref[g * stride + s] * blk, blk)
        o_ref[pl.ds(row, blk), pl.ds(col, blk)] += prod


def gram_call(offs, bs, bc):
    n, local_slots, rows, blk = bs.shape
    chunk = CHUNK
    kernel = functools.partial(gram_kernel, chunk=chunk, local_slots=local_slots, blk=blk)
    out_rows, out_cols = local_slots * IBS * blk, IBS * blk
    return pl.pallas_call(
        kernel,
        grid_spec=pltpu.PrefetchScalarGridSpec(
            num_scalar_prefetch=1,
            grid=(local_slots, n // chunk),
            in_specs=[
                pl.BlockSpec((chunk, 1, rows, blk), lambda s, i, o: (i, s, 0, 0)),
                pl.BlockSpec((chunk, rows, blk), lambda s, i, o: (i, 0, 0)),
            ],
            out_specs=pl.BlockSpec((IBS * blk, out_cols), lambda s, i, o: (s, 0)),
        ),
        out_shape=jax.ShapeDtypeStruct((out_rows, out_cols), jnp.float32),
        compiler_params=pltpu.CompilerParams(
            dimension_semantics=("arbitrary", "arbitrary"), vmem_limit_bytes=48 * 1024 * 1024
        ),
        cost_estimate=pl.CostEstimate(
            flops=2 * n * local_slots * blk * blk * blk,
            transcendentals=0,
            bytes_accessed=n * (local_slots + 1) * blk * blk * 2 + out_rows * out_cols * 4,
        ),
    )(offs, bs, bc)


def with_meta(panel_blocks, user_weights, slot_offset):
    panels, users, local_slots, blk, _ = panel_blocks.shape
    hi = lax.reduce_precision(user_weights, exponent_bits=8, mantissa_bits=7)
    rest = user_weights - hi
    mid = lax.reduce_precision(rest, exponent_bits=8, mantissa_bits=7)
    low = rest - mid
    weight_rows = jnp.stack([hi, mid, low], axis=2).astype(jnp.bfloat16)[:, :, None]
    weight_rows = jnp.broadcast_to(weight_rows, (panels, users, local_slots, 3, blk))
    offset_rows = jnp.broadcast_to(
        slot_offset.astype(jnp.bfloat16)[..., None, None], (panels, users, local_slots, 1, blk)
    )
    pad = jnp.zeros((panels, users, local_slots, META - 4, blk), jnp.bfloat16)
    return jnp.concatenate([panel_blocks, weight_rows, offset_rows, pad], axis=3)


def local(panel_blocks, user_weights, slot_offset, *, nrow, ncol):
    panels, _, local_slots, blk, _ = panel_blocks.shape
    r = lax.axis_index("row")
    c = lax.axis_index("col")
    x = with_meta(panel_blocks, user_weights, slot_offset)

    outer = ncol // 2
    cycle = [a * 2 for a in range(outer)] + [a * 2 + 1 for a in reversed(range(outer))]
    forward = [(cycle[i], cycle[(i + 1) % ncol]) for i in range(ncol)]
    backward = [(b, a) for a, b in forward]

    src = c // local_slots
    which = (r - src + nrow) % nrow
    slot = c % local_slots
    fans = [
        [
            ((cc // local_slots) * ncol + cc, ((cc // local_slots + j) % nrow) * ncol + cc)
            for cc in range(ncol)
        ]
        for j in range(1, nrow)
    ]

    nx = nrow // 2
    is_s, is_p = which == 0, r == src + 1 - 2 * (src % 2)
    is_d1 = (which % 2 == 0) & (which != 0)

    def send(v, pairs):
        return lax.ppermute(v, ("row", "col"), [(a * ncol + cc, b * ncol + cc) for a, b, cc in pairs])

    def last_fan(own):
        heads = [cc // local_slots for cc in range(ncol)]
        to_partner = send(own, [(h, h ^ 1, cc) for cc, h in enumerate(heads)])
        to_d1 = None
        for j in range(1, nx):
            v = send(own, [(h, (h + 2 * j) % nrow, cc) for cc, h in enumerate(heads)])
            to_d1 = v if to_d1 is None else jnp.where(which // 2 == j, v, to_d1)
        to_d2 = send(
            to_d1,
            [((h + 2 * j) % nrow, ((h + 2 * j) % nrow) ^ 1, cc) for cc, h in enumerate(heads) for j in range(1, nx)],
        )
        return jnp.where(is_s, own, jnp.where(is_p, to_partner, jnp.where(is_d1, to_d1, to_d2)))

    def pick_slot(piece):
        return lax.dynamic_index_in_dim(piece, slot, axis=2, keepdims=False)

    batches = [[k, k + 1] for k in range(0, ncol - 2, 2)] + [[ncol - 2], [ncol - 1]]
    half = x.shape[1] // 2
    a, b = x[:, :half], x[:, half:]
    pieces, columns, pending = [], [], []
    for step in range(ncol):
        if step:
            a = lax.ppermute(a, "col", forward)
            b = lax.ppermute(b, "col", backward)
        pieces += [a, b]
        pending += [pick_slot(a), pick_slot(b)]
        if any(batch[-1] == step for batch in batches):
            own = jnp.concatenate(pending, axis=1)
            pending = []
            if step < 0:
                got = own
                for j, fan in enumerate(fans, start=1):
                    got = jnp.where(which == j, lax.ppermute(own, ("row", "col"), fan), got)
            else:
                got = last_fan(own)
            columns.append(got)

    blocks = jnp.concatenate(pieces, axis=1)
    column_blocks = jnp.concatenate(columns, axis=1)
    n = panels * blocks.shape[1]
    blocks = blocks.reshape(n, local_slots, blk + META, blk)
    column_blocks = column_blocks.reshape(n, blk + META, blk)

    c_offs = jnp.concatenate([got[:, :, blk + 3, 0] for got in columns], axis=1).reshape(n, 1)
    offs = jnp.concatenate([blocks[:, :, blk + 3, 0], c_offs], axis=1)
    offs = jnp.clip(offs.astype(jnp.int32), 0, IBS - 1).reshape(-1)
    return gram_call(offs, blocks, column_blocks)


def solution(mesh):
    nrow, ncol = mesh.shape["row"], mesh.shape["col"]
    return jax.shard_map(
        functools.partial(local, nrow=nrow, ncol=ncol),
        mesh=mesh,
        in_specs=(P(None, "col", "row", None, None), P(None, "col", None), P(None, "col", "row")),
        out_specs=P("row", "col"),
        check_vma=False,
    )
```

```python
import functools

import jax
import jax.numpy as jnp
from jax import lax
from jax.experimental import pallas as pl
from jax.experimental.pallas import tpu as pltpu
from jax.sharding import PartitionSpec as P

IBS = 8
CHUNK = 48
META = 16


def gram_kernel(offs_ref, bs_ref, bc_ref, o_ref, *, chunk, local_slots, blk):
    s = pl.program_id(0)
    step = pl.program_id(1)

    @pl.when(step == 0)
    def _():
        o_ref[...] = jnp.zeros_like(o_ref)

    stride = local_slots + 1
    for k in range(chunk):
        g = step * chunk + k
        meta = bs_ref[k, 0, blk : blk + META].astype(jnp.float32)
        w = meta[0:1] + meta[1:2] + meta[2:3]
        lhs = (bs_ref[k, 0, :blk].T.astype(jnp.float32) * w).astype(jnp.bfloat16)
        prod = jnp.dot(lhs, bc_ref[k, :blk], preferred_element_type=jnp.float32)
        col = pl.multiple_of(offs_ref[g * stride + local_slots] * blk, blk)
        row = pl.multiple_of(offs_ref[g * stride + s] * blk, blk)
        o_ref[pl.ds(row, blk), pl.ds(col, blk)] += prod


def gram_call(offs, bs, bc):
    n, local_slots, rows, blk = bs.shape
    chunk = CHUNK
    kernel = functools.partial(gram_kernel, chunk=chunk, local_slots=local_slots, blk=blk)
    out_rows, out_cols = local_slots * IBS * blk, IBS * blk
    return pl.pallas_call(
        kernel,
        grid_spec=pltpu.PrefetchScalarGridSpec(
            num_scalar_prefetch=1,
            grid=(local_slots, n // chunk),
            in_specs=[
                pl.BlockSpec((chunk, 1, rows, blk), lambda s, i, o: (i, s, 0, 0)),
                pl.BlockSpec((chunk, rows, blk), lambda s, i, o: (i, 0, 0)),
            ],
            out_specs=pl.BlockSpec((IBS * blk, out_cols), lambda s, i, o: (s, 0)),
        ),
        out_shape=jax.ShapeDtypeStruct((out_rows, out_cols), jnp.float32),
        compiler_params=pltpu.CompilerParams(
            dimension_semantics=("arbitrary", "arbitrary"), vmem_limit_bytes=48 * 1024 * 1024
        ),
        cost_estimate=pl.CostEstimate(
            flops=2 * n * local_slots * blk * blk * blk,
            transcendentals=0,
            bytes_accessed=n * (local_slots + 1) * blk * blk * 2 + out_rows * out_cols * 4,
        ),
    )(offs, bs, bc)


def with_meta(panel_blocks, user_weights, slot_offset):
    panels, users, local_slots, blk, _ = panel_blocks.shape
    hi = lax.reduce_precision(user_weights, exponent_bits=8, mantissa_bits=7)
    rest = user_weights - hi
    mid = lax.reduce_precision(rest, exponent_bits=8, mantissa_bits=7)
    low = rest - mid
    weight_rows = jnp.stack([hi, mid, low], axis=2).astype(jnp.bfloat16)[:, :, None]
    weight_rows = jnp.broadcast_to(weight_rows, (panels, users, local_slots, 3, blk))
    offset_rows = jnp.broadcast_to(
        slot_offset.astype(jnp.bfloat16)[..., None, None], (panels, users, local_slots, 1, blk)
    )
    pad = jnp.zeros((panels, users, local_slots, META - 4, blk), jnp.bfloat16)
    return jnp.concatenate([panel_blocks, weight_rows, offset_rows, pad], axis=3)


def local(panel_blocks, user_weights, slot_offset, *, nrow, ncol):
    panels, _, local_slots, blk, _ = panel_blocks.shape
    r = lax.axis_index("row")
    c = lax.axis_index("col")
    x = with_meta(panel_blocks, user_weights, slot_offset)

    outer = ncol // 2
    cycle = [a * 2 for a in range(outer)] + [a * 2 + 1 for a in reversed(range(outer))]
    forward = [(cycle[i], cycle[(i + 1) % ncol]) for i in range(ncol)]
    backward = [(b, a) for a, b in forward]

    src = c // local_slots
    which = (r - src + nrow) % nrow
    slot = c % local_slots
    fans = [
        [
            ((cc // local_slots) * ncol + cc, ((cc // local_slots + j) % nrow) * ncol + cc)
            for cc in range(ncol)
        ]
        for j in range(1, nrow)
    ]

    nx = nrow // 2
    is_s, is_p = which == 0, r == src + 1 - 2 * (src % 2)
    is_d1 = (which % 2 == 0) & (which != 0)

    def send(v, pairs):
        return lax.ppermute(v, ("row", "col"), [(a * ncol + cc, b * ncol + cc) for a, b, cc in pairs])

    def last_fan(own):
        heads = [cc // local_slots for cc in range(ncol)]
        to_partner = send(own, [(h, h ^ 1, cc) for cc, h in enumerate(heads)])
        to_d1 = None
        for j in range(1, nx):
            v = send(own, [(h, (h + 2 * j) % nrow, cc) for cc, h in enumerate(heads)])
            to_d1 = v if to_d1 is None else jnp.where(which // 2 == j, v, to_d1)
        to_d2 = send(
            to_d1,
            [((h + 2 * j) % nrow, ((h + 2 * j) % nrow) ^ 1, cc) for cc, h in enumerate(heads) for j in range(1, nx)],
        )
        return jnp.where(is_s, own, jnp.where(is_p, to_partner, jnp.where(is_d1, to_d1, to_d2)))

    def pick_slot(piece):
        return lax.dynamic_index_in_dim(piece, slot, axis=2, keepdims=False)

    batches = [[k] for k in range(ncol)]
    half = x.shape[1] // 2
    a, b = x[:, :half], x[:, half:]
    pieces, columns, pending = [], [], []
    for step in range(ncol):
        if step:
            a = lax.ppermute(a, "col", forward)
            b = lax.ppermute(b, "col", backward)
        pieces += [a, b]
        pending += [pick_slot(a), pick_slot(b)]
        if any(batch[-1] == step for batch in batches):
            own = jnp.concatenate(pending, axis=1)
            pending = []
            if step < 0:
                got = own
                for j, fan in enumerate(fans, start=1):
                    got = jnp.where(which == j, lax.ppermute(own, ("row", "col"), fan), got)
            else:
                got = last_fan(own)
            columns.append(got)

    blocks = jnp.concatenate(pieces, axis=1)
    column_blocks = jnp.concatenate(columns, axis=1)
    n = panels * blocks.shape[1]
    blocks = blocks.reshape(n, local_slots, blk + META, blk)
    column_blocks = column_blocks.reshape(n, blk + META, blk)

    offs = jnp.concatenate([blocks[:, :, blk + 3, 0], column_blocks[:, blk + 3, 0][:, None]], axis=1)
    offs = jnp.clip(offs.astype(jnp.int32), 0, IBS - 1).reshape(-1)
    return gram_call(offs, blocks, column_blocks)


def solution(mesh):
    nrow, ncol = mesh.shape["row"], mesh.shape["col"]
    return jax.shard_map(
        functools.partial(local, nrow=nrow, ncol=ncol),
        mesh=mesh,
        in_specs=(P(None, "col", "row", None, None), P(None, "col", None), P(None, "col", "row")),
        out_specs=P("row", "col"),
        check_vma=False,
    )
```

```python
import functools

import jax
import jax.numpy as jnp
from jax import lax
from jax.experimental import pallas as pl
from jax.experimental.pallas import tpu as pltpu
from jax.sharding import PartitionSpec as P

IBS = 8
CHUNK = 48
META = 16


def gram_kernel(offs_ref, bs_ref, bc_ref, o_ref, *, chunk, local_slots, blk):
    s = pl.program_id(0)
    step = pl.program_id(1)

    @pl.when(step == 0)
    def _():
        o_ref[...] = jnp.zeros_like(o_ref)

    stride = local_slots + 1
    for k in range(chunk):
        g = step * chunk + k
        meta = bs_ref[k, 0, blk : blk + META].astype(jnp.float32)
        w = meta[0:1] + meta[1:2] + meta[2:3]
        lhs = (bs_ref[k, 0, :blk].T.astype(jnp.float32) * w).astype(jnp.bfloat16)
        prod = jnp.dot(lhs, bc_ref[k, :blk], preferred_element_type=jnp.float32)
        col = pl.multiple_of(offs_ref[g * stride + local_slots] * blk, blk)
        row = pl.multiple_of(offs_ref[g * stride + s] * blk, blk)
        o_ref[pl.ds(row, blk), pl.ds(col, blk)] += prod


def gram_call(offs, bs, bc):
    n, local_slots, rows, blk = bs.shape
    chunk = CHUNK
    kernel = functools.partial(gram_kernel, chunk=chunk, local_slots=local_slots, blk=blk)
    out_rows, out_cols = local_slots * IBS * blk, IBS * blk
    return pl.pallas_call(
        kernel,
        grid_spec=pltpu.PrefetchScalarGridSpec(
            num_scalar_prefetch=1,
            grid=(local_slots, n // chunk),
            in_specs=[
                pl.BlockSpec((chunk, 1, rows, blk), lambda s, i, o: (i, s, 0, 0)),
                pl.BlockSpec((chunk, rows, blk), lambda s, i, o: (i, 0, 0)),
            ],
            out_specs=pl.BlockSpec((IBS * blk, out_cols), lambda s, i, o: (s, 0)),
        ),
        out_shape=jax.ShapeDtypeStruct((out_rows, out_cols), jnp.float32),
        compiler_params=pltpu.CompilerParams(
            dimension_semantics=("arbitrary", "arbitrary"), vmem_limit_bytes=48 * 1024 * 1024
        ),
        cost_estimate=pl.CostEstimate(
            flops=2 * n * local_slots * blk * blk * blk,
            transcendentals=0,
            bytes_accessed=n * (local_slots + 1) * blk * blk * 2 + out_rows * out_cols * 4,
        ),
    )(offs, bs, bc)


def with_meta(panel_blocks, user_weights, slot_offset):
    panels, users, local_slots, blk, _ = panel_blocks.shape
    hi = lax.reduce_precision(user_weights, exponent_bits=8, mantissa_bits=7)
    rest = user_weights - hi
    mid = lax.reduce_precision(rest, exponent_bits=8, mantissa_bits=7)
    low = rest - mid
    weight_rows = jnp.stack([hi, mid, low], axis=2).astype(jnp.bfloat16)[:, :, None]
    weight_rows = jnp.broadcast_to(weight_rows, (panels, users, local_slots, 3, blk))
    offset_rows = jnp.broadcast_to(
        slot_offset.astype(jnp.bfloat16)[..., None, None], (panels, users, local_slots, 1, blk)
    )
    pad = jnp.zeros((panels, users, local_slots, META - 4, blk), jnp.bfloat16)
    return jnp.concatenate([panel_blocks, weight_rows, offset_rows, pad], axis=3)


def local(panel_blocks, user_weights, slot_offset, *, nrow, ncol):
    panels, _, local_slots, blk, _ = panel_blocks.shape
    r = lax.axis_index("row")
    c = lax.axis_index("col")
    x = with_meta(panel_blocks, user_weights, slot_offset)

    outer = ncol // 2
    cycle = [a * 2 for a in range(outer)] + [a * 2 + 1 for a in reversed(range(outer))]
    forward = [(cycle[i], cycle[(i + 1) % ncol]) for i in range(ncol)]
    backward = [(b, a) for a, b in forward]

    src = c // local_slots
    which = (r - src + nrow) % nrow
    slot = c % local_slots
    fans = [
        [
            ((cc // local_slots) * ncol + cc, ((cc // local_slots + j) % nrow) * ncol + cc)
            for cc in range(ncol)
        ]
        for j in range(1, nrow)
    ]

    nx = nrow // 2
    is_s, is_p = which == 0, r == src + 1 - 2 * (src % 2)
    is_d1 = (which % 2 == 0) & (which != 0)

    def send(v, pairs):
        return lax.ppermute(v, ("row", "col"), [(a * ncol + cc, b * ncol + cc) for a, b, cc in pairs])

    def last_fan(own, flip):
        heads = [cc // local_slots for cc in range(ncol)]
        land = lambda h, j: ((h + 2 * j) % nrow) ^ flip
        to_d1 = None
        for j in range(1, nx):
            v = send(own, [(h, land(h, j), cc) for cc, h in enumerate(heads)])
            to_d1 = v if to_d1 is None else jnp.where((r // 2 - src // 2 + nx) % nx == j, v, to_d1)
        to_partner = send(own, [(h, h ^ 1, cc) for cc, h in enumerate(heads)])
        to_d2 = send(
            to_d1,
            [(land(h, j), land(h, j) ^ 1, cc) for cc, h in enumerate(heads) for j in range(1, nx)],
        )
        landed = is_d1 if flip == 0 else (which % 2 == 1) & jnp.logical_not(is_p)
        return jnp.where(is_s, own, jnp.where(is_p, to_partner, jnp.where(landed, to_d1, to_d2)))

    def pick_slot(piece):
        return lax.dynamic_index_in_dim(piece, slot, axis=2, keepdims=False)

    batches = [[k] for k in range(ncol)]
    half = x.shape[1] // 2
    a, b = x[:, :half], x[:, half:]
    pieces, columns, pending = [], [], []
    for step in range(ncol):
        if step:
            a = lax.ppermute(a, "col", forward)
            b = lax.ppermute(b, "col", backward)
        pieces += [a, b]
        pending += [pick_slot(a), pick_slot(b)]
        if any(batch[-1] == step for batch in batches):
            own = jnp.concatenate(pending, axis=1)
            pending = []
            if step < 0:
                got = own
                for j, fan in enumerate(fans, start=1):
                    got = jnp.where(which == j, lax.ppermute(own, ("row", "col"), fan), got)
            else:
                got = last_fan(own, step % 2)
            columns.append(got)

    blocks = jnp.concatenate(pieces, axis=1)
    column_blocks = jnp.concatenate(columns, axis=1)
    n = panels * blocks.shape[1]
    blocks = blocks.reshape(n, local_slots, blk + META, blk)
    column_blocks = column_blocks.reshape(n, blk + META, blk)

    offs = jnp.concatenate([blocks[:, :, blk + 3, 0], column_blocks[:, blk + 3, 0][:, None]], axis=1)
    offs = jnp.clip(offs.astype(jnp.int32), 0, IBS - 1).reshape(-1)
    return gram_call(offs, blocks, column_blocks)


def solution(mesh):
    nrow, ncol = mesh.shape["row"], mesh.shape["col"]
    return jax.shard_map(
        functools.partial(local, nrow=nrow, ncol=ncol),
        mesh=mesh,
        in_specs=(P(None, "col", "row", None, None), P(None, "col", None), P(None, "col", "row")),
        out_specs=P("row", "col"),
        check_vma=False,
    )
```

```python
import functools

import jax
import jax.numpy as jnp
from jax import lax
from jax.experimental import pallas as pl
from jax.experimental.pallas import tpu as pltpu
from jax.sharding import PartitionSpec as P

IBS = 8
CHUNK = 24
META = 16


def gram_kernel(offs_ref, bs_ref, bc_ref, o_ref, *, chunk, local_slots, blk):
    s = pl.program_id(0)
    step = pl.program_id(1)

    @pl.when(step == 0)
    def _():
        o_ref[...] = jnp.zeros_like(o_ref)

    stride = local_slots + 1
    for k in range(chunk):
        g = step * chunk + k
        meta = bs_ref[k, 0, blk : blk + META].astype(jnp.float32)
        w = meta[0:1] + meta[1:2] + meta[2:3]
        lhs = (bs_ref[k, 0, :blk].T.astype(jnp.float32) * w).astype(jnp.bfloat16)
        prod = jnp.dot(lhs, bc_ref[k, :blk], preferred_element_type=jnp.float32)
        col = pl.multiple_of(offs_ref[g * stride + local_slots] * blk, blk)
        row = pl.multiple_of(offs_ref[g * stride + s] * blk, blk)
        o_ref[pl.ds(row, blk), pl.ds(col, blk)] += prod


def gram_call(offs, bs, bc):
    n, local_slots, rows, blk = bs.shape
    chunk = CHUNK
    kernel = functools.partial(gram_kernel, chunk=chunk, local_slots=local_slots, blk=blk)
    out_rows, out_cols = local_slots * IBS * blk, IBS * blk
    return pl.pallas_call(
        kernel,
        grid_spec=pltpu.PrefetchScalarGridSpec(
            num_scalar_prefetch=1,
            grid=(local_slots, n // chunk),
            in_specs=[
                pl.BlockSpec((chunk, 1, rows, blk), lambda s, i, o: (i, s, 0, 0)),
                pl.BlockSpec((chunk, rows, blk), lambda s, i, o: (i, 0, 0)),
            ],
            out_specs=pl.BlockSpec((IBS * blk, out_cols), lambda s, i, o: (s, 0)),
        ),
        out_shape=jax.ShapeDtypeStruct((out_rows, out_cols), jnp.float32),
        compiler_params=pltpu.CompilerParams(
            dimension_semantics=("arbitrary", "arbitrary"), vmem_limit_bytes=48 * 1024 * 1024
        ),
        cost_estimate=pl.CostEstimate(
            flops=2 * n * local_slots * blk * blk * blk,
            transcendentals=0,
            bytes_accessed=n * (local_slots + 1) * blk * blk * 2 + out_rows * out_cols * 4,
        ),
    )(offs, bs, bc)


def with_meta(panel_blocks, user_weights, slot_offset):
    panels, users, local_slots, blk, _ = panel_blocks.shape
    hi = lax.reduce_precision(user_weights, exponent_bits=8, mantissa_bits=7)
    rest = user_weights - hi
    mid = lax.reduce_precision(rest, exponent_bits=8, mantissa_bits=7)
    low = rest - mid
    weight_rows = jnp.stack([hi, mid, low], axis=2).astype(jnp.bfloat16)[:, :, None]
    weight_rows = jnp.broadcast_to(weight_rows, (panels, users, local_slots, 3, blk))
    offset_rows = jnp.broadcast_to(
        slot_offset.astype(jnp.bfloat16)[..., None, None], (panels, users, local_slots, 1, blk)
    )
    pad = jnp.zeros((panels, users, local_slots, META - 4, blk), jnp.bfloat16)
    return jnp.concatenate([panel_blocks, weight_rows, offset_rows, pad], axis=3)


def local(panel_blocks, user_weights, slot_offset, *, nrow, ncol):
    panels, _, local_slots, blk, _ = panel_blocks.shape
    r = lax.axis_index("row")
    c = lax.axis_index("col")
    x = with_meta(panel_blocks, user_weights, slot_offset)

    outer = ncol // 2
    cycle = [a * 2 for a in range(outer)] + [a * 2 + 1 for a in reversed(range(outer))]
    forward = [(cycle[i], cycle[(i + 1) % ncol]) for i in range(ncol)]
    backward = [(b, a) for a, b in forward]

    src = c // local_slots
    which = (r - src + nrow) % nrow
    slot = c % local_slots
    fans = [
        [
            ((cc // local_slots) * ncol + cc, ((cc // local_slots + j) % nrow) * ncol + cc)
            for cc in range(ncol)
        ]
        for j in range(1, nrow)
    ]

    nx = nrow // 2
    is_s, is_p = which == 0, r == src + 1 - 2 * (src % 2)
    is_d1 = (which % 2 == 0) & (which != 0)

    def send(v, pairs):
        return lax.ppermute(v, ("row", "col"), [(a * ncol + cc, b * ncol + cc) for a, b, cc in pairs])

    def last_fan(own):
        heads = [cc // local_slots for cc in range(ncol)]
        to_partner = send(own, [(h, h ^ 1, cc) for cc, h in enumerate(heads)])
        to_d1 = None
        for j in range(1, nx):
            v = send(own, [(h, (h + 2 * j) % nrow, cc) for cc, h in enumerate(heads)])
            to_d1 = v if to_d1 is None else jnp.where(which // 2 == j, v, to_d1)
        to_d2 = send(
            to_d1,
            [((h + 2 * j) % nrow, ((h + 2 * j) % nrow) ^ 1, cc) for cc, h in enumerate(heads) for j in range(1, nx)],
        )
        return jnp.where(is_s, own, jnp.where(is_p, to_partner, jnp.where(is_d1, to_d1, to_d2)))

    def pick_slot(piece):
        return lax.dynamic_index_in_dim(piece, slot, axis=2, keepdims=False)

    batches = [[k] for k in range(ncol)]
    half = x.shape[1] // 2
    a, b = x[:, :half], x[:, half:]
    pieces, columns, pending = [], [], []
    for step in range(ncol):
        if step:
            a = lax.ppermute(a, "col", forward)
            b = lax.ppermute(b, "col", backward)
        pieces += [a, b]
        pending += [pick_slot(a), pick_slot(b)]
        if any(batch[-1] == step for batch in batches):
            own = jnp.concatenate(pending, axis=1)
            pending = []
            if step < 0:
                got = own
                for j, fan in enumerate(fans, start=1):
                    got = jnp.where(which == j, lax.ppermute(own, ("row", "col"), fan), got)
            else:
                got = last_fan(own)
            columns.append(got)

    blocks = jnp.concatenate(pieces, axis=1)
    column_blocks = jnp.concatenate(columns, axis=1)
    n = panels * blocks.shape[1]
    blocks = blocks.reshape(n, local_slots, blk + META, blk)
    column_blocks = column_blocks.reshape(n, blk + META, blk)

    offs = jnp.concatenate([blocks[:, :, blk + 3, 0], column_blocks[:, blk + 3, 0][:, None]], axis=1)
    offs = jnp.clip(offs.astype(jnp.int32), 0, IBS - 1).reshape(-1)
    return gram_call(offs, blocks, column_blocks)


def solution(mesh):
    nrow, ncol = mesh.shape["row"], mesh.shape["col"]
    return jax.shard_map(
        functools.partial(local, nrow=nrow, ncol=ncol),
        mesh=mesh,
        in_specs=(P(None, "col", "row", None, None), P(None, "col", None), P(None, "col", "row")),
        out_specs=P("row", "col"),
        check_vma=False,
    )
```

```python
import functools

import jax
import jax.numpy as jnp
from jax import lax
from jax.experimental import pallas as pl
from jax.experimental.pallas import tpu as pltpu
from jax.sharding import PartitionSpec as P

IBS = 8
CHUNK = 32
META = 16


def gram_kernel(offs_ref, bs_ref, bc_ref, o_ref, *, chunk, local_slots, blk):
    s = pl.program_id(0)
    step = pl.program_id(1)

    @pl.when(step == 0)
    def _():
        o_ref[...] = jnp.zeros_like(o_ref)

    stride = local_slots + 1
    for k in range(chunk):
        g = step * chunk + k
        meta = bs_ref[k, 0, blk : blk + META].astype(jnp.float32)
        w = meta[0:1] + meta[1:2] + meta[2:3]
        lhs = (bs_ref[k, 0, :blk].T.astype(jnp.float32) * w).astype(jnp.bfloat16)
        prod = jnp.dot(lhs, bc_ref[k, :blk], preferred_element_type=jnp.float32)
        col = pl.multiple_of(offs_ref[g * stride + local_slots] * blk, blk)
        row = pl.multiple_of(offs_ref[g * stride + s] * blk, blk)
        o_ref[pl.ds(row, blk), pl.ds(col, blk)] += prod


def gram_call(offs, bs, bc):
    n, local_slots, rows, blk = bs.shape
    chunk = CHUNK
    kernel = functools.partial(gram_kernel, chunk=chunk, local_slots=local_slots, blk=blk)
    out_rows, out_cols = local_slots * IBS * blk, IBS * blk
    return pl.pallas_call(
        kernel,
        grid_spec=pltpu.PrefetchScalarGridSpec(
            num_scalar_prefetch=1,
            grid=(local_slots, n // chunk),
            in_specs=[
                pl.BlockSpec((chunk, 1, rows, blk), lambda s, i, o: (i, s, 0, 0)),
                pl.BlockSpec((chunk, rows, blk), lambda s, i, o: (i, 0, 0)),
            ],
            out_specs=pl.BlockSpec((IBS * blk, out_cols), lambda s, i, o: (s, 0)),
        ),
        out_shape=jax.ShapeDtypeStruct((out_rows, out_cols), jnp.float32),
        compiler_params=pltpu.CompilerParams(
            dimension_semantics=("arbitrary", "arbitrary"), vmem_limit_bytes=48 * 1024 * 1024
        ),
        cost_estimate=pl.CostEstimate(
            flops=2 * n * local_slots * blk * blk * blk,
            transcendentals=0,
            bytes_accessed=n * (local_slots + 1) * blk * blk * 2 + out_rows * out_cols * 4,
        ),
    )(offs, bs, bc)


def with_meta(panel_blocks, user_weights, slot_offset):
    panels, users, local_slots, blk, _ = panel_blocks.shape
    hi = lax.reduce_precision(user_weights, exponent_bits=8, mantissa_bits=7)
    rest = user_weights - hi
    mid = lax.reduce_precision(rest, exponent_bits=8, mantissa_bits=7)
    low = rest - mid
    weight_rows = jnp.stack([hi, mid, low], axis=2).astype(jnp.bfloat16)[:, :, None]
    weight_rows = jnp.broadcast_to(weight_rows, (panels, users, local_slots, 3, blk))
    offset_rows = jnp.broadcast_to(
        slot_offset.astype(jnp.bfloat16)[..., None, None], (panels, users, local_slots, 1, blk)
    )
    pad = jnp.zeros((panels, users, local_slots, META - 4, blk), jnp.bfloat16)
    return jnp.concatenate([panel_blocks, weight_rows, offset_rows, pad], axis=3)


def local(panel_blocks, user_weights, slot_offset, *, nrow, ncol):
    panels, _, local_slots, blk, _ = panel_blocks.shape
    r = lax.axis_index("row")
    c = lax.axis_index("col")
    x = with_meta(panel_blocks, user_weights, slot_offset)

    outer = ncol // 2
    cycle = [a * 2 for a in range(outer)] + [a * 2 + 1 for a in reversed(range(outer))]
    forward = [(cycle[i], cycle[(i + 1) % ncol]) for i in range(ncol)]
    backward = [(b, a) for a, b in forward]

    src = c // local_slots
    which = (r - src + nrow) % nrow
    slot = c % local_slots
    fans = [
        [
            ((cc // local_slots) * ncol + cc, ((cc // local_slots + j) % nrow) * ncol + cc)
            for cc in range(ncol)
        ]
        for j in range(1, nrow)
    ]

    nx = nrow // 2
    is_s, is_p = which == 0, r == src + 1 - 2 * (src % 2)
    is_d1 = (which % 2 == 0) & (which != 0)

    def send(v, pairs):
        return lax.ppermute(v, ("row", "col"), [(a * ncol + cc, b * ncol + cc) for a, b, cc in pairs])

    def last_fan(own):
        heads = [cc // local_slots for cc in range(ncol)]
        to_partner = send(own, [(h, h ^ 1, cc) for cc, h in enumerate(heads)])
        to_d1 = None
        for j in range(1, nx):
            v = send(own, [(h, (h + 2 * j) % nrow, cc) for cc, h in enumerate(heads)])
            to_d1 = v if to_d1 is None else jnp.where(which // 2 == j, v, to_d1)
        to_d2 = send(
            to_d1,
            [((h + 2 * j) % nrow, ((h + 2 * j) % nrow) ^ 1, cc) for cc, h in enumerate(heads) for j in range(1, nx)],
        )
        return jnp.where(is_s, own, jnp.where(is_p, to_partner, jnp.where(is_d1, to_d1, to_d2)))

    def pick_slot(piece):
        return lax.dynamic_index_in_dim(piece, slot, axis=2, keepdims=False)

    batches = [[k] for k in range(ncol)]
    half = x.shape[1] // 2
    a, b = x[:, :half], x[:, half:]
    pieces, columns, pending = [], [], []
    for step in range(ncol):
        if step:
            a = lax.ppermute(a, "col", forward)
            b = lax.ppermute(b, "col", backward)
        pieces += [a, b]
        pending += [pick_slot(a), pick_slot(b)]
        if any(batch[-1] == step for batch in batches):
            own = jnp.concatenate(pending, axis=1)
            pending = []
            if step < 0:
                got = own
                for j, fan in enumerate(fans, start=1):
                    got = jnp.where(which == j, lax.ppermute(own, ("row", "col"), fan), got)
            else:
                got = last_fan(own)
            columns.append(got)

    blocks = jnp.concatenate(pieces, axis=1)
    column_blocks = jnp.concatenate(columns, axis=1)
    n = panels * blocks.shape[1]
    blocks = blocks.reshape(n, local_slots, blk + META, blk)
    column_blocks = column_blocks.reshape(n, blk + META, blk)

    offs = jnp.concatenate([blocks[:, :, blk + 3, 0], column_blocks[:, blk + 3, 0][:, None]], axis=1)
    offs = jnp.clip(offs.astype(jnp.int32), 0, IBS - 1).reshape(-1)
    return gram_call(offs, blocks, column_blocks)


def solution(mesh):
    nrow, ncol = mesh.shape["row"], mesh.shape["col"]
    return jax.shard_map(
        functools.partial(local, nrow=nrow, ncol=ncol),
        mesh=mesh,
        in_specs=(P(None, "col", "row", None, None), P(None, "col", None), P(None, "col", "row")),
        out_specs=P("row", "col"),
        check_vma=False,
    )
```

```python
import functools

import jax
import jax.numpy as jnp
from jax import lax
from jax.experimental import pallas as pl
from jax.experimental.pallas import tpu as pltpu
from jax.sharding import PartitionSpec as P

IBS = 8
CHUNK = 48
META = 16


def gram_kernel(offs_ref, bs_ref, bc_ref, o_ref, *, chunk, local_slots, blk):
    s = pl.program_id(0)
    step = pl.program_id(1)

    @pl.when(step == 0)
    def _():
        o_ref[...] = jnp.zeros_like(o_ref)

    stride = local_slots + 1
    for k in range(chunk):
        g = step * chunk + k
        meta = bs_ref[k, 0, blk : blk + META].astype(jnp.float32)
        w = meta[0:1] + meta[1:2] + meta[2:3]
        lhs = (bs_ref[k, 0, :blk].T.astype(jnp.float32) * w).astype(jnp.bfloat16)
        prod = jnp.dot(lhs, bc_ref[k, :blk], preferred_element_type=jnp.float32)
        col = pl.multiple_of(offs_ref[g * stride + local_slots] * blk, blk)
        row = pl.multiple_of(offs_ref[g * stride + s] * blk, blk)
        o_ref[pl.ds(row, blk), pl.ds(col, blk)] += prod


def gram_call(offs, bs, bc):
    n, local_slots, rows, blk = bs.shape
    chunk = CHUNK
    kernel = functools.partial(gram_kernel, chunk=chunk, local_slots=local_slots, blk=blk)
    out_rows, out_cols = local_slots * IBS * blk, IBS * blk
    return pl.pallas_call(
        kernel,
        grid_spec=pltpu.PrefetchScalarGridSpec(
            num_scalar_prefetch=1,
            grid=(local_slots, n // chunk),
            in_specs=[
                pl.BlockSpec((chunk, 1, rows, blk), lambda s, i, o: (i, s, 0, 0)),
                pl.BlockSpec((chunk, rows, blk), lambda s, i, o: (i, 0, 0)),
            ],
            out_specs=pl.BlockSpec((IBS * blk, out_cols), lambda s, i, o: (s, 0)),
        ),
        out_shape=jax.ShapeDtypeStruct((out_rows, out_cols), jnp.float32),
        compiler_params=pltpu.CompilerParams(
            dimension_semantics=("arbitrary", "arbitrary"), vmem_limit_bytes=48 * 1024 * 1024
        ),
        cost_estimate=pl.CostEstimate(
            flops=2 * n * local_slots * blk * blk * blk,
            transcendentals=0,
            bytes_accessed=n * (local_slots + 1) * blk * blk * 2 + out_rows * out_cols * 4,
        ),
    )(offs, bs, bc)


def with_meta(panel_blocks, user_weights, slot_offset):
    panels, users, local_slots, blk, _ = panel_blocks.shape
    hi = lax.reduce_precision(user_weights, exponent_bits=8, mantissa_bits=7)
    rest = user_weights - hi
    mid = lax.reduce_precision(rest, exponent_bits=8, mantissa_bits=7)
    low = rest - mid
    weight_rows = jnp.stack([hi, mid, low], axis=2).astype(jnp.bfloat16)[:, :, None]
    weight_rows = jnp.broadcast_to(weight_rows, (panels, users, local_slots, 3, blk))
    offset_rows = jnp.broadcast_to(
        slot_offset.astype(jnp.bfloat16)[..., None, None], (panels, users, local_slots, 1, blk)
    )
    pad = jnp.zeros((panels, users, local_slots, META - 4, blk), jnp.bfloat16)
    return jnp.concatenate([panel_blocks, weight_rows, offset_rows, pad], axis=3)


def local(panel_blocks, user_weights, slot_offset, *, nrow, ncol):
    panels, _, local_slots, blk, _ = panel_blocks.shape
    r = lax.axis_index("row")
    c = lax.axis_index("col")
    x = with_meta(panel_blocks, user_weights, slot_offset)

    outer = ncol // 2
    cycle = [a * 2 for a in range(outer)] + [a * 2 + 1 for a in reversed(range(outer))]
    forward = [(cycle[i], cycle[(i + 1) % ncol]) for i in range(ncol)]
    backward = [(b, a) for a, b in forward]

    src = c // local_slots
    which = (r - src + nrow) % nrow
    slot = c % local_slots
    fans = [
        [
            ((cc // local_slots) * ncol + cc, ((cc // local_slots + j) % nrow) * ncol + cc)
            for cc in range(ncol)
        ]
        for j in range(1, nrow)
    ]

    nx = nrow // 2
    is_s, is_p = which == 0, r == src + 1 - 2 * (src % 2)
    is_d1 = (which % 2 == 0) & (which != 0)

    def send(v, pairs):
        return lax.ppermute(v, ("row", "col"), [(a * ncol + cc, b * ncol + cc) for a, b, cc in pairs])

    def last_fan(own):
        heads = [cc // local_slots for cc in range(ncol)]
        to_partner = send(own, [(h, h ^ 1, cc) for cc, h in enumerate(heads)])
        to_d1 = None
        for j in range(1, nx):
            v = send(own, [(h, (h + 2 * j) % nrow, cc) for cc, h in enumerate(heads)])
            to_d1 = v if to_d1 is None else jnp.where(which // 2 == j, v, to_d1)
        to_d2 = send(
            to_d1,
            [((h + 2 * j) % nrow, ((h + 2 * j) % nrow) ^ 1, cc) for cc, h in enumerate(heads) for j in range(1, nx)],
        )
        return jnp.where(is_s, own, jnp.where(is_p, to_partner, jnp.where(is_d1, to_d1, to_d2)))

    def pick_slot(piece):
        picked = piece[:, :, 0]
        for k in range(1, local_slots):
            picked = jnp.where(slot == k, piece[:, :, k], picked)
        return picked

    batches = [[k] for k in range(ncol)]
    half = x.shape[1] // 2
    a, b = x[:, :half], x[:, half:]
    pieces, columns, pending = [], [], []
    for step in range(ncol):
        if step:
            a = lax.ppermute(a, "col", forward)
            b = lax.ppermute(b, "col", backward)
        pieces += [a, b]
        pending += [pick_slot(a), pick_slot(b)]
        if any(batch[-1] == step for batch in batches):
            own = jnp.concatenate(pending, axis=1)
            pending = []
            if step < 0:
                got = own
                for j, fan in enumerate(fans, start=1):
                    got = jnp.where(which == j, lax.ppermute(own, ("row", "col"), fan), got)
            else:
                got = last_fan(own)
            columns.append(got)

    blocks = jnp.concatenate(pieces, axis=1)
    column_blocks = jnp.concatenate(columns, axis=1)
    n = panels * blocks.shape[1]
    blocks = blocks.reshape(n, local_slots, blk + META, blk)
    column_blocks = column_blocks.reshape(n, blk + META, blk)

    offs = jnp.concatenate([blocks[:, :, blk + 3, 0], column_blocks[:, blk + 3, 0][:, None]], axis=1)
    offs = jnp.clip(offs.astype(jnp.int32), 0, IBS - 1).reshape(-1)
    return gram_call(offs, blocks, column_blocks)


def solution(mesh):
    nrow, ncol = mesh.shape["row"], mesh.shape["col"]
    return jax.shard_map(
        functools.partial(local, nrow=nrow, ncol=ncol),
        mesh=mesh,
        in_specs=(P(None, "col", "row", None, None), P(None, "col", None), P(None, "col", "row")),
        out_specs=P("row", "col"),
        check_vma=False,
    )
```
